32 devices in a mesh: outer: 4 (over z), dp: 2 (over y), cent: 4 (over x, core).
Axes of the slice: x: 2, y: 2, z: 4, core: 2. Of those that a mesh axis runs over, the one named last changes fastest.
Arguments:
- rows: float32 [2048, 1024], P(('outer', 'dp')), may hold values from -256 to 256
- centroids: float32 [4096, 1024], P(('dp', 'cent')), may hold values from -0.5 to 0.5
Outputs:
- centroid_shift: float32 [4096, 1024], P(('dp', 'cent'))
The draws below stay inside these ranges and needn't reach their ends.
All inputs are finite; a program needn't handle non-finite values.
Results may differ from the reference program's by a relative error of at most 0.0081.
Values may be sent and summed in bfloat16 or wider, within the bound.
No kernel may reach another device: no remote copies, remote signals or barrier semaphores. Data moves between devices by JAX's collectives and lax.ppermute only.
A program may use at most 64 MiB of HBM per device.

```python
import jax
import jax.numpy as jnp
from jax import lax

D = 1024
TOK_DEV = 256
K = 4096
ROWS = 2048
N_OUTER = 4
N_DP = 2


def centroid_table(key):
    inner = jax.random.fold_in(key, 11)
    table = jnp.clip(jax.random.normal(inner, (K, D), jnp.float32) * 0.1, -0.5, 0.5)
    return table


def draw_centroids(key, part):
    return centroid_table(key)


def draw_rows(key, part):
    spread_key = jax.random.fold_in(key, 21)
    value_key = jax.random.fold_in(key, 22)
    spread = jnp.exp(jax.random.uniform(spread_key, (ROWS, 1), jnp.float32, jnp.log(1.8), jnp.log(2.6)))
    mean_square = D * 0.01
    scales = spread / jnp.sqrt(jnp.float32(mean_square))
    result = jnp.clip(jax.random.normal(value_key, (ROWS, D), jnp.float32), -6.0, 6.0) * scales
    return result


def setup_inputs(seed: int = 0) -> dict:
    arg_keys = jax.random.split(jax.random.key(seed), 3)
    return {
        "rows": draw_rows(jax.random.fold_in(arg_keys[2], 71), 0),
        "centroids": draw_centroids(jax.random.fold_in(arg_keys[2], 71), 0),
    }


def reference(rows, centroids):
    squares = jnp.sum(centroids * centroids, axis=1)
    cent_bf = centroids.astype(jnp.bfloat16)
    pods = rows.reshape(N_OUTER, N_DP * TOK_DEV, D)

    def one_pod(pod_rows):
        rows_bf = pod_rows.astype(jnp.bfloat16)
        logits = 0.5 * (2.0 * jnp.dot(rows_bf, cent_bf.T, preferred_element_type=jnp.float32) - squares[None, :])
        row_peak = jnp.max(logits, axis=1)
        row_mass = jnp.sum(jnp.exp(logits - row_peak[:, None]), axis=1)
        weights = (jnp.exp(logits - row_peak[:, None]) / row_mass[:, None]).astype(jnp.bfloat16)
        weight_sum = jnp.sum(weights.astype(jnp.float32), axis=0)
        pull = jnp.dot(weights.T, rows_bf, preferred_element_type=jnp.float32)
        return (pull - weight_sum[:, None] * centroids) / (weight_sum[:, None] + 1.0)

    deltas = lax.map(one_pod, pods)
    return jnp.sum(deltas, axis=0) / N_OUTER
```

```python
import itertools

import jax
import jax.numpy as jnp
from jax import lax
from jax.sharding import PartitionSpec as P


def scores_for(piece, cent_bf, squares):
    product = lax.dot_general(
        piece, cent_bf, (((1,), (1,)), ((), ())), preferred_element_type=jnp.float32
    )
    return 0.5 * (2.0 * product - squares[None, :])


def row_summary(logits):
    local_max = jnp.max(logits, axis=1)
    local_sum = jnp.sum(jnp.exp(logits - local_max[:, None]), axis=1)
    return (local_max, local_sum)


def global_stats(local_max, local_sum):
    row_peak = lax.pmax(local_max, ("dp", "cent"))
    row_mass = lax.psum(local_sum * jnp.exp(local_max - row_peak), ("dp", "cent"))
    return (row_peak, row_mass)


def gathered_stats(local_max, local_sum):
    both = lax.all_gather(jnp.stack([local_max, local_sum]), ("dp", "cent"), axis=0)
    maxes, sums = both[:, 0], both[:, 1]
    row_peak = jnp.max(maxes, axis=0)
    row_mass = jnp.sum(sums * jnp.exp(maxes - row_peak[None, :]), axis=0)
    return (row_peak, row_mass)


def shards_pod(rows, centroids):
    rows_bf = rows.astype(jnp.bfloat16)
    cent_bf = centroids.astype(jnp.bfloat16)
    squares = jnp.sum(centroids * centroids, axis=1)
    gathered = lax.all_gather(rows_bf, "dp", axis=0, tiled=True)
    logits = scores_for(gathered, cent_bf, squares)
    local_max, local_sum = row_summary(logits)
    row_peak, row_mass = global_stats(local_max, local_sum)
    weights = (jnp.exp(logits - row_peak[:, None]) / row_mass[:, None]).astype(jnp.bfloat16)
    weight_sum = jnp.sum(weights.astype(jnp.float32), axis=0)
    pull = lax.dot_general(
        weights, gathered, (((0,), (0,)), ((), ())), preferred_element_type=jnp.float32
    )
    delta = (pull - weight_sum[:, None] * centroids) / (weight_sum[:, None] + 1.0)
    return lax.psum(delta, "outer") / lax.axis_size("outer")


def gather_all_rows(rows_bf):
    n_o = lax.axis_size("outer")
    n_d = lax.axis_size("dp")
    n_c = lax.axis_size("cent")
    z = lax.axis_index("outer")
    y = lax.axis_index("dp")
    q = lax.axis_index("cent")
    t, d = rows_bf.shape
    tq = t // n_c
    quarter = lax.dynamic_slice_in_dim(rows_bf, q * tq, tq, 0)

    n_od = n_o * n_d
    me = z * n_d + y
    slots = [quarter]
    shifts = [(sz, sy) for sz, sy in itertools.product(range(n_o), range(n_d)) if (sz, sy) != (0, 0)]
    for sz, sy in shifts:
        perm = []
        for i, j in itertools.product(range(n_o), range(n_d)):
            perm.append((i * n_d + j, ((i + sz) % n_o) * n_d + (j + sy) % n_d))
        slots.append(lax.ppermute(quarter, ("outer", "dp"), perm))
    stack_a = jnp.stack(slots)
    src_of_slot = [(0, 0)] + shifts
    inv = [0] * n_od
    for k, (sz, sy) in enumerate(src_of_slot):
        inv[sz * n_d + sy] = k
    a = jnp.arange(n_od)
    rel = ((z - a // n_d) % n_o) * n_d + (y - a % n_d) % n_d
    stack_a = jnp.take(stack_a, jnp.asarray(inv, jnp.int32)[rel], axis=0)

    bits = []
    b = 1
    while b < n_c:
        bits.append(b)
        b *= 2
    cur = stack_a[None]
    xs = [0]
    for bit in reversed(bits):
        other = lax.ppermute(cur, "cent", [(i, i ^ bit) for i in range(n_c)])
        cur = jnp.concatenate([cur, other], axis=0)
        xs = xs + [x ^ bit for x in xs]
    inv_c = [0] * n_c
    for k, x in enumerate(xs):
        inv_c[x] = k
    cidx = jnp.asarray(inv_c, jnp.int32)[q ^ jnp.arange(n_c)]
    cur = jnp.take(cur, cidx, axis=0)
    return cur.transpose(1, 0, 2, 3).reshape(n_od * n_c * tq, d)


def shards_all(rows, centroids):
    n_o = lax.axis_size("outer")
    rows_bf = rows.astype(jnp.bfloat16)
    cent_bf = centroids.astype(jnp.bfloat16)
    squares = jnp.sum(centroids * centroids, axis=1)
    everything = gather_all_rows(rows_bf)
    logits = scores_for(everything, cent_bf, squares)
    local_max, local_sum = row_summary(logits)
    row_peak, row_mass = gathered_stats(local_max, local_sum)
    weights = (jnp.exp(logits - row_peak[:, None]) / row_mass[:, None]).astype(jnp.bfloat16)
    n_all, d = everything.shape
    k = centroids.shape[0]
    pod = n_all // n_o
    w_pods = weights.reshape(n_o, pod, k)
    r_pods = everything.reshape(n_o, pod, d)
    weight_sum = jnp.sum(w_pods.astype(jnp.float32), axis=1)
    pull = lax.dot_general(
        w_pods, r_pods, (((1,), (1,)), ((0,), (0,))), preferred_element_type=jnp.float32
    )
    delta = (pull - weight_sum[:, :, None] * centroids[None]) / (weight_sum[:, :, None] + 1.0)
    return jnp.sum(delta, axis=0) / n_o


def solution(mesh):
    n_o, n_d, n_c = mesh.shape["outer"], mesh.shape["dp"], mesh.shape["cent"]

    def shards(rows, centroids):
        t, d = rows.shape
        k = centroids.shape[0]
        n_all = t * n_o * n_d
        footprint = n_all * d * 2 + n_all * k * 4 * 2
        if footprint <= (24 << 20) and t % n_c == 0 and (n_c & (n_c - 1)) == 0:
            return shards_all(rows, centroids)
        return shards_pod(rows, centroids)

    return jax.shard_map(
        shards,
        mesh=mesh,
        in_specs=(P(("outer", "dp"), None), P(("dp", "cent"), None)),
        out_specs=P(("dp", "cent"), None),
        check_vma=False,
    )
```

```python
import itertools

import jax
import jax.numpy as jnp
from jax import lax
from jax.sharding import PartitionSpec as P


def scores_for(piece, cent_bf, squares):
    product = lax.dot_general(
        piece, cent_bf, (((1,), (1,)), ((), ())), preferred_element_type=jnp.float32
    )
    return 0.5 * (2.0 * product - squares[None, :])


def row_summary(logits):
    local_max = jnp.max(logits, axis=1)
    local_sum = jnp.sum(jnp.exp(logits - local_max[:, None]), axis=1)
    return (local_max, local_sum)


def global_stats(local_max, local_sum):
    row_peak = lax.pmax(local_max, ("dp", "cent"))
    row_mass = lax.psum(local_sum * jnp.exp(local_max - row_peak), ("dp", "cent"))
    return (row_peak, row_mass)


def shards_pod(rows, centroids):
    rows_bf = rows.astype(jnp.bfloat16)
    cent_bf = centroids.astype(jnp.bfloat16)
    squares = jnp.sum(centroids * centroids, axis=1)
    gathered = lax.all_gather(rows_bf, "dp", axis=0, tiled=True)
    logits = scores_for(gathered, cent_bf, squares)
    local_max, local_sum = row_summary(logits)
    row_peak, row_mass = global_stats(local_max, local_sum)
    weights = (jnp.exp(logits - row_peak[:, None]) / row_mass[:, None]).astype(jnp.bfloat16)
    weight_sum = jnp.sum(weights.astype(jnp.float32), axis=0)
    pull = lax.dot_general(
        weights, gathered, (((0,), (0,)), ((), ())), preferred_element_type=jnp.float32
    )
    delta = (pull - weight_sum[:, None] * centroids) / (weight_sum[:, None] + 1.0)
    return lax.psum(delta, "outer") / lax.axis_size("outer")


def shards_all(rows, centroids):
    n_o = lax.axis_size("outer")
    n_d = lax.axis_size("dp")
    n_c = lax.axis_size("cent")
    z = lax.axis_index("outer")
    y = lax.axis_index("dp")
    q = lax.axis_index("cent")
    t, d = rows.shape
    tq = t // n_c
    n_od = n_o * n_d

    rows_bf = rows.astype(jnp.bfloat16)
    cent_bf = centroids.astype(jnp.bfloat16)
    squares = jnp.sum(centroids * centroids, axis=1)

    bits = []
    b = 1
    while b < n_c:
        bits.append(b)
        b *= 2
    xs = [0]
    for bit in reversed(bits):
        xs = xs + [x ^ bit for x in xs]

    def quarter_of(x):
        return lax.dynamic_slice_in_dim(rows_bf, (q ^ x) * tq, tq, 0)

    own = jnp.concatenate([quarter_of(x) for x in xs], axis=0)
    mine = quarter_of(0)

    def spread(piece):
        cur = piece
        for bit in reversed(bits):
            other = lax.ppermute(cur, "cent", [(i, i ^ bit) for i in range(n_c)])
            cur = jnp.concatenate([cur, other], axis=0)
        return cur

    shifts = list(itertools.product(range(n_o), range(n_d)))
    blocks = []
    for sz, sy in shifts:
        if (sz, sy) == (0, 0):
            blocks.append(own)
            continue
        perm = []
        for i, j in itertools.product(range(n_o), range(n_d)):
            perm.append((i * n_d + j, ((i + sz) % n_o) * n_d + (j + sy) % n_d))
        blocks.append(spread(lax.ppermute(mine, ("outer", "dp"), perm)))

    logits = [scores_for(blk, cent_bf, squares) for blk in blocks]
    summaries = [row_summary(lg) for lg in logits]
    local_max = jnp.concatenate([s[0] for s in summaries])
    local_sum = jnp.concatenate([s[1] for s in summaries])

    k_idx = jnp.arange(n_od * n_c * tq) // (n_c * tq)
    j_idx = (jnp.arange(n_od * n_c * tq) // tq) % n_c
    r_idx = jnp.arange(n_od * n_c * tq) % tq
    sz_of = jnp.asarray([s[0] for s in shifts], jnp.int32)[k_idx]
    sy_of = jnp.asarray([s[1] for s in shifts], jnp.int32)[k_idx]
    x_of = jnp.asarray(xs, jnp.int32)[j_idx]
    src = ((z - sz_of) % n_o) * n_d + (y - sy_of) % n_d
    absolute = (src * n_c + (q ^ x_of)) * tq + r_idx
    order = jnp.zeros_like(absolute).at[absolute].set(jnp.arange(absolute.shape[0]))

    both = jnp.stack([local_max, local_sum])[:, order]
    every = lax.all_gather(both, ("dp", "cent"), axis=0)
    maxes, sums = every[:, 0], every[:, 1]
    peak_abs = jnp.max(maxes, axis=0)
    mass_abs = jnp.sum(sums * jnp.exp(maxes - peak_abs[None, :]), axis=0)
    row_peak = peak_abs[absolute]
    row_mass = mass_abs[absolute]

    blk = n_c * tq
    weight_sum = [None] * n_o
    pull = [None] * n_o
    for k, (sz, sy) in enumerate(shifts):
        pk = row_peak[k * blk:(k + 1) * blk]
        mk = row_mass[k * blk:(k + 1) * blk]
        w = (jnp.exp(logits[k] - pk[:, None]) / mk[:, None]).astype(jnp.bfloat16)
        ws = jnp.sum(w.astype(jnp.float32), axis=0)
        pl = lax.dot_general(
            w, blocks[k], (((0,), (0,)), ((), ())), preferred_element_type=jnp.float32
        )
        weight_sum[sz] = ws if weight_sum[sz] is None else weight_sum[sz] + ws
        pull[sz] = pl if pull[sz] is None else pull[sz] + pl

    total = None
    for a in range(n_o):
        rel = (z - a) % n_o
        pick_pull = pull[0]
        pick_ws = weight_sum[0]
        for s in range(1, n_o):
            pick_pull = jnp.where(rel == s, pull[s], pick_pull)
            pick_ws = jnp.where(rel == s, weight_sum[s], pick_ws)
        delta = (pick_pull - pick_ws[:, None] * centroids) / (pick_ws[:, None] + 1.0)
        total = delta if total is None else total + delta
    return total / n_o


def solution(mesh):
    n_o, n_d, n_c = mesh.shape["outer"], mesh.shape["dp"], mesh.shape["cent"]

    def shards(rows, centroids):
        t, d = rows.shape
        k = centroids.shape[0]
        n_all = t * n_o * n_d
        footprint = n_all * d * 2 + n_all * k * 4 * 2
        if footprint <= (24 << 20) and t % n_c == 0 and (n_c & (n_c - 1)) == 0:
            return shards_all(rows, centroids)
        return shards_pod(rows, centroids)

    return jax.shard_map(
        shards,
        mesh=mesh,
        in_specs=(P(("outer", "dp"), None), P(("dp", "cent"), None)),
        out_specs=P(("dp", "cent"), None),
        check_vma=False,
    )
```

```python
import itertools

import jax
import jax.numpy as jnp
from jax import lax
from jax.sharding import PartitionSpec as P


def scores_for(piece, cent_bf, squares):
    product = lax.dot_general(
        piece, cent_bf, (((1,), (1,)), ((), ())), preferred_element_type=jnp.float32
    )
    return 0.5 * (2.0 * product - squares[None, :])


def row_summary(logits):
    local_max = jnp.max(logits, axis=1)
    local_sum = jnp.sum(jnp.exp(logits - local_max[:, None]), axis=1)
    return (local_max, local_sum)


def global_stats(local_max, local_sum):
    row_peak = lax.pmax(local_max, ("dp", "cent"))
    row_mass = lax.psum(local_sum * jnp.exp(local_max - row_peak), ("dp", "cent"))
    return (row_peak, row_mass)


def shards_pod(rows, centroids):
    rows_bf = rows.astype(jnp.bfloat16)
    cent_bf = centroids.astype(jnp.bfloat16)
    squares = jnp.sum(centroids * centroids, axis=1)
    gathered = lax.all_gather(rows_bf, "dp", axis=0, tiled=True)
    logits = scores_for(gathered, cent_bf, squares)
    local_max, local_sum = row_summary(logits)
    row_peak, row_mass = global_stats(local_max, local_sum)
    weights = (jnp.exp(logits - row_peak[:, None]) / row_mass[:, None]).astype(jnp.bfloat16)
    weight_sum = jnp.sum(weights.astype(jnp.float32), axis=0)
    pull = lax.dot_general(
        weights, gathered, (((0,), (0,)), ((), ())), preferred_element_type=jnp.float32
    )
    delta = (pull - weight_sum[:, None] * centroids) / (weight_sum[:, None] + 1.0)
    return lax.psum(delta, "outer") / lax.axis_size("outer")


def shards_all(rows, centroids):
    n_o = lax.axis_size("outer")
    n_d = lax.axis_size("dp")
    n_c = lax.axis_size("cent")
    z = lax.axis_index("outer")
    y = lax.axis_index("dp")
    q = lax.axis_index("cent")
    t, d = rows.shape
    tq = t // n_c
    n_od = n_o * n_d

    rows_bf = rows.astype(jnp.bfloat16)
    cent_bf = centroids.astype(jnp.bfloat16)
    squares = jnp.sum(centroids * centroids, axis=1)

    bits = []
    b = 1
    while b < n_c:
        bits.append(b)
        b *= 2
    xs = [0]
    for bit in reversed(bits):
        xs = xs + [x ^ bit for x in xs]

    def quarter_of(x):
        return lax.dynamic_slice_in_dim(rows_bf, (q ^ x) * tq, tq, 0)

    own = jnp.concatenate([quarter_of(x) for x in xs], axis=0)
    mine = quarter_of(0)

    def spread(piece):
        cur = piece
        for bit in reversed(bits):
            other = lax.ppermute(cur, "cent", [(i, i ^ bit) for i in range(n_c)])
            cur = jnp.concatenate([cur, other], axis=0)
        return cur

    shifts = list(itertools.product(range(n_o), range(n_d)))
    blocks = []
    for sz, sy in shifts:
        if (sz, sy) == (0, 0):
            blocks.append(own)
            continue
        perm = []
        for i, j in itertools.product(range(n_o), range(n_d)):
            perm.append((i * n_d + j, ((i + sz) % n_o) * n_d + (j + sy) % n_d))
        blocks.append(spread(lax.ppermute(mine, ("outer", "dp"), perm)))

    logits = [scores_for(blk, cent_bf, squares) for blk in blocks]
    summaries = [row_summary(lg) for lg in logits]
    local_max = jnp.concatenate([s[0] for s in summaries])
    local_sum = jnp.concatenate([s[1] for s in summaries])

    src_vec = jnp.stack([((z - sz) % n_o) * n_d + (y - sy) % n_d for sz, sy in shifts])
    hot_k = src_vec[None, :] == jnp.arange(n_od)[:, None]
    c_vec = jnp.stack([q ^ x for x in xs])
    hot_c = c_vec[None, :] == jnp.arange(n_c)[:, None]

    def to_absolute(v):
        v = v.reshape(n_od, n_c, tq)
        v = jnp.sum(jnp.where(hot_c[None, :, :, None], v[:, None, :, :], 0.0), axis=2)
        return jnp.sum(jnp.where(hot_k[:, :, None, None], v[None], 0.0), axis=1)

    def to_local(v):
        v = jnp.sum(jnp.where(hot_k[:, :, None, None], v[:, None], 0.0), axis=0)
        v = jnp.sum(jnp.where(hot_c[:, :, None], v[:, :, None, :], 0.0), axis=1)
        return v.reshape(n_od * n_c * tq)

    both = jnp.stack([to_absolute(local_max), to_absolute(local_sum)])
    every = lax.all_gather(both, ("dp", "cent"), axis=0)
    maxes, sums = every[:, 0], every[:, 1]
    peak_abs = jnp.max(maxes, axis=0)
    mass_abs = jnp.sum(sums * jnp.exp(maxes - peak_abs[None]), axis=0)
    row_peak = to_local(peak_abs)
    row_mass = to_local(mass_abs)

    blk = n_c * tq
    weight_sum = [None] * n_o
    pull = [None] * n_o
    for k, (sz, sy) in enumerate(shifts):
        pk = row_peak[k * blk:(k + 1) * blk]
        mk = row_mass[k * blk:(k + 1) * blk]
        w = (jnp.exp(logits[k] - pk[:, None]) / mk[:, None]).astype(jnp.bfloat16)
        ws = jnp.sum(w.astype(jnp.float32), axis=0)
        pl = lax.dot_general(
            w, blocks[k], (((0,), (0,)), ((), ())), preferred_element_type=jnp.float32
        )
        weight_sum[sz] = ws if weight_sum[sz] is None else weight_sum[sz] + ws
        pull[sz] = pl if pull[sz] is None else pull[sz] + pl

    total = None
    for a in range(n_o):
        rel = (z - a) % n_o
        pick_pull = pull[0]
        pick_ws = weight_sum[0]
        for s in range(1, n_o):
            pick_pull = jnp.where(rel == s, pull[s], pick_pull)
            pick_ws = jnp.where(rel == s, weight_sum[s], pick_ws)
        delta = (pick_pull - pick_ws[:, None] * centroids) / (pick_ws[:, None] + 1.0)
        total = delta if total is None else total + delta
    return total / n_o


def solution(mesh):
    n_o, n_d, n_c = mesh.shape["outer"], mesh.shape["dp"], mesh.shape["cent"]

    def shards(rows, centroids):
        t, d = rows.shape
        k = centroids.shape[0]
        n_all = t * n_o * n_d
        footprint = n_all * d * 2 + n_all * k * 4 * 2
        if footprint <= (24 << 20) and t % n_c == 0 and (n_c & (n_c - 1)) == 0:
            return shards_all(rows, centroids)
        return shards_pod(rows, centroids)

    return jax.shard_map(
        shards,
        mesh=mesh,
        in_specs=(P(("outer", "dp"), None), P(("dp", "cent"), None)),
        out_specs=P(("dp", "cent"), None),
        check_vma=False,
    )
```

```python
import itertools

import jax
import jax.numpy as jnp
from jax import lax
from jax.sharding import PartitionSpec as P


def scores_for(piece, cent_bf, squares):
    product = lax.dot_general(
        piece, cent_bf, (((1,), (1,)), ((), ())), preferred_element_type=jnp.float32
    )
    return 0.5 * (2.0 * product - squares[None, :])


def row_summary(logits):
    local_max = jnp.max(logits, axis=1)
    local_sum = jnp.sum(jnp.exp(logits - local_max[:, None]), axis=1)
    return (local_max, local_sum)


def global_stats(local_max, local_sum):
    row_peak = lax.pmax(local_max, ("dp", "cent"))
    row_mass = lax.psum(local_sum * jnp.exp(local_max - row_peak), ("dp", "cent"))
    return (row_peak, row_mass)


def shards_pod(rows, centroids):
    rows_bf = rows.astype(jnp.bfloat16)
    cent_bf = centroids.astype(jnp.bfloat16)
    squares = jnp.sum(centroids * centroids, axis=1)
    gathered = lax.all_gather(rows_bf, "dp", axis=0, tiled=True)
    logits = scores_for(gathered, cent_bf, squares)
    local_max, local_sum = row_summary(logits)
    row_peak, row_mass = global_stats(local_max, local_sum)
    weights = (jnp.exp(logits - row_peak[:, None]) / row_mass[:, None]).astype(jnp.bfloat16)
    weight_sum = jnp.sum(weights.astype(jnp.float32), axis=0)
    pull = lax.dot_general(
        weights, gathered, (((0,), (0,)), ((), ())), preferred_element_type=jnp.float32
    )
    delta = (pull - weight_sum[:, None] * centroids) / (weight_sum[:, None] + 1.0)
    return lax.psum(delta, "outer") / lax.axis_size("outer")


def shards_all(rows, centroids):
    n_o = lax.axis_size("outer")
    n_d = lax.axis_size("dp")
    n_c = lax.axis_size("cent")
    z = lax.axis_index("outer")
    y = lax.axis_index("dp")
    q = lax.axis_index("cent")
    t, d = rows.shape
    tq = t // n_c
    n_od = n_o * n_d

    rows_bf = rows.astype(jnp.bfloat16)
    cent_bf = centroids.astype(jnp.bfloat16)
    squares = jnp.sum(centroids * centroids, axis=1)

    bits = []
    b = 1
    while b < n_c:
        bits.append(b)
        b *= 2
    xs = [0]
    for bit in reversed(bits):
        xs = xs + [x ^ bit for x in xs]

    mine = lax.dynamic_slice_in_dim(rows_bf, q * tq, tq, 0)
    shifts = list(itertools.product(range(n_o), range(n_d)))
    slots = [mine]
    for sz, sy in shifts[1:]:
        perm = []
        for i, j in itertools.product(range(n_o), range(n_d)):
            perm.append((i * n_d + j, ((i + sz) % n_o) * n_d + (j + sy) % n_d))
        slots.append(lax.ppermute(mine, ("outer", "dp"), perm))
    cur = jnp.stack(slots)
    for bit in reversed(bits):
        other = lax.ppermute(cur, "cent", [(i, i ^ bit) for i in range(n_c)])
        cur = jnp.concatenate([cur, other], axis=1)
    everything = cur.reshape(n_od * n_c * tq, d)

    logits = scores_for(everything, cent_bf, squares)
    local_max, local_sum = row_summary(logits)

    src_vec = jnp.stack([((z - sz) % n_o) * n_d + (y - sy) % n_d for sz, sy in shifts])
    hot_k = src_vec[None, :] == jnp.arange(n_od)[:, None]
    c_vec = jnp.stack([q ^ x for x in xs])
    hot_c = c_vec[None, :] == jnp.arange(n_c)[:, None]

    def to_absolute(v):
        v = v.reshape(n_od, n_c, tq)
        v = jnp.sum(jnp.where(hot_c[None, :, :, None], v[:, None, :, :], 0.0), axis=2)
        return jnp.sum(jnp.where(hot_k[:, :, None, None], v[None], 0.0), axis=1)

    def to_local(v):
        v = jnp.sum(jnp.where(hot_k[:, :, None, None], v[:, None], 0.0), axis=0)
        v = jnp.sum(jnp.where(hot_c[:, :, None], v[:, :, None, :], 0.0), axis=1)
        return v.reshape(n_od * n_c * tq)

    both = jnp.stack([to_absolute(local_max), to_absolute(local_sum)])
    every = lax.all_gather(both, ("dp", "cent"), axis=0)
    maxes, sums = every[:, 0], every[:, 1]
    peak_abs = jnp.max(maxes, axis=0)
    mass_abs = jnp.sum(sums * jnp.exp(maxes - peak_abs[None]), axis=0)
    row_peak = to_local(peak_abs)
    row_mass = to_local(mass_abs)

    weights = (jnp.exp(logits - row_peak[:, None]) / row_mass[:, None]).astype(jnp.bfloat16)
    k = centroids.shape[0]
    pod = n_d * n_c * tq
    w_pods = weights.reshape(n_o, pod, k)
    r_pods = everything.reshape(n_o, pod, d)
    weight_sum = jnp.sum(w_pods.astype(jnp.float32), axis=1)
    pull = lax.dot_general(
        w_pods, r_pods, (((1,), (1,)), ((0,), (0,))), preferred_element_type=jnp.float32
    )

    total = None
    for a in range(n_o):
        rel = (z - a) % n_o
        pick_pull = pull[0]
        pick_ws = weight_sum[0]
        for s in range(1, n_o):
            pick_pull = jnp.where(rel == s, pull[s], pick_pull)
            pick_ws = jnp.where(rel == s, weight_sum[s], pick_ws)
        delta = (pick_pull - pick_ws[:, None] * centroids) / (pick_ws[:, None] + 1.0)
        total = delta if total is None else total + delta
    return total / n_o


def solution(mesh):
    n_o, n_d, n_c = mesh.shape["outer"], mesh.shape["dp"], mesh.shape["cent"]

    def shards(rows, centroids):
        t, d = rows.shape
        k = centroids.shape[0]
        n_all = t * n_o * n_d
        footprint = n_all * d * 2 + n_all * k * 4 * 2
        if footprint <= (24 << 20) and t % n_c == 0 and (n_c & (n_c - 1)) == 0:
            return shards_all(rows, centroids)
        return shards_pod(rows, centroids)

    return jax.shard_map(
        shards,
        mesh=mesh,
        in_specs=(P(("outer", "dp"), None), P(("dp", "cent"), None)),
        out_specs=P(("dp", "cent"), None),
        check_vma=False,
    )
```

```python
import itertools

import jax
import jax.numpy as jnp
from jax import lax
from jax.sharding import PartitionSpec as P


def scores_for(piece, cent_bf, squares):
    product = lax.dot_general(
        piece, cent_bf, (((1,), (1,)), ((), ())), preferred_element_type=jnp.float32
    )
    return 0.5 * (2.0 * product - squares[None, :])


def row_summary(logits):
    local_max = jnp.max(logits, axis=1)
    local_sum = jnp.sum(jnp.exp(logits - local_max[:, None]), axis=1)
    return (local_max, local_sum)


def global_stats(local_max, local_sum):
    row_peak = lax.pmax(local_max, ("dp", "cent"))
    row_mass = lax.psum(local_sum * jnp.exp(local_max - row_peak), ("dp", "cent"))
    return (row_peak, row_mass)


def shards_pod(rows, centroids):
    rows_bf = rows.astype(jnp.bfloat16)
    cent_bf = centroids.astype(jnp.bfloat16)
    squares = jnp.sum(centroids * centroids, axis=1)
    gathered = lax.all_gather(rows_bf, "dp", axis=0, tiled=True)
    logits = scores_for(gathered, cent_bf, squares)
    local_max, local_sum = row_summary(logits)
    row_peak, row_mass = global_stats(local_max, local_sum)
    weights = (jnp.exp(logits - row_peak[:, None]) / row_mass[:, None]).astype(jnp.bfloat16)
    weight_sum = jnp.sum(weights.astype(jnp.float32), axis=0)
    pull = lax.dot_general(
        weights, gathered, (((0,), (0,)), ((), ())), preferred_element_type=jnp.float32
    )
    delta = (pull - weight_sum[:, None] * centroids) / (weight_sum[:, None] + 1.0)
    return lax.psum(delta, "outer") / lax.axis_size("outer")


def shards_all(rows, centroids):
    n_o = lax.axis_size("outer")
    n_d = lax.axis_size("dp")
    n_c = lax.axis_size("cent")
    z = lax.axis_index("outer")
    y = lax.axis_index("dp")
    q = lax.axis_index("cent")
    t, d = rows.shape
    tq = t // n_c
    n_od = n_o * n_d

    rows_bf = rows.astype(jnp.bfloat16)
    cent_bf = centroids.astype(jnp.bfloat16)
    squares = jnp.sum(centroids * centroids, axis=1)

    bits = []
    b = 1
    while b < n_c:
        bits.append(b)
        b *= 2
    xs = [0]
    for bit in reversed(bits):
        xs = xs + [x ^ bit for x in xs]

    mine = lax.dynamic_slice_in_dim(rows_bf, q * tq, tq, 0)
    shifts = list(itertools.product(range(n_o), range(n_d)))
    slots = [mine]
    for sz, sy in shifts[1:]:
        perm = []
        for i, j in itertools.product(range(n_o), range(n_d)):
            perm.append((i * n_d + j, ((i + sz) % n_o) * n_d + (j + sy) % n_d))
        slots.append(lax.ppermute(mine, ("outer", "dp"), perm))
    groups = 2 if n_od % 2 == 0 else 1
    per = n_od // groups
    parts = []
    for g in range(groups):
        cur = jnp.stack(slots[g * per:(g + 1) * per])
        for bit in reversed(bits):
            other = lax.ppermute(cur, "cent", [(i, i ^ bit) for i in range(n_c)])
            cur = jnp.concatenate([cur, other], axis=1)
        parts.append(cur)
    cur = jnp.concatenate(parts, axis=0)
    everything = cur.reshape(n_od * n_c * tq, d)

    logits = scores_for(everything, cent_bf, squares)
    local_max, local_sum = row_summary(logits)

    src_vec = jnp.stack([((z - sz) % n_o) * n_d + (y - sy) % n_d for sz, sy in shifts])
    hot_k = src_vec[None, :] == jnp.arange(n_od)[:, None]
    c_vec = jnp.stack([q ^ x for x in xs])
    hot_c = c_vec[None, :] == jnp.arange(n_c)[:, None]

    def to_absolute(v):
        v = v.reshape(n_od, n_c, tq)
        v = jnp.sum(jnp.where(hot_c[None, :, :, None], v[:, None, :, :], 0.0), axis=2)
        return jnp.sum(jnp.where(hot_k[:, :, None, None], v[None], 0.0), axis=1)

    def to_local(v):
        v = jnp.sum(jnp.where(hot_k[:, :, None, None], v[:, None], 0.0), axis=0)
        v = jnp.sum(jnp.where(hot_c[:, :, None], v[:, :, None, :], 0.0), axis=1)
        return v.reshape(n_od * n_c * tq)

    both = jnp.stack([to_absolute(local_max), to_absolute(local_sum)])
    every = lax.all_gather(both, ("dp", "cent"), axis=0)
    maxes, sums = every[:, 0], every[:, 1]
    peak_abs = jnp.max(maxes, axis=0)
    mass_abs = jnp.sum(sums * jnp.exp(maxes - peak_abs[None]), axis=0)
    row_peak = to_local(peak_abs)
    row_mass = to_local(mass_abs)

    weights = (jnp.exp(logits - row_peak[:, None]) / row_mass[:, None]).astype(jnp.bfloat16)
    k = centroids.shape[0]
    pod = n_d * n_c * tq
    w_pods = weights.reshape(n_o, pod, k)
    r_pods = everything.reshape(n_o, pod, d)
    weight_sum = jnp.sum(w_pods.astype(jnp.float32), axis=1)
    pull = lax.dot_general(
        w_pods, r_pods, (((1,), (1,)), ((0,), (0,))), preferred_element_type=jnp.float32
    )

    total = None
    for a in range(n_o):
        rel = (z - a) % n_o
        pick_pull = pull[0]
        pick_ws = weight_sum[0]
        for s in range(1, n_o):
            pick_pull = jnp.where(rel == s, pull[s], pick_pull)
            pick_ws = jnp.where(rel == s, weight_sum[s], pick_ws)
        delta = (pick_pull - pick_ws[:, None] * centroids) / (pick_ws[:, None] + 1.0)
        total = delta if total is None else total + delta
    return total / n_o


def solution(mesh):
    n_o, n_d, n_c = mesh.shape["outer"], mesh.shape["dp"], mesh.shape["cent"]

    def shards(rows, centroids):
        t, d = rows.shape
        k = centroids.shape[0]
        n_all = t * n_o * n_d
        footprint = n_all * d * 2 + n_all * k * 4 * 2
        if footprint <= (24 << 20) and t % n_c == 0 and (n_c & (n_c - 1)) == 0:
            return shards_all(rows, centroids)
        return shards_pod(rows, centroids)

    return jax.shard_map(
        shards,
        mesh=mesh,
        in_specs=(P(("outer", "dp"), None), P(("dp", "cent"), None)),
        out_specs=P(("dp", "cent"), None),
        check_vma=False,
    )
```

```python
import itertools

import jax
import jax.numpy as jnp
from jax import lax
from jax.sharding import PartitionSpec as P


def scores_for(piece, cent_bf, squares):
    product = lax.dot_general(
        piece, cent_bf, (((1,), (1,)), ((), ())), preferred_element_type=jnp.float32
    )
    return 0.5 * (2.0 * product - squares[None, :])


def row_summary(logits):
    local_max = jnp.max(logits, axis=1)
    local_sum = jnp.sum(jnp.exp(logits - local_max[:, None]), axis=1)
    return (local_max, local_sum)


def global_stats(local_max, local_sum):
    row_peak = lax.pmax(local_max, ("dp", "cent"))
    row_mass = lax.psum(local_sum * jnp.exp(local_max - row_peak), ("dp", "cent"))
    return (row_peak, row_mass)


def shards_pod(rows, centroids):
    rows_bf = rows.astype(jnp.bfloat16)
    cent_bf = centroids.astype(jnp.bfloat16)
    squares = jnp.sum(centroids * centroids, axis=1)
    gathered = lax.all_gather(rows_bf, "dp", axis=0, tiled=True)
    logits = scores_for(gathered, cent_bf, squares)
    local_max, local_sum = row_summary(logits)
    row_peak, row_mass = global_stats(local_max, local_sum)
    weights = (jnp.exp(logits - row_peak[:, None]) / row_mass[:, None]).astype(jnp.bfloat16)
    weight_sum = jnp.sum(weights.astype(jnp.float32), axis=0)
    pull = lax.dot_general(
        weights, gathered, (((0,), (0,)), ((), ())), preferred_element_type=jnp.float32
    )
    delta = (pull - weight_sum[:, None] * centroids) / (weight_sum[:, None] + 1.0)
    return lax.psum(delta, "outer") / lax.axis_size("outer")


def shards_all(rows, centroids):
    n_o = lax.axis_size("outer")
    n_d = lax.axis_size("dp")
    n_c = lax.axis_size("cent")
    z = lax.axis_index("outer")
    y = lax.axis_index("dp")
    q = lax.axis_index("cent")
    t, d = rows.shape
    tq = t // n_c
    n_od = n_o * n_d

    rows_bf = rows.astype(jnp.bfloat16)
    cent_bf = centroids.astype(jnp.bfloat16)
    squares = jnp.sum(centroids * centroids, axis=1)

    bits = []
    b = 1
    while b < n_c:
        bits.append(b)
        b *= 2
    xs = [0]
    for bit in reversed(bits):
        xs = xs + [x ^ bit for x in xs]

    mine = lax.dynamic_slice_in_dim(rows_bf, q * tq, tq, 0)
    shifts = list(itertools.product(range(n_o), range(n_d)))
    across = [mine]
    for sy in range(1, n_d):
        across.append(lax.ppermute(mine, "dp", [(j, (j + sy) % n_d) for j in range(n_d)]))
    pair = jnp.stack(across)

    def spread(cur):
        for bit in reversed(bits):
            other = lax.ppermute(cur, "cent", [(i, i ^ bit) for i in range(n_c)])
            cur = jnp.concatenate([cur, other], axis=1)
        return cur

    parts = [spread(pair)]
    for sz in range(1, n_o):
        moved = lax.ppermute(pair, "outer", [(i, (i + sz) % n_o) for i in range(n_o)])
        parts.append(spread(moved))
    cur = jnp.concatenate(parts, axis=0)
    everything = cur.reshape(n_od * n_c * tq, d)

    logits = scores_for(everything, cent_bf, squares)
    local_max, local_sum = row_summary(logits)

    src_vec = jnp.stack([((z - sz) % n_o) * n_d + (y - sy) % n_d for sz, sy in shifts])
    hot_k = src_vec[None, :] == jnp.arange(n_od)[:, None]
    c_vec = jnp.stack([q ^ x for x in xs])
    hot_c = c_vec[None, :] == jnp.arange(n_c)[:, None]

    def to_absolute(v):
        v = v.reshape(n_od, n_c, tq)
        v = jnp.sum(jnp.where(hot_c[None, :, :, None], v[:, None, :, :], 0.0), axis=2)
        return jnp.sum(jnp.where(hot_k[:, :, None, None], v[None], 0.0), axis=1)

    def to_local(v):
        v = jnp.sum(jnp.where(hot_k[:, :, None, None], v[:, None], 0.0), axis=0)
        v = jnp.sum(jnp.where(hot_c[:, :, None], v[:, :, None, :], 0.0), axis=1)
        return v.reshape(n_od * n_c * tq)

    both = jnp.stack([to_absolute(local_max), to_absolute(local_sum)])
    every = lax.all_gather(both, ("dp", "cent"), axis=0)
    maxes, sums = every[:, 0], every[:, 1]
    peak_abs = jnp.max(maxes, axis=0)
    mass_abs = jnp.sum(sums * jnp.exp(maxes - peak_abs[None]), axis=0)
    row_peak = to_local(peak_abs)
    row_mass = to_local(mass_abs)

    weights = (jnp.exp(logits - row_peak[:, None]) / row_mass[:, None]).astype(jnp.bfloat16)
    k = centroids.shape[0]
    pod = n_d * n_c * tq
    w_pods = weights.reshape(n_o, pod, k)
    r_pods = everything.reshape(n_o, pod, d)
    weight_sum = jnp.sum(w_pods.astype(jnp.float32), axis=1)
    pull = lax.dot_general(
        w_pods, r_pods, (((1,), (1,)), ((0,), (0,))), preferred_element_type=jnp.float32
    )

    total = None
    for a in range(n_o):
        rel = (z - a) % n_o
        pick_pull = pull[0]
        pick_ws = weight_sum[0]
        for s in range(1, n_o):
            pick_pull = jnp.where(rel == s, pull[s], pick_pull)
            pick_ws = jnp.where(rel == s, weight_sum[s], pick_ws)
        delta = (pick_pull - pick_ws[:, None] * centroids) / (pick_ws[:, None] + 1.0)
        total = delta if total is None else total + delta
    return total / n_o


def solution(mesh):
    n_o, n_d, n_c = mesh.shape["outer"], mesh.shape["dp"], mesh.shape["cent"]

    def shards(rows, centroids):
        t, d = rows.shape
        k = centroids.shape[0]
        n_all = t * n_o * n_d
        footprint = n_all * d * 2 + n_all * k * 4 * 2
        if footprint <= (24 << 20) and t % n_c == 0 and (n_c & (n_c - 1)) == 0:
            return shards_all(rows, centroids)
        return shards_pod(rows, centroids)

    return jax.shard_map(
        shards,
        mesh=mesh,
        in_specs=(P(("outer", "dp"), None), P(("dp", "cent"), None)),
        out_specs=P(("dp", "cent"), None),
        check_vma=False,
    )
```

```python
import itertools

import jax
import jax.numpy as jnp
from jax import lax
from jax.sharding import PartitionSpec as P


def scores_for(piece, cent_bf, squares):
    product = lax.dot_general(
        piece, cent_bf, (((1,), (1,)), ((), ())), preferred_element_type=jnp.float32
    )
    return 0.5 * (2.0 * product - squares[None, :])


def row_summary(logits):
    local_max = jnp.max(logits, axis=1)
    local_sum = jnp.sum(jnp.exp(logits - local_max[:, None]), axis=1)
    return (local_max, local_sum)


def global_stats(local_max, local_sum):
    row_peak = lax.pmax(local_max, ("dp", "cent"))
    row_mass = lax.psum(local_sum * jnp.exp(local_max - row_peak), ("dp", "cent"))
    return (row_peak, row_mass)


def shards_pod(rows, centroids):
    rows_bf = rows.astype(jnp.bfloat16)
    cent_bf = centroids.astype(jnp.bfloat16)
    squares = jnp.sum(centroids * centroids, axis=1)
    gathered = lax.all_gather(rows_bf, "dp", axis=0, tiled=True)
    logits = scores_for(gathered, cent_bf, squares)
    local_max, local_sum = row_summary(logits)
    row_peak, row_mass = global_stats(local_max, local_sum)
    weights = (jnp.exp(logits - row_peak[:, None]) / row_mass[:, None]).astype(jnp.bfloat16)
    weight_sum = jnp.sum(weights.astype(jnp.float32), axis=0)
    pull = lax.dot_general(
        weights, gathered, (((0,), (0,)), ((), ())), preferred_element_type=jnp.float32
    )
    delta = (pull - weight_sum[:, None] * centroids) / (weight_sum[:, None] + 1.0)
    return lax.psum(delta, "outer") / lax.axis_size("outer")


def shards_all(rows, centroids):
    n_o = lax.axis_size("outer")
    n_d = lax.axis_size("dp")
    n_c = lax.axis_size("cent")
    z = lax.axis_index("outer")
    y = lax.axis_index("dp")
    q = lax.axis_index("cent")
    t, d = rows.shape
    tq = t // n_c
    n_od = n_o * n_d

    rows_bf = rows.astype(jnp.bfloat16)
    cent_bf = centroids.astype(jnp.bfloat16)
    squares = jnp.sum(centroids * centroids, axis=1)

    bits = []
    b = 1
    while b < n_c:
        bits.append(b)
        b *= 2
    xs = [0]
    for bit in reversed(bits):
        xs = xs + [x ^ bit for x in xs]

    mine = lax.dynamic_slice_in_dim(rows_bf, q * tq, tq, 0)
    shifts = list(itertools.product(range(n_o), range(n_d)))
    across = [mine]
    for sy in range(1, n_d):
        across.append(lax.ppermute(mine, "dp", [(j, (j + sy) % n_d) for j in range(n_d)]))
    pair = jnp.stack(across)

    def spread(cur):
        for bit in reversed(bits):
            other = lax.ppermute(cur, "cent", [(i, i ^ bit) for i in range(n_c)])
            cur = jnp.concatenate([cur, other], axis=1)
        return cur

    parts = [spread(pair)]
    for sz in range(1, n_o):
        moved = lax.ppermute(pair, "outer", [(i, (i + sz) % n_o) for i in range(n_o)])
        parts.append(spread(moved))
    part_rows = [p.reshape(n_d * n_c * tq, d) for p in parts]
    part_logits = [scores_for(r, cent_bf, squares) for r in part_rows]
    part_stats = [row_summary(lg) for lg in part_logits]
    local_max = jnp.concatenate([st[0] for st in part_stats])
    local_sum = jnp.concatenate([st[1] for st in part_stats])
    cur = jnp.concatenate(parts, axis=0)
    everything = cur.reshape(n_od * n_c * tq, d)

    logits = jnp.concatenate(part_logits, axis=0)

    src_vec = jnp.stack([((z - sz) % n_o) * n_d + (y - sy) % n_d for sz, sy in shifts])
    hot_k = src_vec[None, :] == jnp.arange(n_od)[:, None]
    c_vec = jnp.stack([q ^ x for x in xs])
    hot_c = c_vec[None, :] == jnp.arange(n_c)[:, None]

    def to_absolute(v):
        v = v.reshape(n_od, n_c, tq)
        v = jnp.sum(jnp.where(hot_c[None, :, :, None], v[:, None, :, :], 0.0), axis=2)
        return jnp.sum(jnp.where(hot_k[:, :, None, None], v[None], 0.0), axis=1)

    def to_local(v):
        v = jnp.sum(jnp.where(hot_k[:, :, None, None], v[:, None], 0.0), axis=0)
        v = jnp.sum(jnp.where(hot_c[:, :, None], v[:, :, None, :], 0.0), axis=1)
        return v.reshape(n_od * n_c * tq)

    both = jnp.stack([to_absolute(local_max), to_absolute(local_sum)])
    every = lax.all_gather(both, ("dp", "cent"), axis=0)
    maxes, sums = every[:, 0], every[:, 1]
    peak_abs = jnp.max(maxes, axis=0)
    mass_abs = jnp.sum(sums * jnp.exp(maxes - peak_abs[None]), axis=0)
    row_peak = to_local(peak_abs)
    row_mass = to_local(mass_abs)

    weights = (jnp.exp(logits - row_peak[:, None]) / row_mass[:, None]).astype(jnp.bfloat16)
    k = centroids.shape[0]
    pod = n_d * n_c * tq
    w_pods = weights.reshape(n_o, pod, k)
    r_pods = everything.reshape(n_o, pod, d)
    weight_sum = jnp.sum(w_pods.astype(jnp.float32), axis=1)
    pull = lax.dot_general(
        w_pods, r_pods, (((1,), (1,)), ((0,), (0,))), preferred_element_type=jnp.float32
    )

    total = None
    for a in range(n_o):
        rel = (z - a) % n_o
        pick_pull = pull[0]
        pick_ws = weight_sum[0]
        for s in range(1, n_o):
            pick_pull = jnp.where(rel == s, pull[s], pick_pull)
            pick_ws = jnp.where(rel == s, weight_sum[s], pick_ws)
        delta = (pick_pull - pick_ws[:, None] * centroids) / (pick_ws[:, None] + 1.0)
        total = delta if total is None else total + delta
    return total / n_o


def solution(mesh):
    n_o, n_d, n_c = mesh.shape["outer"], mesh.shape["dp"], mesh.shape["cent"]

    def shards(rows, centroids):
        t, d = rows.shape
        k = centroids.shape[0]
        n_all = t * n_o * n_d
        footprint = n_all * d * 2 + n_all * k * 4 * 2
        if footprint <= (24 << 20) and t % n_c == 0 and (n_c & (n_c - 1)) == 0:
            return shards_all(rows, centroids)
        return shards_pod(rows, centroids)

    return jax.shard_map(
        shards,
        mesh=mesh,
        in_specs=(P(("outer", "dp"), None), P(("dp", "cent"), None)),
        out_specs=P(("dp", "cent"), None),
        check_vma=False,
    )
```

```python
import itertools

import jax
import jax.numpy as jnp
from jax import lax
from jax.sharding import PartitionSpec as P


def scores_for(piece, cent_bf, squares):
    product = lax.dot_general(
        piece, cent_bf, (((1,), (1,)), ((), ())), preferred_element_type=jnp.float32
    )
    return 0.5 * (2.0 * product - squares[None, :])


def row_summary(logits):
    local_max = jnp.max(logits, axis=1)
    local_sum = jnp.sum(jnp.exp(logits - local_max[:, None]), axis=1)
    return (local_max, local_sum)


def global_stats(local_max, local_sum):
    row_peak = lax.pmax(local_max, ("dp", "cent"))
    row_mass = lax.psum(local_sum * jnp.exp(local_max - row_peak), ("dp", "cent"))
    return (row_peak, row_mass)


def shards_pod(rows, centroids):
    rows_bf = rows.astype(jnp.bfloat16)
    cent_bf = centroids.astype(jnp.bfloat16)
    squares = jnp.sum(centroids * centroids, axis=1)
    gathered = lax.all_gather(rows_bf, "dp", axis=0, tiled=True)
    logits = scores_for(gathered, cent_bf, squares)
    local_max, local_sum = row_summary(logits)
    row_peak, row_mass = global_stats(local_max, local_sum)
    weights = (jnp.exp(logits - row_peak[:, None]) / row_mass[:, None]).astype(jnp.bfloat16)
    weight_sum = jnp.sum(weights.astype(jnp.float32), axis=0)
    pull = lax.dot_general(
        weights, gathered, (((0,), (0,)), ((), ())), preferred_element_type=jnp.float32
    )
    delta = (pull - weight_sum[:, None] * centroids) / (weight_sum[:, None] + 1.0)
    return lax.psum(delta, "outer") / lax.axis_size("outer")


def shards_all(rows, centroids):
    n_o = lax.axis_size("outer")
    n_d = lax.axis_size("dp")
    n_c = lax.axis_size("cent")
    z = lax.axis_index("outer")
    y = lax.axis_index("dp")
    q = lax.axis_index("cent")
    t, d = rows.shape
    tq = t // n_c
    n_od = n_o * n_d

    rows_bf = rows.astype(jnp.bfloat16)
    cent_bf = centroids.astype(jnp.bfloat16)
    squares = jnp.sum(centroids * centroids, axis=1)

    bits = []
    b = 1
    while b < n_c:
        bits.append(b)
        b *= 2
    xs = [0]
    for bit in reversed(bits):
        xs = xs + [x ^ bit for x in xs]

    mine = lax.dynamic_slice_in_dim(rows_bf, q * tq, tq, 0)
    shifts = list(itertools.product(range(n_o), range(n_d)))
    def pair_of(piece):
        across = [piece]
        for sy in range(1, n_d):
            across.append(lax.ppermute(piece, "dp", [(j, (j + sy) % n_d) for j in range(n_d)]))
        return jnp.stack(across)

    def spread(cur):
        for bit in reversed(bits):
            other = lax.ppermute(cur, "cent", [(i, i ^ bit) for i in range(n_c)])
            cur = jnp.concatenate([cur, other], axis=1)
        return cur

    landed = [mine]
    for sz in range(1, n_o):
        landed.append(lax.ppermute(mine, "outer", [(i, (i + sz) % n_o) for i in range(n_o)]))
    parts = [spread(pair_of(piece)) for piece in landed]
    cur = jnp.concatenate(parts, axis=0)
    everything = cur.reshape(n_od * n_c * tq, d)

    logits = scores_for(everything, cent_bf, squares)
    local_max, local_sum = row_summary(logits)

    src_vec = jnp.stack([((z - sz) % n_o) * n_d + (y - sy) % n_d for sz, sy in shifts])
    hot_k = src_vec[None, :] == jnp.arange(n_od)[:, None]
    c_vec = jnp.stack([q ^ x for x in xs])
    hot_c = c_vec[None, :] == jnp.arange(n_c)[:, None]

    def to_absolute(v):
        v = v.reshape(n_od, n_c, tq)
        v = jnp.sum(jnp.where(hot_c[None, :, :, None], v[:, None, :, :], 0.0), axis=2)
        return jnp.sum(jnp.where(hot_k[:, :, None, None], v[None], 0.0), axis=1)

    def to_local(v):
        v = jnp.sum(jnp.where(hot_k[:, :, None, None], v[:, None], 0.0), axis=0)
        v = jnp.sum(jnp.where(hot_c[:, :, None], v[:, :, None, :], 0.0), axis=1)
        return v.reshape(n_od * n_c * tq)

    both = jnp.stack([to_absolute(local_max), to_absolute(local_sum)])
    every = lax.all_gather(both, ("dp", "cent"), axis=0)
    maxes, sums = every[:, 0], every[:, 1]
    peak_abs = jnp.max(maxes, axis=0)
    mass_abs = jnp.sum(sums * jnp.exp(maxes - peak_abs[None]), axis=0)
    row_peak = to_local(peak_abs)
    row_mass = to_local(mass_abs)

    weights = (jnp.exp(logits - row_peak[:, None]) / row_mass[:, None]).astype(jnp.bfloat16)
    k = centroids.shape[0]
    pod = n_d * n_c * tq
    w_pods = weights.reshape(n_o, pod, k)
    r_pods = everything.reshape(n_o, pod, d)
    weight_sum = jnp.sum(w_pods.astype(jnp.float32), axis=1)
    pull = lax.dot_general(
        w_pods, r_pods, (((1,), (1,)), ((0,), (0,))), preferred_element_type=jnp.float32
    )

    total = None
    for a in range(n_o):
        rel = (z - a) % n_o
        pick_pull = pull[0]
        pick_ws = weight_sum[0]
        for s in range(1, n_o):
            pick_pull = jnp.where(rel == s, pull[s], pick_pull)
            pick_ws = jnp.where(rel == s, weight_sum[s], pick_ws)
        delta = (pick_pull - pick_ws[:, None] * centroids) / (pick_ws[:, None] + 1.0)
        total = delta if total is None else total + delta
    return total / n_o


def solution(mesh):
    n_o, n_d, n_c = mesh.shape["outer"], mesh.shape["dp"], mesh.shape["cent"]

    def shards(rows, centroids):
        t, d = rows.shape
        k = centroids.shape[0]
        n_all = t * n_o * n_d
        footprint = n_all * d * 2 + n_all * k * 4 * 2
        if footprint <= (24 << 20) and t % n_c == 0 and (n_c & (n_c - 1)) == 0:
            return shards_all(rows, centroids)
        return shards_pod(rows, centroids)

    return jax.shard_map(
        shards,
        mesh=mesh,
        in_specs=(P(("outer", "dp"), None), P(("dp", "cent"), None)),
        out_specs=P(("dp", "cent"), None),
        check_vma=False,
    )
```

```python
import itertools

import jax
import jax.numpy as jnp
from jax import lax
from jax.sharding import PartitionSpec as P


def scores_for(piece, cent_bf, squares):
    product = lax.dot_general(
        piece, cent_bf, (((1,), (1,)), ((), ())), preferred_element_type=jnp.float32
    )
    return 0.5 * (2.0 * product - squares[None, :])


def row_summary(logits):
    local_max = jnp.max(logits, axis=1)
    local_sum = jnp.sum(jnp.exp(logits - local_max[:, None]), axis=1)
    return (local_max, local_sum)


def global_stats(local_max, local_sum):
    row_peak = lax.pmax(local_max, ("dp", "cent"))
    row_mass = lax.psum(local_sum * jnp.exp(local_max - row_peak), ("dp", "cent"))
    return (row_peak, row_mass)


def shards_pod(rows, centroids):
    rows_bf = rows.astype(jnp.bfloat16)
    cent_bf = centroids.astype(jnp.bfloat16)
    squares = jnp.sum(centroids * centroids, axis=1)
    gathered = lax.all_gather(rows_bf, "dp", axis=0, tiled=True)
    logits = scores_for(gathered, cent_bf, squares)
    local_max, local_sum = row_summary(logits)
    row_peak, row_mass = global_stats(local_max, local_sum)
    weights = (jnp.exp(logits - row_peak[:, None]) / row_mass[:, None]).astype(jnp.bfloat16)
    weight_sum = jnp.sum(weights.astype(jnp.float32), axis=0)
    pull = lax.dot_general(
        weights, gathered, (((0,), (0,)), ((), ())), preferred_element_type=jnp.float32
    )
    delta = (pull - weight_sum[:, None] * centroids) / (weight_sum[:, None] + 1.0)
    return lax.psum(delta, "outer") / lax.axis_size("outer")


def shards_all(rows, centroids):
    n_o = lax.axis_size("outer")
    n_d = lax.axis_size("dp")
    n_c = lax.axis_size("cent")
    z = lax.axis_index("outer")
    y = lax.axis_index("dp")
    q = lax.axis_index("cent")
    t, d = rows.shape
    tq = t // n_c
    n_od = n_o * n_d

    rows_bf = rows.astype(jnp.bfloat16)
    cent_bf = centroids.astype(jnp.bfloat16)
    squares = jnp.sum(centroids * centroids, axis=1)

    bits = []
    b = 1
    while b < n_c:
        bits.append(b)
        b *= 2
    xs = [0]
    for bit in reversed(bits):
        xs = xs + [x ^ bit for x in xs]

    mine = lax.dynamic_slice_in_dim(rows_bf, q * tq, tq, 0)
    shifts = list(itertools.product(range(n_o), range(n_d)))
    def spread(cur):
        for bit in reversed(bits):
            other = lax.ppermute(cur, "cent", [(i, i ^ bit) for i in range(n_c)])
            cur = jnp.concatenate([cur, other], axis=1)
        return cur

    parts = []
    for sz in range(n_o):
        group = []
        for sy in range(n_d):
            if (sz, sy) == (0, 0):
                group.append(mine)
                continue
            perm = []
            for i, j in itertools.product(range(n_o), range(n_d)):
                perm.append((i * n_d + j, ((i + sz) % n_o) * n_d + (j + sy) % n_d))
            group.append(lax.ppermute(mine, ("outer", "dp"), perm))
        parts.append(spread(jnp.stack(group)))
    cur = jnp.concatenate(parts, axis=0)
    everything = cur.reshape(n_od * n_c * tq, d)

    logits = scores_for(everything, cent_bf, squares)
    local_max, local_sum = row_summary(logits)

    src_vec = jnp.stack([((z - sz) % n_o) * n_d + (y - sy) % n_d for sz, sy in shifts])
    hot_k = src_vec[None, :] == jnp.arange(n_od)[:, None]
    c_vec = jnp.stack([q ^ x for x in xs])
    hot_c = c_vec[None, :] == jnp.arange(n_c)[:, None]

    def to_absolute(v):
        v = v.reshape(n_od, n_c, tq)
        v = jnp.sum(jnp.where(hot_c[None, :, :, None], v[:, None, :, :], 0.0), axis=2)
        return jnp.sum(jnp.where(hot_k[:, :, None, None], v[None], 0.0), axis=1)

    def to_local(v):
        v = jnp.sum(jnp.where(hot_k[:, :, None, None], v[:, None], 0.0), axis=0)
        v = jnp.sum(jnp.where(hot_c[:, :, None], v[:, :, None, :], 0.0), axis=1)
        return v.reshape(n_od * n_c * tq)

    both = jnp.stack([to_absolute(local_max), to_absolute(local_sum)])
    every = lax.all_gather(both, ("dp", "cent"), axis=0)
    maxes, sums = every[:, 0], every[:, 1]
    peak_abs = jnp.max(maxes, axis=0)
    mass_abs = jnp.sum(sums * jnp.exp(maxes - peak_abs[None]), axis=0)
    row_peak = to_local(peak_abs)
    row_mass = to_local(mass_abs)

    weights = (jnp.exp(logits - row_peak[:, None]) / row_mass[:, None]).astype(jnp.bfloat16)
    k = centroids.shape[0]
    pod = n_d * n_c * tq
    w_pods = weights.reshape(n_o, pod, k)
    r_pods = everything.reshape(n_o, pod, d)
    weight_sum = jnp.sum(w_pods.astype(jnp.float32), axis=1)
    pull = lax.dot_general(
        w_pods, r_pods, (((1,), (1,)), ((0,), (0,))), preferred_element_type=jnp.float32
    )

    total = None
    for a in range(n_o):
        rel = (z - a) % n_o
        pick_pull = pull[0]
        pick_ws = weight_sum[0]
        for s in range(1, n_o):
            pick_pull = jnp.where(rel == s, pull[s], pick_pull)
            pick_ws = jnp.where(rel == s, weight_sum[s], pick_ws)
        delta = (pick_pull - pick_ws[:, None] * centroids) / (pick_ws[:, None] + 1.0)
        total = delta if total is None else total + delta
    return total / n_o


def solution(mesh):
    n_o, n_d, n_c = mesh.shape["outer"], mesh.shape["dp"], mesh.shape["cent"]

    def shards(rows, centroids):
        t, d = rows.shape
        k = centroids.shape[0]
        n_all = t * n_o * n_d
        footprint = n_all * d * 2 + n_all * k * 4 * 2
        if footprint <= (24 << 20) and t % n_c == 0 and (n_c & (n_c - 1)) == 0:
            return shards_all(rows, centroids)
        return shards_pod(rows, centroids)

    return jax.shard_map(
        shards,
        mesh=mesh,
        in_specs=(P(("outer", "dp"), None), P(("dp", "cent"), None)),
        out_specs=P(("dp", "cent"), None),
        check_vma=False,
    )
```

```python
import itertools

import jax
import jax.numpy as jnp
from jax import lax
from jax.sharding import PartitionSpec as P


def scores_for(piece, cent_bf, squares):
    product = lax.dot_general(
        piece, cent_bf, (((1,), (1,)), ((), ())), preferred_element_type=jnp.float32
    )
    return 0.5 * (2.0 * product - squares[None, :])


def row_summary(logits):
    local_max = jnp.max(logits, axis=1)
    local_sum = jnp.sum(jnp.exp(logits - local_max[:, None]), axis=1)
    return (local_max, local_sum)


def global_stats(local_max, local_sum):
    row_peak = lax.pmax(local_max, ("dp", "cent"))
    row_mass = lax.psum(local_sum * jnp.exp(local_max - row_peak), ("dp", "cent"))
    return (row_peak, row_mass)


def shards_pod(rows, centroids):
    rows_bf = rows.astype(jnp.bfloat16)
    cent_bf = centroids.astype(jnp.bfloat16)
    squares = jnp.sum(centroids * centroids, axis=1)
    gathered = lax.all_gather(rows_bf, "dp", axis=0, tiled=True)
    logits = scores_for(gathered, cent_bf, squares)
    local_max, local_sum = row_summary(logits)
    row_peak, row_mass = global_stats(local_max, local_sum)
    weights = (jnp.exp(logits - row_peak[:, None]) / row_mass[:, None]).astype(jnp.bfloat16)
    weight_sum = jnp.sum(weights.astype(jnp.float32), axis=0)
    pull = lax.dot_general(
        weights, gathered, (((0,), (0,)), ((), ())), preferred_element_type=jnp.float32
    )
    delta = (pull - weight_sum[:, None] * centroids) / (weight_sum[:, None] + 1.0)
    return lax.psum(delta, "outer") / lax.axis_size("outer")


def shards_all(rows, centroids):
    n_o = lax.axis_size("outer")
    n_d = lax.axis_size("dp")
    n_c = lax.axis_size("cent")
    z = lax.axis_index("outer")
    y = lax.axis_index("dp")
    q = lax.axis_index("cent")
    t, d = rows.shape
    tq = t // n_c
    n_od = n_o * n_d

    rows_bf = rows.astype(jnp.bfloat16)
    cent_bf = centroids.astype(jnp.bfloat16)
    squares = jnp.sum(centroids * centroids, axis=1)

    bits = []
    b = 1
    while b < n_c:
        bits.append(b)
        b *= 2
    xs = [0]
    for bit in reversed(bits):
        xs = xs + [x ^ bit for x in xs]

    mine = lax.dynamic_slice_in_dim(rows_bf, q * tq, tq, 0)
    shifts = list(itertools.product(range(n_o), range(n_d)))
    def pair_of(piece):
        across = [piece]
        for sy in range(1, n_d):
            across.append(lax.ppermute(piece, "dp", [(j, (j + sy) % n_d) for j in range(n_d)]))
        return jnp.stack(across)

    def spread(cur):
        for bit in reversed(bits):
            other = lax.ppermute(cur, "cent", [(i, i ^ bit) for i in range(n_c)])
            cur = jnp.concatenate([cur, other], axis=1)
        return cur

    landed = [mine]
    for sz in range(1, n_o):
        landed.append(lax.ppermute(mine, "outer", [(i, (i + sz) % n_o) for i in range(n_o)]))
    parts = [spread(pair_of(piece)) for piece in landed]
    cur = jnp.zeros((n_o * n_d,) + parts[0].shape[1:], parts[0].dtype)
    for sz in range(n_o):
        cur = lax.dynamic_update_slice_in_dim(cur, parts[sz], ((z - sz) % n_o) * n_d, axis=0)
    everything = cur.reshape(n_od * n_c * tq, d)

    logits = scores_for(everything, cent_bf, squares)
    local_max, local_sum = row_summary(logits)

    src_vec = jnp.stack([a * n_d + (y - sy) % n_d for a, sy in shifts])
    hot_k = src_vec[None, :] == jnp.arange(n_od)[:, None]
    c_vec = jnp.stack([q ^ x for x in xs])
    hot_c = c_vec[None, :] == jnp.arange(n_c)[:, None]

    def to_absolute(v):
        v = v.reshape(n_od, n_c, tq)
        v = jnp.sum(jnp.where(hot_c[None, :, :, None], v[:, None, :, :], 0.0), axis=2)
        return jnp.sum(jnp.where(hot_k[:, :, None, None], v[None], 0.0), axis=1)

    def to_local(v):
        v = jnp.sum(jnp.where(hot_k[:, :, None, None], v[:, None], 0.0), axis=0)
        v = jnp.sum(jnp.where(hot_c[:, :, None], v[:, :, None, :], 0.0), axis=1)
        return v.reshape(n_od * n_c * tq)

    both = jnp.stack([to_absolute(local_max), to_absolute(local_sum)])
    every = lax.all_gather(both, ("dp", "cent"), axis=0)
    maxes, sums = every[:, 0], every[:, 1]
    peak_abs = jnp.max(maxes, axis=0)
    mass_abs = jnp.sum(sums * jnp.exp(maxes - peak_abs[None]), axis=0)
    row_peak = to_local(peak_abs)
    row_mass = to_local(mass_abs)

    weights = (jnp.exp(logits - row_peak[:, None]) / row_mass[:, None]).astype(jnp.bfloat16)
    k = centroids.shape[0]
    pod = n_d * n_c * tq
    w_pods = weights.reshape(n_o, pod, k).astype(jnp.float32)
    weight_sum = jnp.sum(w_pods, axis=1)
    scaled = (w_pods / (weight_sum[:, None, :] + 1.0)).astype(jnp.bfloat16)
    pull = lax.dot_general(
        scaled.reshape(n_o * pod, k), everything, (((0,), (0,)), ((), ())),
        preferred_element_type=jnp.float32,
    )
    coef = None
    for a in range(n_o):
        term = weight_sum[a] / (weight_sum[a] + 1.0)
        coef = term if coef is None else coef + term
    return (pull - coef[:, None] * centroids) / n_o


def solution(mesh):
    n_o, n_d, n_c = mesh.shape["outer"], mesh.shape["dp"], mesh.shape["cent"]

    def shards(rows, centroids):
        t, d = rows.shape
        k = centroids.shape[0]
        n_all = t * n_o * n_d
        footprint = n_all * d * 2 + n_all * k * 4 * 2
        if footprint <= (24 << 20) and t % n_c == 0 and (n_c & (n_c - 1)) == 0:
            return shards_all(rows, centroids)
        return shards_pod(rows, centroids)

    return jax.shard_map(
        shards,
        mesh=mesh,
        in_specs=(P(("outer", "dp"), None), P(("dp", "cent"), None)),
        out_specs=P(("dp", "cent"), None),
        check_vma=False,
    )
```

```python
import itertools

import jax
import jax.numpy as jnp
from jax import lax
from jax.sharding import PartitionSpec as P


def scores_for(piece, cent_bf, squares):
    product = lax.dot_general(
        piece, cent_bf, (((1,), (1,)), ((), ())), preferred_element_type=jnp.float32
    )
    return 0.5 * (2.0 * product - squares[None, :])


def row_summary(logits):
    local_max = jnp.max(logits, axis=1)
    local_sum = jnp.sum(jnp.exp(logits - local_max[:, None]), axis=1)
    return (local_max, local_sum)


def global_stats(local_max, local_sum):
    row_peak = lax.pmax(local_max, ("dp", "cent"))
    row_mass = lax.psum(local_sum * jnp.exp(local_max - row_peak), ("dp", "cent"))
    return (row_peak, row_mass)


def shards_pod(rows, centroids):
    rows_bf = rows.astype(jnp.bfloat16)
    cent_bf = centroids.astype(jnp.bfloat16)
    squares = jnp.sum(centroids * centroids, axis=1)
    gathered = lax.all_gather(rows_bf, "dp", axis=0, tiled=True)
    logits = scores_for(gathered, cent_bf, squares)
    local_max, local_sum = row_summary(logits)
    row_peak, row_mass = global_stats(local_max, local_sum)
    weights = (jnp.exp(logits - row_peak[:, None]) / row_mass[:, None]).astype(jnp.bfloat16)
    weight_sum = jnp.sum(weights.astype(jnp.float32), axis=0)
    pull = lax.dot_general(
        weights, gathered, (((0,), (0,)), ((), ())), preferred_element_type=jnp.float32
    )
    delta = (pull - weight_sum[:, None] * centroids) / (weight_sum[:, None] + 1.0)
    return lax.psum(delta, "outer") / lax.axis_size("outer")


def shards_all(rows, centroids):
    n_o = lax.axis_size("outer")
    n_d = lax.axis_size("dp")
    n_c = lax.axis_size("cent")
    z = lax.axis_index("outer")
    y = lax.axis_index("dp")
    q = lax.axis_index("cent")
    t, d = rows.shape
    tq = t // n_c
    n_od = n_o * n_d

    rows_bf = rows.astype(jnp.bfloat16)
    cent_bf = centroids.astype(jnp.bfloat16)
    squares = jnp.sum(centroids * centroids, axis=1)

    bits = []
    b = 1
    while b < n_c:
        bits.append(b)
        b *= 2
    xs = [0]
    for bit in reversed(bits):
        xs = xs + [x ^ bit for x in xs]

    mine = lax.dynamic_slice_in_dim(rows_bf, q * tq, tq, 0)
    shifts = list(itertools.product(range(n_o), range(n_d)))
    def pair_of(piece):
        across = [piece]
        for sy in range(1, n_d):
            across.append(lax.ppermute(piece, "dp", [(j, (j + sy) % n_d) for j in range(n_d)]))
        return jnp.stack(across)

    def spread(cur):
        for bit in reversed(bits):
            other = lax.ppermute(cur, "cent", [(i, i ^ bit) for i in range(n_c)])
            cur = jnp.concatenate([cur, other], axis=1)
        return cur

    landed = [mine]
    for sz in range(1, n_o):
        landed.append(lax.ppermute(mine, "outer", [(i, (i + sz) % n_o) for i in range(n_o)]))

    k = centroids.shape[0]
    pod = n_d * n_c * tq
    everything = jnp.zeros((n_o * pod, d), rows_bf.dtype)
    logits = jnp.zeros((n_o * pod, k), jnp.float32)
    local_max = jnp.zeros((n_o * pod,), jnp.float32)
    local_sum = jnp.zeros((n_o * pod,), jnp.float32)

    def store(done, bufs):
        part, lg, mx, sm, sz = done
        at = ((z - sz) % n_o) * pod
        e_b, l_b, m_b, s_b = bufs
        e_b = lax.dynamic_update_slice_in_dim(e_b, part, at, 0)
        l_b = lax.dynamic_update_slice_in_dim(l_b, lg, at, 0)
        m_b = lax.dynamic_update_slice_in_dim(m_b, mx, at, 0)
        s_b = lax.dynamic_update_slice_in_dim(s_b, sm, at, 0)
        return (e_b, l_b, m_b, s_b)

    bufs = (everything, logits, local_max, local_sum)
    prev = None
    for sz in range(n_o):
        cur = pair_of(landed[sz])
        for bi, bit in enumerate(reversed(bits)):
            if bi == len(bits) - 1 and prev is not None:
                prev_arrays, cur = lax.optimization_barrier((prev[:4], cur))
                prev = prev_arrays + (prev[4],)
            other = lax.ppermute(cur, "cent", [(i, i ^ bit) for i in range(n_c)])
            cur = jnp.concatenate([cur, other], axis=1)
        if prev is not None:
            bufs = store(prev, bufs)
        part = cur.reshape(pod, d)
        lg = scores_for(part, cent_bf, squares)
        mx, sm = row_summary(lg)
        prev = (part, lg, mx, sm, sz)
    everything, logits, local_max, local_sum = store(prev, bufs)

    src_vec = jnp.stack([a * n_d + (y - sy) % n_d for a, sy in shifts])
    hot_k = src_vec[None, :] == jnp.arange(n_od)[:, None]
    c_vec = jnp.stack([q ^ x for x in xs])
    hot_c = c_vec[None, :] == jnp.arange(n_c)[:, None]

    def to_absolute(v):
        v = v.reshape(n_od, n_c, tq)
        v = jnp.sum(jnp.where(hot_c[None, :, :, None], v[:, None, :, :], 0.0), axis=2)
        return jnp.sum(jnp.where(hot_k[:, :, None, None], v[None], 0.0), axis=1)

    def to_local(v):
        v = jnp.sum(jnp.where(hot_k[:, :, None, None], v[:, None], 0.0), axis=0)
        v = jnp.sum(jnp.where(hot_c[:, :, None], v[:, :, None, :], 0.0), axis=1)
        return v.reshape(n_od * n_c * tq)

    both = jnp.stack([to_absolute(local_max), to_absolute(local_sum)])
    every = lax.all_gather(both, ("dp", "cent"), axis=0)
    maxes, sums = every[:, 0], every[:, 1]
    peak_abs = jnp.max(maxes, axis=0)
    mass_abs = jnp.sum(sums * jnp.exp(maxes - peak_abs[None]), axis=0)
    row_peak = to_local(peak_abs)
    row_mass = to_local(mass_abs)

    weights = (jnp.exp(logits - row_peak[:, None]) / row_mass[:, None]).astype(jnp.bfloat16)
    w_pods = weights.reshape(n_o, pod, k).astype(jnp.float32)
    weight_sum = jnp.sum(w_pods, axis=1)
    scaled = (w_pods / (weight_sum[:, None, :] + 1.0)).astype(jnp.bfloat16)
    pull = lax.dot_general(
        scaled.reshape(n_o * pod, k), everything, (((0,), (0,)), ((), ())),
        preferred_element_type=jnp.float32,
    )
    coef = None
    for a in range(n_o):
        term = weight_sum[a] / (weight_sum[a] + 1.0)
        coef = term if coef is None else coef + term
    return (pull - coef[:, None] * centroids) / n_o


def solution(mesh):
    n_o, n_d, n_c = mesh.shape["outer"], mesh.shape["dp"], mesh.shape["cent"]

    def shards(rows, centroids):
        t, d = rows.shape
        k = centroids.shape[0]
        n_all = t * n_o * n_d
        footprint = n_all * d * 2 + n_all * k * 4 * 2
        if footprint <= (24 << 20) and t % n_c == 0 and (n_c & (n_c - 1)) == 0:
            return shards_all(rows, centroids)
        return shards_pod(rows, centroids)

    return jax.shard_map(
        shards,
        mesh=mesh,
        in_specs=(P(("outer", "dp"), None), P(("dp", "cent"), None)),
        out_specs=P(("dp", "cent"), None),
        check_vma=False,
    )
```

```python
import itertools

import jax
import jax.numpy as jnp
from jax import lax
from jax.sharding import PartitionSpec as P


def scores_for(piece, cent_bf, squares):
    product = lax.dot_general(
        piece, cent_bf, (((1,), (1,)), ((), ())), preferred_element_type=jnp.float32
    )
    return 0.5 * (2.0 * product - squares[None, :])


def row_summary(logits):
    local_max = jnp.max(logits, axis=1)
    local_sum = jnp.sum(jnp.exp(logits - local_max[:, None]), axis=1)
    return (local_max, local_sum)


def global_stats(local_max, local_sum):
    row_peak = lax.pmax(local_max, ("dp", "cent"))
    row_mass = lax.psum(local_sum * jnp.exp(local_max - row_peak), ("dp", "cent"))
    return (row_peak, row_mass)


def shards_pod(rows, centroids):
    rows_bf = rows.astype(jnp.bfloat16)
    cent_bf = centroids.astype(jnp.bfloat16)
    squares = jnp.sum(centroids * centroids, axis=1)
    gathered = lax.all_gather(rows_bf, "dp", axis=0, tiled=True)
    logits = scores_for(gathered, cent_bf, squares)
    local_max, local_sum = row_summary(logits)
    row_peak, row_mass = global_stats(local_max, local_sum)
    weights = (jnp.exp(logits - row_peak[:, None]) / row_mass[:, None]).astype(jnp.bfloat16)
    weight_sum = jnp.sum(weights.astype(jnp.float32), axis=0)
    pull = lax.dot_general(
        weights, gathered, (((0,), (0,)), ((), ())), preferred_element_type=jnp.float32
    )
    delta = (pull - weight_sum[:, None] * centroids) / (weight_sum[:, None] + 1.0)
    return lax.psum(delta, "outer") / lax.axis_size("outer")


def shards_all(rows, centroids):
    n_o = lax.axis_size("outer")
    n_d = lax.axis_size("dp")
    n_c = lax.axis_size("cent")
    z = lax.axis_index("outer")
    y = lax.axis_index("dp")
    q = lax.axis_index("cent")
    t, d = rows.shape
    tq = t // n_c
    n_od = n_o * n_d

    rows_bf = rows.astype(jnp.bfloat16)
    cent_bf = centroids.astype(jnp.bfloat16)
    squares = jnp.sum(centroids * centroids, axis=1)

    bits = []
    b = 1
    while b < n_c:
        bits.append(b)
        b *= 2
    xs = [0]
    for bit in reversed(bits):
        xs = xs + [x ^ bit for x in xs]

    mine = lax.dynamic_slice_in_dim(rows_bf, q * tq, tq, 0)
    shifts = list(itertools.product(range(n_o), range(n_d)))
    def pair_of(piece):
        across = [piece]
        for sy in range(1, n_d):
            across.append(lax.ppermute(piece, "dp", [(j, (j + sy) % n_d) for j in range(n_d)]))
        return jnp.stack(across)

    def spread(cur):
        for bit in reversed(bits):
            other = lax.ppermute(cur, "cent", [(i, i ^ bit) for i in range(n_c)])
            cur = jnp.concatenate([cur, other], axis=1)
        return cur

    landed = [mine]
    for sz in range(1, n_o):
        landed.append(lax.ppermute(mine, "outer", [(i, (i + sz) % n_o) for i in range(n_o)]))
    parts = [None] + [spread(pair_of(piece)) for piece in landed[1:]]

    h = q % 2
    half = t // 2
    my_half = lax.dynamic_slice_in_dim(rows_bf, h * half, half, 0)
    own_blocks = [rows_bf]
    for sy in range(1, n_d):
        got = lax.ppermute(my_half, "dp", [(j, (j + sy) % n_d) for j in range(n_d)])
        mate = lax.ppermute(got, "cent", [(i, i ^ 1) for i in range(n_c)])
        own_blocks.append(jnp.concatenate([got, mate], axis=0))
    parts[0] = jnp.stack(own_blocks)

    cur = jnp.zeros((n_o * n_d,) + parts[0].shape[1:], parts[0].dtype)
    for sz in range(n_o):
        cur = lax.dynamic_update_slice_in_dim(cur, parts[sz], ((z - sz) % n_o) * n_d, axis=0)
    everything = cur.reshape(n_od * n_c * tq, d)

    logits = scores_for(everything, cent_bf, squares)
    local_max, local_sum = row_summary(logits)

    src_vec = jnp.stack([a * n_d + (y - sy) % n_d for a, sy in shifts])
    hot_k = src_vec[None, :] == jnp.arange(n_od)[:, None]
    jj = jnp.arange(n_c)
    xor_map = q ^ jnp.asarray(xs, jnp.int32)
    hq = n_c // 2
    half_map = ((jj // hq) ^ h) * hq + jj % hq
    maps = []
    for a, sy in shifts:
        own_map = jj if sy == 0 else half_map
        maps.append(jnp.where(a == z, own_map, xor_map))
    c_map = jnp.stack(maps)
    hot_kc = c_map[:, None, :] == jj[None, :, None]

    def to_absolute(v):
        v = v.reshape(n_od, n_c, tq)
        v = jnp.sum(jnp.where(hot_kc[:, :, :, None], v[:, None, :, :], 0.0), axis=2)
        return jnp.sum(jnp.where(hot_k[:, :, None, None], v[None], 0.0), axis=1)

    def to_local(v):
        v = jnp.sum(jnp.where(hot_k[:, :, None, None], v[:, None], 0.0), axis=0)
        v = jnp.sum(jnp.where(hot_kc[:, :, :, None], v[:, :, None, :], 0.0), axis=1)
        return v.reshape(n_od * n_c * tq)

    both = jnp.stack([to_absolute(local_max), to_absolute(local_sum)])
    every = lax.all_gather(both, ("dp", "cent"), axis=0)
    maxes, sums = every[:, 0], every[:, 1]
    peak_abs = jnp.max(maxes, axis=0)
    mass_abs = jnp.sum(sums * jnp.exp(maxes - peak_abs[None]), axis=0)
    row_peak = to_local(peak_abs)
    row_mass = to_local(mass_abs)

    weights = (jnp.exp(logits - row_peak[:, None]) / row_mass[:, None]).astype(jnp.bfloat16)
    k = centroids.shape[0]
    pod = n_d * n_c * tq
    w_pods = weights.reshape(n_o, pod, k).astype(jnp.float32)
    weight_sum = jnp.sum(w_pods, axis=1)
    scaled = (w_pods / (weight_sum[:, None, :] + 1.0)).astype(jnp.bfloat16)
    pull = lax.dot_general(
        scaled.reshape(n_o * pod, k), everything, (((0,), (0,)), ((), ())),
        preferred_element_type=jnp.float32,
    )
    coef = None
    for a in range(n_o):
        term = weight_sum[a] / (weight_sum[a] + 1.0)
        coef = term if coef is None else coef + term
    return (pull - coef[:, None] * centroids) / n_o


def solution(mesh):
    n_o, n_d, n_c = mesh.shape["outer"], mesh.shape["dp"], mesh.shape["cent"]

    def shards(rows, centroids):
        t, d = rows.shape
        k = centroids.shape[0]
        n_all = t * n_o * n_d
        footprint = n_all * d * 2 + n_all * k * 4 * 2
        if footprint <= (24 << 20) and t % n_c == 0 and n_c >= 2 and (n_c & (n_c - 1)) == 0:
            return shards_all(rows, centroids)
        return shards_pod(rows, centroids)

    return jax.shard_map(
        shards,
        mesh=mesh,
        in_specs=(P(("outer", "dp"), None), P(("dp", "cent"), None)),
        out_specs=P(("dp", "cent"), None),
        check_vma=False,
    )
```

```python
import itertools

import jax
import jax.numpy as jnp
from jax import lax
from jax.sharding import PartitionSpec as P


def scores_for(piece, cent_bf, squares):
    product = lax.dot_general(
        piece, cent_bf, (((1,), (1,)), ((), ())), preferred_element_type=jnp.float32
    )
    return 0.5 * (2.0 * product - squares[None, :])


def row_summary(logits):
    local_max = jnp.max(logits, axis=1)
    local_sum = jnp.sum(jnp.exp(logits - local_max[:, None]), axis=1)
    return (local_max, local_sum)


def global_stats(local_max, local_sum):
    row_peak = lax.pmax(local_max, ("dp", "cent"))
    row_mass = lax.psum(local_sum * jnp.exp(local_max - row_peak), ("dp", "cent"))
    return (row_peak, row_mass)


def shards_pod(rows, centroids):
    rows_bf = rows.astype(jnp.bfloat16)
    cent_bf = centroids.astype(jnp.bfloat16)
    squares = jnp.sum(centroids * centroids, axis=1)
    gathered = lax.all_gather(rows_bf, "dp", axis=0, tiled=True)
    logits = scores_for(gathered, cent_bf, squares)
    local_max, local_sum = row_summary(logits)
    row_peak, row_mass = global_stats(local_max, local_sum)
    weights = (jnp.exp(logits - row_peak[:, None]) / row_mass[:, None]).astype(jnp.bfloat16)
    weight_sum = jnp.sum(weights.astype(jnp.float32), axis=0)
    pull = lax.dot_general(
        weights, gathered, (((0,), (0,)), ((), ())), preferred_element_type=jnp.float32
    )
    delta = (pull - weight_sum[:, None] * centroids) / (weight_sum[:, None] + 1.0)
    return lax.psum(delta, "outer") / lax.axis_size("outer")


def shards_all(rows, centroids):
    n_o = lax.axis_size("outer")
    n_d = lax.axis_size("dp")
    n_c = lax.axis_size("cent")
    z = lax.axis_index("outer")
    y = lax.axis_index("dp")
    q = lax.axis_index("cent")
    t, d = rows.shape
    tq = t // n_c
    n_od = n_o * n_d

    rows_bf = rows.astype(jnp.bfloat16)
    cent_bf = centroids.astype(jnp.bfloat16)
    squares = jnp.sum(centroids * centroids, axis=1)

    bits = []
    b = 1
    while b < n_c:
        bits.append(b)
        b *= 2
    xs = [0]
    for bit in reversed(bits):
        xs = xs + [x ^ bit for x in xs]

    mine = lax.dynamic_slice_in_dim(rows, q * tq, tq, 0).astype(jnp.bfloat16)
    shifts = list(itertools.product(range(n_o), range(n_d)))
    def pair_of(piece):
        across = [piece]
        for sy in range(1, n_d):
            across.append(lax.ppermute(piece, "dp", [(j, (j + sy) % n_d) for j in range(n_d)]))
        return jnp.stack(across)

    def spread(cur):
        for bit in reversed(bits):
            other = lax.ppermute(cur, "cent", [(i, i ^ bit) for i in range(n_c)])
            cur = jnp.concatenate([cur, other], axis=1)
        return cur

    landed = [mine]
    for sz in range(1, n_o):
        landed.append(lax.ppermute(mine, "outer", [(i, (i + sz) % n_o) for i in range(n_o)]))
    parts = [None] + [spread(pair_of(piece)) for piece in landed[1:]]

    h = q % 2
    half = t // 2
    my_half = lax.dynamic_slice_in_dim(rows, h * half, half, 0).astype(jnp.bfloat16)
    own_blocks = [rows_bf]
    for sy in range(1, n_d):
        got = lax.ppermute(my_half, "dp", [(j, (j + sy) % n_d) for j in range(n_d)])
        mate = lax.ppermute(got, "cent", [(i, i ^ 1) for i in range(n_c)])
        own_blocks.append(jnp.concatenate([got, mate], axis=0))
    parts[0] = jnp.stack(own_blocks)

    cur = jnp.zeros((n_o * n_d,) + parts[0].shape[1:], parts[0].dtype)
    for sz in range(n_o):
        cur = lax.dynamic_update_slice_in_dim(cur, parts[sz], ((z - sz) % n_o) * n_d, axis=0)
    everything = cur.reshape(n_od * n_c * tq, d)

    logits = scores_for(everything, cent_bf, squares)
    local_max, local_sum = row_summary(logits)

    src_vec = jnp.stack([a * n_d + (y - sy) % n_d for a, sy in shifts])
    hot_k = src_vec[None, :] == jnp.arange(n_od)[:, None]
    jj = jnp.arange(n_c)
    xor_map = q ^ jnp.asarray(xs, jnp.int32)
    hq = n_c // 2
    half_map = ((jj // hq) ^ h) * hq + jj % hq
    maps = []
    for a, sy in shifts:
        own_map = jj if sy == 0 else half_map
        maps.append(jnp.where(a == z, own_map, xor_map))
    c_map = jnp.stack(maps)
    hot_kc = c_map[:, None, :] == jj[None, :, None]

    def to_absolute(v):
        v = v.reshape(n_od, n_c, tq)
        v = jnp.sum(jnp.where(hot_kc[:, :, :, None], v[:, None, :, :], 0.0), axis=2)
        return jnp.sum(jnp.where(hot_k[:, :, None, None], v[None], 0.0), axis=1)

    def to_local(v):
        v = jnp.sum(jnp.where(hot_k[:, :, None, None], v[:, None], 0.0), axis=0)
        v = jnp.sum(jnp.where(hot_kc[:, :, :, None], v[:, :, None, :], 0.0), axis=1)
        return v.reshape(n_od * n_c * tq)

    both = jnp.stack([to_absolute(local_max), to_absolute(local_sum)])
    every = lax.all_gather(both, ("dp", "cent"), axis=0)
    maxes, sums = every[:, 0], every[:, 1]
    peak_abs = jnp.max(maxes, axis=0)
    mass_abs = jnp.sum(sums * jnp.exp(maxes - peak_abs[None]), axis=0)
    row_peak = to_local(peak_abs)
    row_mass = to_local(mass_abs)

    weights = (jnp.exp(logits - row_peak[:, None]) / row_mass[:, None]).astype(jnp.bfloat16)
    k = centroids.shape[0]
    pod = n_d * n_c * tq
    w_pods = weights.reshape(n_o, pod, k).astype(jnp.float32)
    weight_sum = jnp.sum(w_pods, axis=1)
    scaled = (w_pods / (weight_sum[:, None, :] + 1.0)).astype(jnp.bfloat16)
    pull = lax.dot_general(
        scaled.reshape(n_o * pod, k), everything, (((0,), (0,)), ((), ())),
        preferred_element_type=jnp.float32,
    )
    coef = None
    for a in range(n_o):
        term = weight_sum[a] / (weight_sum[a] + 1.0)
        coef = term if coef is None else coef + term
    return (pull - coef[:, None] * centroids) / n_o


def solution(mesh):
    n_o, n_d, n_c = mesh.shape["outer"], mesh.shape["dp"], mesh.shape["cent"]

    def shards(rows, centroids):
        t, d = rows.shape
        k = centroids.shape[0]
        n_all = t * n_o * n_d
        footprint = n_all * d * 2 + n_all * k * 4 * 2
        if footprint <= (24 << 20) and t % n_c == 0 and n_c >= 2 and (n_c & (n_c - 1)) == 0:
            return shards_all(rows, centroids)
        return shards_pod(rows, centroids)

    return jax.shard_map(
        shards,
        mesh=mesh,
        in_specs=(P(("outer", "dp"), None), P(("dp", "cent"), None)),
        out_specs=P(("dp", "cent"), None),
        check_vma=False,
    )
```

```python
import itertools

import jax
import jax.numpy as jnp
from jax import lax
from jax.experimental import pallas as pl
from jax.sharding import PartitionSpec as P


def scores_for(piece, cent_bf, squares):
    product = lax.dot_general(
        piece, cent_bf, (((1,), (1,)), ((), ())), preferred_element_type=jnp.float32
    )
    return 0.5 * (2.0 * product - squares[None, :])


def row_summary(logits):
    local_max = jnp.max(logits, axis=1)
    local_sum = jnp.sum(jnp.exp(logits - local_max[:, None]), axis=1)
    return (local_max, local_sum)


def _logit_kernel(r_ref, c_ref, sq_ref, l_ref, m_ref, s_ref):
    prod = lax.dot_general(
        r_ref[...], c_ref[...], (((1,), (1,)), ((), ())), preferred_element_type=jnp.float32
    )
    lg = 0.5 * (2.0 * prod - sq_ref[...])
    l_ref[...] = lg
    mx = jnp.max(lg, axis=1, keepdims=True)
    m_ref[...] = mx
    s_ref[...] = jnp.sum(jnp.exp(lg - mx), axis=1, keepdims=True)


def logits_and_stats(rows_bf, cent_bf, squares):
    n, d = rows_bf.shape
    k = cent_bf.shape[0]
    bm = 256 if n % 256 == 0 else n
    lg, mx, sm = pl.pallas_call(
        _logit_kernel,
        grid=(n // bm,),
        in_specs=[
            pl.BlockSpec((bm, d), lambda i: (i, 0)),
            pl.BlockSpec((k, d), lambda i: (0, 0)),
            pl.BlockSpec((1, k), lambda i: (0, 0)),
        ],
        out_specs=[
            pl.BlockSpec((bm, k), lambda i: (i, 0)),
            pl.BlockSpec((bm, 1), lambda i: (i, 0)),
            pl.BlockSpec((bm, 1), lambda i: (i, 0)),
        ],
        out_shape=[
            jax.ShapeDtypeStruct((n, k), jnp.float32),
            jax.ShapeDtypeStruct((n, 1), jnp.float32),
            jax.ShapeDtypeStruct((n, 1), jnp.float32),
        ],
    )(rows_bf, cent_bf, squares[None, :])
    return lg, mx[:, 0], sm[:, 0]


def global_stats(local_max, local_sum):
    row_peak = lax.pmax(local_max, ("dp", "cent"))
    row_mass = lax.psum(local_sum * jnp.exp(local_max - row_peak), ("dp", "cent"))
    return (row_peak, row_mass)


def shards_pod(rows, centroids):
    rows_bf = rows.astype(jnp.bfloat16)
    cent_bf = centroids.astype(jnp.bfloat16)
    squares = jnp.sum(centroids * centroids, axis=1)
    gathered = lax.all_gather(rows_bf, "dp", axis=0, tiled=True)
    logits = scores_for(gathered, cent_bf, squares)
    local_max, local_sum = row_summary(logits)
    row_peak, row_mass = global_stats(local_max, local_sum)
    weights = (jnp.exp(logits - row_peak[:, None]) / row_mass[:, None]).astype(jnp.bfloat16)
    weight_sum = jnp.sum(weights.astype(jnp.float32), axis=0)
    pull = lax.dot_general(
        weights, gathered, (((0,), (0,)), ((), ())), preferred_element_type=jnp.float32
    )
    delta = (pull - weight_sum[:, None] * centroids) / (weight_sum[:, None] + 1.0)
    return lax.psum(delta, "outer") / lax.axis_size("outer")


def shards_all(rows, centroids):
    n_o = lax.axis_size("outer")
    n_d = lax.axis_size("dp")
    n_c = lax.axis_size("cent")
    z = lax.axis_index("outer")
    y = lax.axis_index("dp")
    q = lax.axis_index("cent")
    t, d = rows.shape
    tq = t // n_c
    n_od = n_o * n_d

    rows_bf = rows.astype(jnp.bfloat16)
    cent_bf = centroids.astype(jnp.bfloat16)
    squares = jnp.sum(centroids * centroids, axis=1)

    bits = []
    b = 1
    while b < n_c:
        bits.append(b)
        b *= 2
    xs = [0]
    for bit in reversed(bits):
        xs = xs + [x ^ bit for x in xs]

    mine = lax.dynamic_slice_in_dim(rows, q * tq, tq, 0).astype(jnp.bfloat16)
    shifts = list(itertools.product(range(n_o), range(n_d)))
    def pair_of(piece):
        across = [piece]
        for sy in range(1, n_d):
            across.append(lax.ppermute(piece, "dp", [(j, (j + sy) % n_d) for j in range(n_d)]))
        return jnp.stack(across)

    def spread(cur):
        for bit in reversed(bits):
            other = lax.ppermute(cur, "cent", [(i, i ^ bit) for i in range(n_c)])
            cur = jnp.concatenate([cur, other], axis=1)
        return cur

    landed = [mine]
    for sz in range(1, n_o):
        landed.append(lax.ppermute(mine, "outer", [(i, (i + sz) % n_o) for i in range(n_o)]))
    parts = [None] + [spread(pair_of(piece)) for piece in landed[1:]]

    h = q % 2
    half = t // 2
    my_half = lax.dynamic_slice_in_dim(rows, h * half, half, 0).astype(jnp.bfloat16)
    own_blocks = [rows_bf]
    for sy in range(1, n_d):
        got = lax.ppermute(my_half, "dp", [(j, (j + sy) % n_d) for j in range(n_d)])
        mate = lax.ppermute(got, "cent", [(i, i ^ 1) for i in range(n_c)])
        own_blocks.append(jnp.concatenate([got, mate], axis=0))
    parts[0] = jnp.stack(own_blocks)

    cur = jnp.zeros((n_o * n_d,) + parts[0].shape[1:], parts[0].dtype)
    for sz in range(n_o):
        cur = lax.dynamic_update_slice_in_dim(cur, parts[sz], ((z - sz) % n_o) * n_d, axis=0)
    everything = cur.reshape(n_od * n_c * tq, d)

    logits, local_max, local_sum = logits_and_stats(everything, cent_bf, squares)

    src_vec = jnp.stack([a * n_d + (y - sy) % n_d for a, sy in shifts])
    hot_k = src_vec[None, :] == jnp.arange(n_od)[:, None]
    jj = jnp.arange(n_c)
    xor_map = q ^ jnp.asarray(xs, jnp.int32)
    hq = n_c // 2
    half_map = ((jj // hq) ^ h) * hq + jj % hq
    maps = []
    for a, sy in shifts:
        own_map = jj if sy == 0 else half_map
        maps.append(jnp.where(a == z, own_map, xor_map))
    c_map = jnp.stack(maps)
    hot_kc = c_map[:, None, :] == jj[None, :, None]

    def to_absolute(v):
        v = v.reshape(n_od, n_c, tq)
        v = jnp.sum(jnp.where(hot_kc[:, :, :, None], v[:, None, :, :], 0.0), axis=2)
        return jnp.sum(jnp.where(hot_k[:, :, None, None], v[None], 0.0), axis=1)

    def to_local(v):
        v = jnp.sum(jnp.where(hot_k[:, :, None, None], v[:, None], 0.0), axis=0)
        v = jnp.sum(jnp.where(hot_kc[:, :, :, None], v[:, :, None, :], 0.0), axis=1)
        return v.reshape(n_od * n_c * tq)

    both = jnp.stack([to_absolute(local_max), to_absolute(local_sum)])
    every = lax.all_gather(both, ("dp", "cent"), axis=0)
    maxes, sums = every[:, 0], every[:, 1]
    peak_abs = jnp.max(maxes, axis=0)
    mass_abs = jnp.sum(sums * jnp.exp(maxes - peak_abs[None]), axis=0)
    row_peak = to_local(peak_abs)
    row_mass = to_local(mass_abs)

    weights = (jnp.exp(logits - row_peak[:, None]) / row_mass[:, None]).astype(jnp.bfloat16)
    k = centroids.shape[0]
    pod = n_d * n_c * tq
    w_pods = weights.reshape(n_o, pod, k).astype(jnp.float32)
    weight_sum = jnp.sum(w_pods, axis=1)
    scaled = (w_pods / (weight_sum[:, None, :] + 1.0)).astype(jnp.bfloat16)
    pull = lax.dot_general(
        scaled.reshape(n_o * pod, k), everything, (((0,), (0,)), ((), ())),
        preferred_element_type=jnp.float32,
    )
    coef = None
    for a in range(n_o):
        term = weight_sum[a] / (weight_sum[a] + 1.0)
        coef = term if coef is None else coef + term
    return (pull - coef[:, None] * centroids) / n_o


def solution(mesh):
    n_o, n_d, n_c = mesh.shape["outer"], mesh.shape["dp"], mesh.shape["cent"]

    def shards(rows, centroids):
        t, d = rows.shape
        k = centroids.shape[0]
        n_all = t * n_o * n_d
        footprint = n_all * d * 2 + n_all * k * 4 * 2
        if footprint <= (24 << 20) and t % n_c == 0 and n_c >= 2 and (n_c & (n_c - 1)) == 0:
            return shards_all(rows, centroids)
        return shards_pod(rows, centroids)

    return jax.shard_map(
        shards,
        mesh=mesh,
        in_specs=(P(("outer", "dp"), None), P(("dp", "cent"), None)),
        out_specs=P(("dp", "cent"), None),
        check_vma=False,
    )
```

```python
import itertools

import jax
import jax.numpy as jnp
from jax import lax
from jax.sharding import PartitionSpec as P


def scores_for(piece, cent_bf, squares):
    product = lax.dot_general(
        piece, cent_bf, (((1,), (1,)), ((), ())), preferred_element_type=jnp.float32
    )
    return 0.5 * (2.0 * product - squares[None, :])


def row_summary(logits):
    local_max = jnp.max(logits, axis=1)
    local_sum = jnp.sum(jnp.exp(logits - local_max[:, None]), axis=1)
    return (local_max, local_sum)


def global_stats(local_max, local_sum):
    row_peak = lax.pmax(local_max, ("dp", "cent"))
    row_mass = lax.psum(local_sum * jnp.exp(local_max - row_peak), ("dp", "cent"))
    return (row_peak, row_mass)


def shards_pod(rows, centroids):
    rows_bf = rows.astype(jnp.bfloat16)
    cent_bf = centroids.astype(jnp.bfloat16)
    squares = jnp.sum(centroids * centroids, axis=1)
    gathered = lax.all_gather(rows_bf, "dp", axis=0, tiled=True)
    logits = scores_for(gathered, cent_bf, squares)
    local_max, local_sum = row_summary(logits)
    row_peak, row_mass = global_stats(local_max, local_sum)
    weights = (jnp.exp(logits - row_peak[:, None]) / row_mass[:, None]).astype(jnp.bfloat16)
    weight_sum = jnp.sum(weights.astype(jnp.float32), axis=0)
    pull = lax.dot_general(
        weights, gathered, (((0,), (0,)), ((), ())), preferred_element_type=jnp.float32
    )
    delta = (pull - weight_sum[:, None] * centroids) / (weight_sum[:, None] + 1.0)
    return lax.psum(delta, "outer") / lax.axis_size("outer")


def shards_all(rows, centroids):
    n_o = lax.axis_size("outer")
    n_d = lax.axis_size("dp")
    n_c = lax.axis_size("cent")
    z = lax.axis_index("outer")
    y = lax.axis_index("dp")
    q = lax.axis_index("cent")
    t, d = rows.shape
    tq = t // n_c
    n_od = n_o * n_d

    rows_bf = rows.astype(jnp.bfloat16)
    cent_bf = centroids.astype(jnp.bfloat16)
    squares = jnp.sum(centroids * centroids, axis=1)

    bits = []
    b = 1
    while b < n_c:
        bits.append(b)
        b *= 2
    xs = [0]
    for bit in reversed(bits):
        xs = xs + [x ^ bit for x in xs]

    mine = lax.dynamic_slice_in_dim(rows_bf, q * tq, tq, 0)
    shifts = list(itertools.product(range(n_o), range(n_d)))
    def pair_of(piece):
        across = [piece]
        for sy in range(1, n_d):
            across.append(lax.ppermute(piece, "dp", [(j, (j + sy) % n_d) for j in range(n_d)]))
        return jnp.stack(across)

    def spread(cur):
        for bit in reversed(bits):
            other = lax.ppermute(cur, "cent", [(i, i ^ bit) for i in range(n_c)])
            cur = jnp.concatenate([cur, other], axis=1)
        return cur

    landed = [mine]
    for sz in range(1, n_o):
        if n_o & (n_o - 1) == 0:
            pairs = [(i, i ^ sz) for i in range(n_o)]
        else:
            pairs = [(i, (i + sz) % n_o) for i in range(n_o)]
        landed.append(lax.ppermute(mine, "outer", pairs))
    parts = [None] + [spread(pair_of(piece)) for piece in landed[1:]]

    h = q % 2
    half = t // 2
    my_half = lax.dynamic_slice_in_dim(rows_bf, h * half, half, 0)
    own_blocks = [rows_bf]
    for sy in range(1, n_d):
        got = lax.ppermute(my_half, "dp", [(j, (j + sy) % n_d) for j in range(n_d)])
        mate = lax.ppermute(got, "cent", [(i, i ^ 1) for i in range(n_c)])
        own_blocks.append(jnp.concatenate([got, mate], axis=0))
    parts[0] = jnp.stack(own_blocks)

    cur = jnp.zeros((n_o * n_d,) + parts[0].shape[1:], parts[0].dtype)
    for sz in range(n_o):
        pod_of = (z ^ sz) if n_o & (n_o - 1) == 0 else (z - sz) % n_o
        cur = lax.dynamic_update_slice_in_dim(cur, parts[sz], pod_of * n_d, axis=0)
    everything = cur.reshape(n_od * n_c * tq, d)

    logits = scores_for(everything, cent_bf, squares)
    local_max, local_sum = row_summary(logits)

    src_vec = jnp.stack([a * n_d + (y - sy) % n_d for a, sy in shifts])
    hot_k = src_vec[None, :] == jnp.arange(n_od)[:, None]
    jj = jnp.arange(n_c)
    xor_map = q ^ jnp.asarray(xs, jnp.int32)
    hq = n_c // 2
    half_map = ((jj // hq) ^ h) * hq + jj % hq
    maps = []
    for a, sy in shifts:
        own_map = jj if sy == 0 else half_map
        maps.append(jnp.where(a == z, own_map, xor_map))
    c_map = jnp.stack(maps)
    hot_kc = c_map[:, None, :] == jj[None, :, None]

    def to_absolute(v):
        v = v.reshape(n_od, n_c, tq)
        v = jnp.sum(jnp.where(hot_kc[:, :, :, None], v[:, None, :, :], 0.0), axis=2)
        return jnp.sum(jnp.where(hot_k[:, :, None, None], v[None], 0.0), axis=1)

    def to_local(v):
        v = jnp.sum(jnp.where(hot_k[:, :, None, None], v[:, None], 0.0), axis=0)
        v = jnp.sum(jnp.where(hot_kc[:, :, :, None], v[:, :, None, :], 0.0), axis=1)
        return v.reshape(n_od * n_c * tq)

    both = jnp.stack([to_absolute(local_max), to_absolute(local_sum)])
    every = lax.all_gather(both, ("dp", "cent"), axis=0)
    maxes, sums = every[:, 0], every[:, 1]
    peak_abs = jnp.max(maxes, axis=0)
    mass_abs = jnp.sum(sums * jnp.exp(maxes - peak_abs[None]), axis=0)
    row_peak = to_local(peak_abs)
    row_mass = to_local(mass_abs)

    weights = (jnp.exp(logits - row_peak[:, None]) / row_mass[:, None]).astype(jnp.bfloat16)
    k = centroids.shape[0]
    pod = n_d * n_c * tq
    w_pods = weights.reshape(n_o, pod, k).astype(jnp.float32)
    weight_sum = jnp.sum(w_pods, axis=1)
    scaled = (w_pods / (weight_sum[:, None, :] + 1.0)).astype(jnp.bfloat16)
    pull = lax.dot_general(
        scaled.reshape(n_o * pod, k), everything, (((0,), (0,)), ((), ())),
        preferred_element_type=jnp.float32,
    )
    coef = None
    for a in range(n_o):
        term = weight_sum[a] / (weight_sum[a] + 1.0)
        coef = term if coef is None else coef + term
    return (pull - coef[:, None] * centroids) / n_o


def solution(mesh):
    n_o, n_d, n_c = mesh.shape["outer"], mesh.shape["dp"], mesh.shape["cent"]

    def shards(rows, centroids):
        t, d = rows.shape
        k = centroids.shape[0]
        n_all = t * n_o * n_d
        footprint = n_all * d * 2 + n_all * k * 4 * 2
        if footprint <= (24 << 20) and t % n_c == 0 and n_c >= 2 and (n_c & (n_c - 1)) == 0:
            return shards_all(rows, centroids)
        return shards_pod(rows, centroids)

    return jax.shard_map(
        shards,
        mesh=mesh,
        in_specs=(P(("outer", "dp"), None), P(("dp", "cent"), None)),
        out_specs=P(("dp", "cent"), None),
        check_vma=False,
    )
```

```python
import itertools

import jax
import jax.numpy as jnp
from jax import lax
from jax.sharding import PartitionSpec as P


def scores_for(piece, cent_bf, squares):
    product = lax.dot_general(
        piece, cent_bf, (((1,), (1,)), ((), ())), preferred_element_type=jnp.float32
    )
    return 0.5 * (2.0 * product - squares[None, :])


def row_summary(logits):
    local_max = jnp.max(logits, axis=1)
    local_sum = jnp.sum(jnp.exp(logits - local_max[:, None]), axis=1)
    return (local_max, local_sum)


def global_stats(local_max, local_sum):
    row_peak = lax.pmax(local_max, ("dp", "cent"))
    row_mass = lax.psum(local_sum * jnp.exp(local_max - row_peak), ("dp", "cent"))
    return (row_peak, row_mass)


def shards_pod(rows, centroids):
    rows_bf = rows.astype(jnp.bfloat16)
    cent_bf = centroids.astype(jnp.bfloat16)
    squares = jnp.sum(centroids * centroids, axis=1)
    gathered = lax.all_gather(rows_bf, "dp", axis=0, tiled=True)
    logits = scores_for(gathered, cent_bf, squares)
    local_max, local_sum = row_summary(logits)
    row_peak, row_mass = global_stats(local_max, local_sum)
    weights = (jnp.exp(logits - row_peak[:, None]) / row_mass[:, None]).astype(jnp.bfloat16)
    weight_sum = jnp.sum(weights.astype(jnp.float32), axis=0)
    pull = lax.dot_general(
        weights, gathered, (((0,), (0,)), ((), ())), preferred_element_type=jnp.float32
    )
    delta = (pull - weight_sum[:, None] * centroids) / (weight_sum[:, None] + 1.0)
    return lax.psum(delta, "outer") / lax.axis_size("outer")


def shards_all(rows, centroids):
    n_o = lax.axis_size("outer")
    n_d = lax.axis_size("dp")
    n_c = lax.axis_size("cent")
    z = lax.axis_index("outer")
    y = lax.axis_index("dp")
    q = lax.axis_index("cent")
    t, d = rows.shape
    tq = t // n_c
    n_od = n_o * n_d

    rows_bf = rows.astype(jnp.bfloat16)
    cent_bf = centroids.astype(jnp.bfloat16)
    squares = jnp.sum(centroids * centroids, axis=1)

    bits = []
    b = 1
    while b < n_c:
        bits.append(b)
        b *= 2
    xs = [0]
    for bit in reversed(bits):
        xs = xs + [x ^ bit for x in xs]

    mine = lax.dynamic_slice_in_dim(rows_bf, q * tq, tq, 0)
    shifts = list(itertools.product(range(n_o), range(n_d)))
    def pair_of(piece):
        across = [piece]
        for sy in range(1, n_d):
            across.append(lax.ppermute(piece, "dp", [(j, (j + sy) % n_d) for j in range(n_d)]))
        return jnp.stack(across)

    def spread(cur):
        for bit in reversed(bits):
            other = lax.ppermute(cur, "cent", [(i, i ^ bit) for i in range(n_c)])
            cur = jnp.concatenate([cur, other], axis=1)
        return cur

    landed = [mine]
    for sz in range(1, n_o):
        if n_o & (n_o - 1) == 0:
            pairs = [(i, i ^ sz) for i in range(n_o)]
        else:
            pairs = [(i, (i + sz) % n_o) for i in range(n_o)]
        landed.append(lax.ppermute(mine, "outer", pairs))
    def spread_x_first(piece):
        order = list(reversed(bits))
        other = lax.ppermute(piece, "cent", [(i, i ^ order[0]) for i in range(n_c)])
        cur = pair_of(jnp.concatenate([piece, other], axis=0))
        for bit in order[1:]:
            other = lax.ppermute(cur, "cent", [(i, i ^ bit) for i in range(n_c)])
            cur = jnp.concatenate([cur, other], axis=1)
        return cur

    parts = [None] + [
        spread_x_first(piece) if sz == 1 else spread(pair_of(piece))
        for sz, piece in enumerate(landed[1:], start=1)
    ]

    h = q % 2
    half = t // 2
    my_half = lax.dynamic_slice_in_dim(rows_bf, h * half, half, 0)
    own_blocks = [rows_bf]
    for sy in range(1, n_d):
        got = lax.ppermute(my_half, "dp", [(j, (j + sy) % n_d) for j in range(n_d)])
        mate = lax.ppermute(got, "cent", [(i, i ^ 1) for i in range(n_c)])
        own_blocks.append(jnp.concatenate([got, mate], axis=0))
    parts[0] = jnp.stack(own_blocks)

    cur = jnp.zeros((n_o * n_d,) + parts[0].shape[1:], parts[0].dtype)
    for sz in range(n_o):
        pod_of = (z ^ sz) if n_o & (n_o - 1) == 0 else (z - sz) % n_o
        cur = lax.dynamic_update_slice_in_dim(cur, parts[sz], pod_of * n_d, axis=0)
    everything = cur.reshape(n_od * n_c * tq, d)

    logits = scores_for(everything, cent_bf, squares)
    local_max, local_sum = row_summary(logits)

    src_vec = jnp.stack([a * n_d + (y - sy) % n_d for a, sy in shifts])
    hot_k = src_vec[None, :] == jnp.arange(n_od)[:, None]
    jj = jnp.arange(n_c)
    xor_map = q ^ jnp.asarray(xs, jnp.int32)
    hq = n_c // 2
    half_map = ((jj // hq) ^ h) * hq + jj % hq
    maps = []
    for a, sy in shifts:
        own_map = jj if sy == 0 else half_map
        maps.append(jnp.where(a == z, own_map, xor_map))
    c_map = jnp.stack(maps)
    hot_kc = c_map[:, None, :] == jj[None, :, None]

    def to_absolute(v):
        v = v.reshape(n_od, n_c, tq)
        v = jnp.sum(jnp.where(hot_kc[:, :, :, None], v[:, None, :, :], 0.0), axis=2)
        return jnp.sum(jnp.where(hot_k[:, :, None, None], v[None], 0.0), axis=1)

    def to_local(v):
        v = jnp.sum(jnp.where(hot_k[:, :, None, None], v[:, None], 0.0), axis=0)
        v = jnp.sum(jnp.where(hot_kc[:, :, :, None], v[:, :, None, :], 0.0), axis=1)
        return v.reshape(n_od * n_c * tq)

    both = jnp.stack([to_absolute(local_max), to_absolute(local_sum)])
    every = lax.all_gather(both, ("dp", "cent"), axis=0)
    maxes, sums = every[:, 0], every[:, 1]
    peak_abs = jnp.max(maxes, axis=0)
    mass_abs = jnp.sum(sums * jnp.exp(maxes - peak_abs[None]), axis=0)
    row_peak = to_local(peak_abs)
    row_mass = to_local(mass_abs)

    weights = (jnp.exp(logits - row_peak[:, None]) / row_mass[:, None]).astype(jnp.bfloat16)
    k = centroids.shape[0]
    pod = n_d * n_c * tq
    w_pods = weights.reshape(n_o, pod, k).astype(jnp.float32)
    weight_sum = jnp.sum(w_pods, axis=1)
    scaled = (w_pods / (weight_sum[:, None, :] + 1.0)).astype(jnp.bfloat16)
    pull = lax.dot_general(
        scaled.reshape(n_o * pod, k), everything, (((0,), (0,)), ((), ())),
        preferred_element_type=jnp.float32,
    )
    coef = None
    for a in range(n_o):
        term = weight_sum[a] / (weight_sum[a] + 1.0)
        coef = term if coef is None else coef + term
    return (pull - coef[:, None] * centroids) / n_o


def solution(mesh):
    n_o, n_d, n_c = mesh.shape["outer"], mesh.shape["dp"], mesh.shape["cent"]

    def shards(rows, centroids):
        t, d = rows.shape
        k = centroids.shape[0]
        n_all = t * n_o * n_d
        footprint = n_all * d * 2 + n_all * k * 4 * 2
        if footprint <= (24 << 20) and t % n_c == 0 and n_c >= 2 and (n_c & (n_c - 1)) == 0:
            return shards_all(rows, centroids)
        return shards_pod(rows, centroids)

    return jax.shard_map(
        shards,
        mesh=mesh,
        in_specs=(P(("outer", "dp"), None), P(("dp", "cent"), None)),
        out_specs=P(("dp", "cent"), None),
        check_vma=False,
    )
```

```python
import itertools

import jax
import jax.numpy as jnp
from jax import lax
from jax.sharding import PartitionSpec as P


def scores_for(piece, cent_bf, squares):
    product = lax.dot_general(
        piece, cent_bf, (((1,), (1,)), ((), ())), preferred_element_type=jnp.float32
    )
    return 0.5 * (2.0 * product - squares[None, :])


def row_summary(logits):
    local_max = jnp.max(logits, axis=1)
    local_sum = jnp.sum(jnp.exp(logits - local_max[:, None]), axis=1)
    return (local_max, local_sum)


def global_stats(local_max, local_sum):
    row_peak = lax.pmax(local_max, ("dp", "cent"))
    row_mass = lax.psum(local_sum * jnp.exp(local_max - row_peak), ("dp", "cent"))
    return (row_peak, row_mass)


def shards_pod(rows, centroids):
    rows_bf = rows.astype(jnp.bfloat16)
    cent_bf = centroids.astype(jnp.bfloat16)
    squares = jnp.sum(centroids * centroids, axis=1)
    gathered = lax.all_gather(rows_bf, "dp", axis=0, tiled=True)
    logits = scores_for(gathered, cent_bf, squares)
    local_max, local_sum = row_summary(logits)
    row_peak, row_mass = global_stats(local_max, local_sum)
    weights = (jnp.exp(logits - row_peak[:, None]) / row_mass[:, None]).astype(jnp.bfloat16)
    weight_sum = jnp.sum(weights.astype(jnp.float32), axis=0)
    pull = lax.dot_general(
        weights, gathered, (((0,), (0,)), ((), ())), preferred_element_type=jnp.float32
    )
    delta = (pull - weight_sum[:, None] * centroids) / (weight_sum[:, None] + 1.0)
    return lax.psum(delta, "outer") / lax.axis_size("outer")


def shards_all(rows, centroids):
    n_o = lax.axis_size("outer")
    n_d = lax.axis_size("dp")
    n_c = lax.axis_size("cent")
    z = lax.axis_index("outer")
    y = lax.axis_index("dp")
    q = lax.axis_index("cent")
    t, d = rows.shape
    tq = t // n_c
    n_od = n_o * n_d

    rows_bf = rows.astype(jnp.bfloat16)
    cent_bf = centroids.astype(jnp.bfloat16)
    squares = jnp.sum(centroids * centroids, axis=1)

    bits = []
    b = 1
    while b < n_c:
        bits.append(b)
        b *= 2
    xs = [0]
    for bit in reversed(bits):
        xs = xs + [x ^ bit for x in xs]

    mine = lax.dynamic_slice_in_dim(rows_bf, q * tq, tq, 0)
    shifts = list(itertools.product(range(n_o), range(n_d)))
    def pair_of(piece):
        across = [piece]
        for sy in range(1, n_d):
            across.append(lax.ppermute(piece, "dp", [(j, (j + sy) % n_d) for j in range(n_d)]))
        return jnp.stack(across)

    def spread(cur):
        for bit in reversed(bits):
            other = lax.ppermute(cur, "cent", [(i, i ^ bit) for i in range(n_c)])
            cur = jnp.concatenate([cur, other], axis=1)
        return cur

    landed = [mine]
    for sz in range(1, n_o):
        if n_o & (n_o - 1) == 0:
            pairs = [(i, i ^ sz) for i in range(n_o)]
        else:
            pairs = [(i, (i + sz) % n_o) for i in range(n_o)]
        landed.append(lax.ppermute(mine, "outer", pairs))
    def spread_x_first(piece):
        order = list(reversed(bits))
        other = lax.ppermute(piece, "cent", [(i, i ^ order[0]) for i in range(n_c)])
        cur = pair_of(jnp.concatenate([piece, other], axis=0))
        for bit in order[1:]:
            other = lax.ppermute(cur, "cent", [(i, i ^ bit) for i in range(n_c)])
            cur = jnp.concatenate([cur, other], axis=1)
        return cur

    parts = [None] + [
        spread_x_first(piece) if sz <= 2 else spread(pair_of(piece))
        for sz, piece in enumerate(landed[1:], start=1)
    ]

    h = q % 2
    half = t // 2
    my_half = lax.dynamic_slice_in_dim(rows_bf, h * half, half, 0)
    own_blocks = [rows_bf]
    for sy in range(1, n_d):
        got = lax.ppermute(my_half, "dp", [(j, (j + sy) % n_d) for j in range(n_d)])
        mate = lax.ppermute(got, "cent", [(i, i ^ 1) for i in range(n_c)])
        own_blocks.append(jnp.concatenate([got, mate], axis=0))
    parts[0] = jnp.stack(own_blocks)

    cur = jnp.zeros((n_o * n_d,) + parts[0].shape[1:], parts[0].dtype)
    for sz in range(n_o):
        pod_of = (z ^ sz) if n_o & (n_o - 1) == 0 else (z - sz) % n_o
        cur = lax.dynamic_update_slice_in_dim(cur, parts[sz], pod_of * n_d, axis=0)
    everything = cur.reshape(n_od * n_c * tq, d)

    logits = scores_for(everything, cent_bf, squares)
    local_max, local_sum = row_summary(logits)

    src_vec = jnp.stack([a * n_d + (y - sy) % n_d for a, sy in shifts])
    hot_k = src_vec[None, :] == jnp.arange(n_od)[:, None]
    jj = jnp.arange(n_c)
    xor_map = q ^ jnp.asarray(xs, jnp.int32)
    hq = n_c // 2
    half_map = ((jj // hq) ^ h) * hq + jj % hq
    maps = []
    for a, sy in shifts:
        own_map = jj if sy == 0 else half_map
        maps.append(jnp.where(a == z, own_map, xor_map))
    c_map = jnp.stack(maps)
    hot_kc = c_map[:, None, :] == jj[None, :, None]

    def to_absolute(v):
        v = v.reshape(n_od, n_c, tq)
        v = jnp.sum(jnp.where(hot_kc[:, :, :, None], v[:, None, :, :], 0.0), axis=2)
        return jnp.sum(jnp.where(hot_k[:, :, None, None], v[None], 0.0), axis=1)

    def to_local(v):
        v = jnp.sum(jnp.where(hot_k[:, :, None, None], v[:, None], 0.0), axis=0)
        v = jnp.sum(jnp.where(hot_kc[:, :, :, None], v[:, :, None, :], 0.0), axis=1)
        return v.reshape(n_od * n_c * tq)

    both = jnp.stack([to_absolute(local_max), to_absolute(local_sum)])
    every = lax.all_gather(both, ("dp", "cent"), axis=0)
    maxes, sums = every[:, 0], every[:, 1]
    peak_abs = jnp.max(maxes, axis=0)
    mass_abs = jnp.sum(sums * jnp.exp(maxes - peak_abs[None]), axis=0)
    row_peak = to_local(peak_abs)
    row_mass = to_local(mass_abs)

    weights = (jnp.exp(logits - row_peak[:, None]) / row_mass[:, None]).astype(jnp.bfloat16)
    k = centroids.shape[0]
    pod = n_d * n_c * tq
    w_pods = weights.reshape(n_o, pod, k).astype(jnp.float32)
    weight_sum = jnp.sum(w_pods, axis=1)
    scaled = (w_pods / (weight_sum[:, None, :] + 1.0)).astype(jnp.bfloat16)
    pull = lax.dot_general(
        scaled.reshape(n_o * pod, k), everything, (((0,), (0,)), ((), ())),
        preferred_element_type=jnp.float32,
    )
    coef = None
    for a in range(n_o):
        term = weight_sum[a] / (weight_sum[a] + 1.0)
        coef = term if coef is None else coef + term
    return (pull - coef[:, None] * centroids) / n_o


def solution(mesh):
    n_o, n_d, n_c = mesh.shape["outer"], mesh.shape["dp"], mesh.shape["cent"]

    def shards(rows, centroids):
        t, d = rows.shape
        k = centroids.shape[0]
        n_all = t * n_o * n_d
        footprint = n_all * d * 2 + n_all * k * 4 * 2
        if footprint <= (24 << 20) and t % n_c == 0 and n_c >= 2 and (n_c & (n_c - 1)) == 0:
            return shards_all(rows, centroids)
        return shards_pod(rows, centroids)

    return jax.shard_map(
        shards,
        mesh=mesh,
        in_specs=(P(("outer", "dp"), None), P(("dp", "cent"), None)),
        out_specs=P(("dp", "cent"), None),
        check_vma=False,
    )
```

```python
import itertools

import jax
import jax.numpy as jnp
from jax import lax
from jax.sharding import PartitionSpec as P


def scores_for(piece, cent_bf, squares):
    product = lax.dot_general(
        piece, cent_bf, (((1,), (1,)), ((), ())), preferred_element_type=jnp.float32
    )
    return 0.5 * (2.0 * product - squares[None, :])


def row_summary(logits):
    local_max = jnp.max(logits, axis=1)
    local_sum = jnp.sum(jnp.exp(logits - local_max[:, None]), axis=1)
    return (local_max, local_sum)


def global_stats(local_max, local_sum):
    row_peak = lax.pmax(local_max, ("dp", "cent"))
    row_mass = lax.psum(local_sum * jnp.exp(local_max - row_peak), ("dp", "cent"))
    return (row_peak, row_mass)


def shards_pod(rows, centroids):
    rows_bf = rows.astype(jnp.bfloat16)
    cent_bf = centroids.astype(jnp.bfloat16)
    squares = jnp.sum(centroids * centroids, axis=1)
    gathered = lax.all_gather(rows_bf, "dp", axis=0, tiled=True)
    logits = scores_for(gathered, cent_bf, squares)
    local_max, local_sum = row_summary(logits)
    row_peak, row_mass = global_stats(local_max, local_sum)
    weights = (jnp.exp(logits - row_peak[:, None]) / row_mass[:, None]).astype(jnp.bfloat16)
    weight_sum = jnp.sum(weights.astype(jnp.float32), axis=0)
    pull = lax.dot_general(
        weights, gathered, (((0,), (0,)), ((), ())), preferred_element_type=jnp.float32
    )
    delta = (pull - weight_sum[:, None] * centroids) / (weight_sum[:, None] + 1.0)
    return lax.psum(delta, "outer") / lax.axis_size("outer")


def shards_all(rows, centroids):
    n_o = lax.axis_size("outer")
    n_d = lax.axis_size("dp")
    n_c = lax.axis_size("cent")
    z = lax.axis_index("outer")
    y = lax.axis_index("dp")
    q = lax.axis_index("cent")
    t, d = rows.shape
    tq = t // n_c
    n_od = n_o * n_d

    rows_bf = rows.astype(jnp.bfloat16)
    cent_bf = centroids.astype(jnp.bfloat16)
    squares = jnp.sum(centroids * centroids, axis=1)

    bits = []
    b = 1
    while b < n_c:
        bits.append(b)
        b *= 2
    xs = [0]
    for bit in reversed(bits):
        xs = xs + [x ^ bit for x in xs]

    mine = lax.dynamic_slice_in_dim(rows_bf, q * tq, tq, 0)
    shifts = list(itertools.product(range(n_o), range(n_d)))
    def pair_of(piece):
        across = [piece]
        for sy in range(1, n_d):
            across.append(lax.ppermute(piece, "dp", [(j, (j + sy) % n_d) for j in range(n_d)]))
        return jnp.stack(across)

    def x_stage(pieces, bit):
        keys = list(pieces)
        got = lax.ppermute(tuple(pieces[kk] for kk in keys), "cent", [(i, i ^ bit) for i in range(n_c)])
        out = dict(pieces)
        for (sy, v), arr in zip(keys, got):
            out[(sy, v ^ bit)] = arr
        return out

    def y_stage(pieces):
        keys = list(pieces)
        out = dict(pieces)
        for sh in range(1, n_d):
            got = lax.ppermute(tuple(pieces[kk] for kk in keys), "dp", [(j, (j + sh) % n_d) for j in range(n_d)])
            for (sy, v), arr in zip(keys, got):
                out[((sy + sh) % n_d, v)] = arr
        return out

    landed = [mine]
    for sz in range(1, n_o):
        if n_o & (n_o - 1) == 0:
            pairs = [(i, i ^ sz) for i in range(n_o)]
        else:
            pairs = [(i, (i + sz) % n_o) for i in range(n_o)]
        landed.append(lax.ppermute(mine, "outer", pairs))

    order = list(reversed(bits))
    groups = [None]
    for sz in range(1, n_o):
        g = {(0, 0): landed[sz]}
        if sz == 1:
            g = x_stage(g, order[0])
            g = y_stage(g)
            for bit in order[1:]:
                g = x_stage(g, bit)
        else:
            g = y_stage(g)
            for bit in order:
                g = x_stage(g, bit)
        groups.append(g)

    h = q % 2
    half = t // 2
    hq = n_c // 2
    my_half = lax.dynamic_slice_in_dim(rows_bf, h * half, half, 0)

    def pod_of(sz):
        return (z ^ sz) if n_o & (n_o - 1) == 0 else (z - sz) % n_o

    buf = jnp.zeros((n_o * n_d, n_c, tq, d), rows_bf.dtype)
    own = pod_of(0) * n_d
    buf = lax.dynamic_update_slice(buf, rows_bf.reshape(1, n_c, tq, d), (own, 0, 0, 0))
    for sy in range(1, n_d):
        got = lax.ppermute(my_half, "dp", [(j, (j + sy) % n_d) for j in range(n_d)])
        mate = lax.ppermute(got, "cent", [(i, i ^ 1) for i in range(n_c)])
        buf = lax.dynamic_update_slice(buf, got.reshape(1, hq, tq, d), (own + sy, 0, 0, 0))
        buf = lax.dynamic_update_slice(buf, mate.reshape(1, hq, tq, d), (own + sy, hq, 0, 0))
    for sz in range(1, n_o):
        base = pod_of(sz) * n_d
        for (sy, v), arr in groups[sz].items():
            buf = lax.dynamic_update_slice(buf, arr[None, None], (base + sy, xs.index(v), 0, 0))
    everything = buf.reshape(n_od * n_c * tq, d)

    logits = scores_for(everything, cent_bf, squares)
    local_max, local_sum = row_summary(logits)

    src_vec = jnp.stack([a * n_d + (y - sy) % n_d for a, sy in shifts])
    hot_k = src_vec[None, :] == jnp.arange(n_od)[:, None]
    jj = jnp.arange(n_c)
    xor_map = q ^ jnp.asarray(xs, jnp.int32)
    hq = n_c // 2
    half_map = ((jj // hq) ^ h) * hq + jj % hq
    maps = []
    for a, sy in shifts:
        own_map = jj if sy == 0 else half_map
        maps.append(jnp.where(a == z, own_map, xor_map))
    c_map = jnp.stack(maps)
    hot_kc = c_map[:, None, :] == jj[None, :, None]

    def to_absolute(v):
        v = v.reshape(n_od, n_c, tq)
        v = jnp.sum(jnp.where(hot_kc[:, :, :, None], v[:, None, :, :], 0.0), axis=2)
        return jnp.sum(jnp.where(hot_k[:, :, None, None], v[None], 0.0), axis=1)

    def to_local(v):
        v = jnp.sum(jnp.where(hot_k[:, :, None, None], v[:, None], 0.0), axis=0)
        v = jnp.sum(jnp.where(hot_kc[:, :, :, None], v[:, :, None, :], 0.0), axis=1)
        return v.reshape(n_od * n_c * tq)

    both = jnp.stack([to_absolute(local_max), to_absolute(local_sum)])
    every = lax.all_gather(both, ("dp", "cent"), axis=0)
    maxes, sums = every[:, 0], every[:, 1]
    peak_abs = jnp.max(maxes, axis=0)
    mass_abs = jnp.sum(sums * jnp.exp(maxes - peak_abs[None]), axis=0)
    row_peak = to_local(peak_abs)
    row_mass = to_local(mass_abs)

    weights = (jnp.exp(logits - row_peak[:, None]) / row_mass[:, None]).astype(jnp.bfloat16)
    k = centroids.shape[0]
    pod = n_d * n_c * tq
    w_pods = weights.reshape(n_o, pod, k).astype(jnp.float32)
    weight_sum = jnp.sum(w_pods, axis=1)
    scaled = (w_pods / (weight_sum[:, None, :] + 1.0)).astype(jnp.bfloat16)
    pull = lax.dot_general(
        scaled.reshape(n_o * pod, k), everything, (((0,), (0,)), ((), ())),
        preferred_element_type=jnp.float32,
    )
    coef = None
    for a in range(n_o):
        term = weight_sum[a] / (weight_sum[a] + 1.0)
        coef = term if coef is None else coef + term
    return (pull - coef[:, None] * centroids) / n_o


def solution(mesh):
    n_o, n_d, n_c = mesh.shape["outer"], mesh.shape["dp"], mesh.shape["cent"]

    def shards(rows, centroids):
        t, d = rows.shape
        k = centroids.shape[0]
        n_all = t * n_o * n_d
        footprint = n_all * d * 2 + n_all * k * 4 * 2
        if footprint <= (24 << 20) and t % n_c == 0 and n_c >= 2 and (n_c & (n_c - 1)) == 0:
            return shards_all(rows, centroids)
        return shards_pod(rows, centroids)

    return jax.shard_map(
        shards,
        mesh=mesh,
        in_specs=(P(("outer", "dp"), None), P(("dp", "cent"), None)),
        out_specs=P(("dp", "cent"), None),
        check_vma=False,
    )
```

```python
import itertools

import jax
import jax.numpy as jnp
from jax import lax
from jax.sharding import PartitionSpec as P


def scores_for(piece, cent_bf, squares):
    product = lax.dot_general(
        piece, cent_bf, (((1,), (1,)), ((), ())), preferred_element_type=jnp.float32
    )
    return 0.5 * (2.0 * product - squares[None, :])


def row_summary(logits):
    local_max = jnp.max(logits, axis=1)
    local_sum = jnp.sum(jnp.exp(logits - local_max[:, None]), axis=1)
    return (local_max, local_sum)


def global_stats(local_max, local_sum):
    row_peak = lax.pmax(local_max, ("dp", "cent"))
    row_mass = lax.psum(local_sum * jnp.exp(local_max - row_peak), ("dp", "cent"))
    return (row_peak, row_mass)


def shards_pod(rows, centroids):
    rows_bf = rows.astype(jnp.bfloat16)
    cent_bf = centroids.astype(jnp.bfloat16)
    squares = jnp.sum(centroids * centroids, axis=1)
    gathered = lax.all_gather(rows_bf, "dp", axis=0, tiled=True)
    logits = scores_for(gathered, cent_bf, squares)
    local_max, local_sum = row_summary(logits)
    row_peak, row_mass = global_stats(local_max, local_sum)
    weights = (jnp.exp(logits - row_peak[:, None]) / row_mass[:, None]).astype(jnp.bfloat16)
    weight_sum = jnp.sum(weights.astype(jnp.float32), axis=0)
    pull = lax.dot_general(
        weights, gathered, (((0,), (0,)), ((), ())), preferred_element_type=jnp.float32
    )
    delta = (pull - weight_sum[:, None] * centroids) / (weight_sum[:, None] + 1.0)
    return lax.psum(delta, "outer") / lax.axis_size("outer")


def shards_all(rows, centroids):
    n_o = lax.axis_size("outer")
    n_d = lax.axis_size("dp")
    n_c = lax.axis_size("cent")
    z = lax.axis_index("outer")
    y = lax.axis_index("dp")
    q = lax.axis_index("cent")
    t, d = rows.shape
    tq = t // n_c
    n_od = n_o * n_d

    rows_bf = rows.astype(jnp.bfloat16)
    cent_bf = centroids.astype(jnp.bfloat16)
    squares = jnp.sum(centroids * centroids, axis=1)

    bits = []
    b = 1
    while b < n_c:
        bits.append(b)
        b *= 2
    xs = [0]
    for bit in reversed(bits):
        xs = xs + [x ^ bit for x in xs]

    mine = lax.dynamic_slice_in_dim(rows_bf, q * tq, tq, 0)
    shifts = list(itertools.product(range(n_o), range(n_d)))
    def pair_of(piece):
        across = [piece]
        for sy in range(1, n_d):
            across.append(lax.ppermute(piece, "dp", [(j, (j + sy) % n_d) for j in range(n_d)]))
        return jnp.stack(across)

    def spread(cur):
        for bit in reversed(bits):
            other = lax.ppermute(cur, "cent", [(i, i ^ bit) for i in range(n_c)])
            cur = jnp.concatenate([cur, other], axis=1)
        return cur

    landed = [mine]
    for sz in range(1, n_o):
        if n_o & (n_o - 1) == 0:
            pairs = [(i, i ^ sz) for i in range(n_o)]
        else:
            pairs = [(i, (i + sz) % n_o) for i in range(n_o)]
        landed.append(lax.ppermute(mine, "outer", pairs))
    def spread_x_first(piece):
        order = list(reversed(bits))
        other = lax.ppermute(piece, "cent", [(i, i ^ order[0]) for i in range(n_c)])
        cur = pair_of(jnp.concatenate([piece, other], axis=0))
        for bit in order[1:]:
            other = lax.ppermute(cur, "cent", [(i, i ^ bit) for i in range(n_c)])
            cur = jnp.concatenate([cur, other], axis=1)
        return cur

    parts = [None, spread_x_first(landed[1])] if n_o > 1 else [None]
    if n_o > 2:
        late = pair_of(jnp.stack(landed[2:]))
        for bit in reversed(bits):
            other = lax.ppermute(late, "cent", [(i, i ^ bit) for i in range(n_c)])
            late = jnp.concatenate([late, other], axis=2)
        parts += [late[:, g] for g in range(n_o - 2)]

    h = q % 2
    half = t // 2
    my_half = lax.dynamic_slice_in_dim(rows_bf, h * half, half, 0)
    own_blocks = [rows_bf]
    for sy in range(1, n_d):
        got = lax.ppermute(my_half, "dp", [(j, (j + sy) % n_d) for j in range(n_d)])
        mate = lax.ppermute(got, "cent", [(i, i ^ 1) for i in range(n_c)])
        own_blocks.append(jnp.concatenate([got, mate], axis=0))
    parts[0] = jnp.stack(own_blocks)

    cur = jnp.zeros((n_o * n_d,) + parts[0].shape[1:], parts[0].dtype)
    for sz in range(n_o):
        pod_of = (z ^ sz) if n_o & (n_o - 1) == 0 else (z - sz) % n_o
        cur = lax.dynamic_update_slice_in_dim(cur, parts[sz], pod_of * n_d, axis=0)
    everything = cur.reshape(n_od * n_c * tq, d)

    logits = scores_for(everything, cent_bf, squares)
    local_max, local_sum = row_summary(logits)

    src_vec = jnp.stack([a * n_d + (y - sy) % n_d for a, sy in shifts])
    hot_k = src_vec[None, :] == jnp.arange(n_od)[:, None]
    jj = jnp.arange(n_c)
    xor_map = q ^ jnp.asarray(xs, jnp.int32)
    hq = n_c // 2
    half_map = ((jj // hq) ^ h) * hq + jj % hq
    maps = []
    for a, sy in shifts:
        own_map = jj if sy == 0 else half_map
        maps.append(jnp.where(a == z, own_map, xor_map))
    c_map = jnp.stack(maps)
    hot_kc = c_map[:, None, :] == jj[None, :, None]

    def to_absolute(v):
        v = v.reshape(n_od, n_c, tq)
        v = jnp.sum(jnp.where(hot_kc[:, :, :, None], v[:, None, :, :], 0.0), axis=2)
        return jnp.sum(jnp.where(hot_k[:, :, None, None], v[None], 0.0), axis=1)

    def to_local(v):
        v = jnp.sum(jnp.where(hot_k[:, :, None, None], v[:, None], 0.0), axis=0)
        v = jnp.sum(jnp.where(hot_kc[:, :, :, None], v[:, :, None, :], 0.0), axis=1)
        return v.reshape(n_od * n_c * tq)

    both = jnp.stack([to_absolute(local_max), to_absolute(local_sum)])
    every = lax.all_gather(both, ("dp", "cent"), axis=0)
    maxes, sums = every[:, 0], every[:, 1]
    peak_abs = jnp.max(maxes, axis=0)
    mass_abs = jnp.sum(sums * jnp.exp(maxes - peak_abs[None]), axis=0)
    row_peak = to_local(peak_abs)
    row_mass = to_local(mass_abs)

    weights = (jnp.exp(logits - row_peak[:, None]) / row_mass[:, None]).astype(jnp.bfloat16)
    k = centroids.shape[0]
    pod = n_d * n_c * tq
    w_pods = weights.reshape(n_o, pod, k).astype(jnp.float32)
    weight_sum = jnp.sum(w_pods, axis=1)
    scaled = (w_pods / (weight_sum[:, None, :] + 1.0)).astype(jnp.bfloat16)
    pull = lax.dot_general(
        scaled.reshape(n_o * pod, k), everything, (((0,), (0,)), ((), ())),
        preferred_element_type=jnp.float32,
    )
    coef = None
    for a in range(n_o):
        term = weight_sum[a] / (weight_sum[a] + 1.0)
        coef = term if coef is None else coef + term
    return (pull - coef[:, None] * centroids) / n_o


def solution(mesh):
    n_o, n_d, n_c = mesh.shape["outer"], mesh.shape["dp"], mesh.shape["cent"]

    def shards(rows, centroids):
        t, d = rows.shape
        k = centroids.shape[0]
        n_all = t * n_o * n_d
        footprint = n_all * d * 2 + n_all * k * 4 * 2
        if footprint <= (24 << 20) and t % n_c == 0 and n_c >= 2 and (n_c & (n_c - 1)) == 0:
            return shards_all(rows, centroids)
        return shards_pod(rows, centroids)

    return jax.shard_map(
        shards,
        mesh=mesh,
        in_specs=(P(("outer", "dp"), None), P(("dp", "cent"), None)),
        out_specs=P(("dp", "cent"), None),
        check_vma=False,
    )
```

```python
import itertools

import jax
import jax.numpy as jnp
from jax import lax
from jax.sharding import PartitionSpec as P


def scores_for(piece, cent_bf, squares):
    product = lax.dot_general(
        piece, cent_bf, (((1,), (1,)), ((), ())), preferred_element_type=jnp.float32
    )
    return 0.5 * (2.0 * product - squares[None, :])


def row_summary(logits):
    local_max = jnp.max(logits, axis=1)
    local_sum = jnp.sum(jnp.exp(logits - local_max[:, None]), axis=1)
    return (local_max, local_sum)


def global_stats(local_max, local_sum):
    row_peak = lax.pmax(local_max, ("dp", "cent"))
    row_mass = lax.psum(local_sum * jnp.exp(local_max - row_peak), ("dp", "cent"))
    return (row_peak, row_mass)


def shards_pod(rows, centroids):
    rows_bf = rows.astype(jnp.bfloat16)
    cent_bf = centroids.astype(jnp.bfloat16)
    squares = jnp.sum(centroids * centroids, axis=1)
    gathered = lax.all_gather(rows_bf, "dp", axis=0, tiled=True)
    logits = scores_for(gathered, cent_bf, squares)
    local_max, local_sum = row_summary(logits)
    row_peak, row_mass = global_stats(local_max, local_sum)
    weights = (jnp.exp(logits - row_peak[:, None]) / row_mass[:, None]).astype(jnp.bfloat16)
    weight_sum = jnp.sum(weights.astype(jnp.float32), axis=0)
    pull = lax.dot_general(
        weights, gathered, (((0,), (0,)), ((), ())), preferred_element_type=jnp.float32
    )
    delta = (pull - weight_sum[:, None] * centroids) / (weight_sum[:, None] + 1.0)
    return lax.psum(delta, "outer") / lax.axis_size("outer")


def shards_all(rows, centroids):
    n_o = lax.axis_size("outer")
    n_d = lax.axis_size("dp")
    n_c = lax.axis_size("cent")
    z = lax.axis_index("outer")
    y = lax.axis_index("dp")
    q = lax.axis_index("cent")
    t, d = rows.shape
    tq = t // n_c
    n_od = n_o * n_d

    rows_bf = rows.astype(jnp.bfloat16)
    cent_bf = centroids.astype(jnp.bfloat16)
    squares = jnp.sum(centroids * centroids, axis=1)

    bits = []
    b = 1
    while b < n_c:
        bits.append(b)
        b *= 2
    xs = [0]
    for bit in reversed(bits):
        xs = xs + [x ^ bit for x in xs]

    mine = lax.dynamic_slice_in_dim(rows_bf, q * tq, tq, 0)
    shifts = list(itertools.product(range(n_o), range(n_d)))
    def pair_of(piece):
        across = [piece]
        for sy in range(1, n_d):
            across.append(lax.ppermute(piece, "dp", [(j, (j + sy) % n_d) for j in range(n_d)]))
        return jnp.stack(across)

    def spread(cur, first=None):
        order = list(reversed(bits))
        if first is not None:
            other = lax.ppermute(cur, "cent", [(i, i ^ first) for i in range(n_c)])
            cur = pair_of(jnp.concatenate([cur, other], axis=0))
            order = order[1:]
        else:
            cur = pair_of(cur)
        for bit in order[:-1]:
            other = lax.ppermute(cur, "cent", [(i, i ^ bit) for i in range(n_c)])
            cur = jnp.concatenate([cur, other], axis=1)
        last = lax.ppermute(cur, "cent", [(i, i ^ order[-1]) for i in range(n_c)])
        return cur, last

    landed = [mine]
    for sz in range(1, n_o):
        if n_o & (n_o - 1) == 0:
            pairs = [(i, i ^ sz) for i in range(n_o)]
        else:
            pairs = [(i, (i + sz) % n_o) for i in range(n_o)]
        landed.append(lax.ppermute(mine, "outer", pairs))

    def pod_of(sz):
        return (z ^ sz) if n_o & (n_o - 1) == 0 else (z - sz) % n_o

    cur = jnp.zeros((n_o * n_d, n_c * tq, d), rows_bf.dtype)
    hrows = (n_c // 2) * tq

    h = q % 2
    half = t // 2
    my_half = lax.dynamic_slice_in_dim(rows_bf, h * half, half, 0)
    own = pod_of(0) * n_d
    cur = lax.dynamic_update_slice(cur, rows_bf[None], (own, 0, 0))
    for sy in range(1, n_d):
        got = lax.ppermute(my_half, "dp", [(j, (j + sy) % n_d) for j in range(n_d)])
        mate = lax.ppermute(got, "cent", [(i, i ^ 1) for i in range(n_c)])
        cur = lax.dynamic_update_slice(cur, got[None], (own + sy, 0, 0))
        cur = lax.dynamic_update_slice(cur, mate[None], (own + sy, half, 0))

    order = list(reversed(bits))
    for sz in range(1, n_o):
        kept, brought = spread(landed[sz], first=order[0] if sz == 1 and len(order) > 1 else None)
        base = pod_of(sz) * n_d
        cur = lax.dynamic_update_slice(cur, kept, (base, 0, 0))
        cur = lax.dynamic_update_slice(cur, brought, (base, hrows, 0))

    everything = cur.reshape(n_od * n_c * tq, d)

    logits = scores_for(everything, cent_bf, squares)
    local_max, local_sum = row_summary(logits)

    src_vec = jnp.stack([a * n_d + (y - sy) % n_d for a, sy in shifts])
    hot_k = src_vec[None, :] == jnp.arange(n_od)[:, None]
    jj = jnp.arange(n_c)
    xor_map = q ^ jnp.asarray(xs, jnp.int32)
    hq = n_c // 2
    half_map = ((jj // hq) ^ h) * hq + jj % hq
    maps = []
    for a, sy in shifts:
        own_map = jj if sy == 0 else half_map
        maps.append(jnp.where(a == z, own_map, xor_map))
    c_map = jnp.stack(maps)
    hot_kc = c_map[:, None, :] == jj[None, :, None]

    def to_absolute(v):
        v = v.reshape(n_od, n_c, tq)
        v = jnp.sum(jnp.where(hot_kc[:, :, :, None], v[:, None, :, :], 0.0), axis=2)
        return jnp.sum(jnp.where(hot_k[:, :, None, None], v[None], 0.0), axis=1)

    def to_local(v):
        v = jnp.sum(jnp.where(hot_k[:, :, None, None], v[:, None], 0.0), axis=0)
        v = jnp.sum(jnp.where(hot_kc[:, :, :, None], v[:, :, None, :], 0.0), axis=1)
        return v.reshape(n_od * n_c * tq)

    both = jnp.stack([to_absolute(local_max), to_absolute(local_sum)])
    every = lax.all_gather(both, ("dp", "cent"), axis=0)
    maxes, sums = every[:, 0], every[:, 1]
    peak_abs = jnp.max(maxes, axis=0)
    mass_abs = jnp.sum(sums * jnp.exp(maxes - peak_abs[None]), axis=0)
    row_peak = to_local(peak_abs)
    row_mass = to_local(mass_abs)

    weights = (jnp.exp(logits - row_peak[:, None]) / row_mass[:, None]).astype(jnp.bfloat16)
    k = centroids.shape[0]
    pod = n_d * n_c * tq
    w_pods = weights.reshape(n_o, pod, k).astype(jnp.float32)
    weight_sum = jnp.sum(w_pods, axis=1)
    scaled = (w_pods / (weight_sum[:, None, :] + 1.0)).astype(jnp.bfloat16)
    pull = lax.dot_general(
        scaled.reshape(n_o * pod, k), everything, (((0,), (0,)), ((), ())),
        preferred_element_type=jnp.float32,
    )
    coef = None
    for a in range(n_o):
        term = weight_sum[a] / (weight_sum[a] + 1.0)
        coef = term if coef is None else coef + term
    return (pull - coef[:, None] * centroids) / n_o


def solution(mesh):
    n_o, n_d, n_c = mesh.shape["outer"], mesh.shape["dp"], mesh.shape["cent"]

    def shards(rows, centroids):
        t, d = rows.shape
        k = centroids.shape[0]
        n_all = t * n_o * n_d
        footprint = n_all * d * 2 + n_all * k * 4 * 2
        if footprint <= (24 << 20) and t % n_c == 0 and n_c >= 2 and (n_c & (n_c - 1)) == 0:
            return shards_all(rows, centroids)
        return shards_pod(rows, centroids)

    return jax.shard_map(
        shards,
        mesh=mesh,
        in_specs=(P(("outer", "dp"), None), P(("dp", "cent"), None)),
        out_specs=P(("dp", "cent"), None),
        check_vma=False,
    )
```

```python
import itertools

import jax
import jax.numpy as jnp
from jax import lax
from jax.sharding import PartitionSpec as P


def scores_for(piece, cent_bf, squares):
    product = lax.dot_general(
        piece, cent_bf, (((1,), (1,)), ((), ())), preferred_element_type=jnp.float32
    )
    return 0.5 * (2.0 * product - squares[None, :])


def row_summary(logits):
    local_max = jnp.max(logits, axis=1)
    local_sum = jnp.sum(jnp.exp(logits - local_max[:, None]), axis=1)
    return (local_max, local_sum)


def global_stats(local_max, local_sum):
    row_peak = lax.pmax(local_max, ("dp", "cent"))
    row_mass = lax.psum(local_sum * jnp.exp(local_max - row_peak), ("dp", "cent"))
    return (row_peak, row_mass)


def shards_pod(rows, centroids):
    rows_bf = rows.astype(jnp.bfloat16)
    cent_bf = centroids.astype(jnp.bfloat16)
    squares = jnp.sum(centroids * centroids, axis=1)
    gathered = lax.all_gather(rows_bf, "dp", axis=0, tiled=True)
    logits = scores_for(gathered, cent_bf, squares)
    local_max, local_sum = row_summary(logits)
    row_peak, row_mass = global_stats(local_max, local_sum)
    weights = (jnp.exp(logits - row_peak[:, None]) / row_mass[:, None]).astype(jnp.bfloat16)
    weight_sum = jnp.sum(weights.astype(jnp.float32), axis=0)
    pull = lax.dot_general(
        weights, gathered, (((0,), (0,)), ((), ())), preferred_element_type=jnp.float32
    )
    delta = (pull - weight_sum[:, None] * centroids) / (weight_sum[:, None] + 1.0)
    return lax.psum(delta, "outer") / lax.axis_size("outer")


def shards_all(rows, centroids):
    n_o = lax.axis_size("outer")
    n_d = lax.axis_size("dp")
    n_c = lax.axis_size("cent")
    z = lax.axis_index("outer")
    y = lax.axis_index("dp")
    q = lax.axis_index("cent")
    t, d = rows.shape
    tq = t // n_c
    n_od = n_o * n_d

    rows_bf = rows.astype(jnp.bfloat16)
    cent_bf = centroids.astype(jnp.bfloat16)
    squares = jnp.sum(centroids * centroids, axis=1)

    bits = []
    b = 1
    while b < n_c:
        bits.append(b)
        b *= 2
    xs = [0]
    for bit in reversed(bits):
        xs = xs + [x ^ bit for x in xs]

    mine = lax.dynamic_slice_in_dim(rows_bf, q * tq, tq, 0)
    shifts = list(itertools.product(range(n_o), range(n_d)))
    def pair_of(piece):
        across = [piece]
        for sy in range(1, n_d):
            across.append(lax.ppermute(piece, "dp", [(j, (j + sy) % n_d) for j in range(n_d)]))
        return jnp.stack(across)

    def spread(cur):
        for bit in reversed(bits):
            other = lax.ppermute(cur, "cent", [(i, i ^ bit) for i in range(n_c)])
            cur = jnp.concatenate([cur, other], axis=1)
        return cur

    landed = [mine]
    for sz in range(1, n_o):
        if n_o & (n_o - 1) == 0:
            pairs = [(i, i ^ sz) for i in range(n_o)]
        else:
            pairs = [(i, (i + sz) % n_o) for i in range(n_o)]
        landed.append(lax.ppermute(mine, "outer", pairs))
    def spread_x_first(piece):
        order = list(reversed(bits))
        other = lax.ppermute(piece, "cent", [(i, i ^ order[0]) for i in range(n_c)])
        cur = pair_of(jnp.concatenate([piece, other], axis=0))
        for bit in order[1:]:
            other = lax.ppermute(cur, "cent", [(i, i ^ bit) for i in range(n_c)])
            cur = jnp.concatenate([cur, other], axis=1)
        return cur

    parts = [None] + [
        spread_x_first(piece) if sz in (1, 3) else spread(pair_of(piece))
        for sz, piece in enumerate(landed[1:], start=1)
    ]

    h = q % 2
    half = t // 2
    my_half = lax.dynamic_slice_in_dim(rows_bf, h * half, half, 0)
    own_blocks = [rows_bf]
    for sy in range(1, n_d):
        got = lax.ppermute(my_half, "dp", [(j, (j + sy) % n_d) for j in range(n_d)])
        mate = lax.ppermute(got, "cent", [(i, i ^ 1) for i in range(n_c)])
        own_blocks.append(jnp.concatenate([got, mate], axis=0))
    parts[0] = jnp.stack(own_blocks)

    cur = jnp.zeros((n_o * n_d,) + parts[0].shape[1:], parts[0].dtype)
    for sz in range(n_o):
        pod_of = (z ^ sz) if n_o & (n_o - 1) == 0 else (z - sz) % n_o
        cur = lax.dynamic_update_slice_in_dim(cur, parts[sz], pod_of * n_d, axis=0)
    everything = cur.reshape(n_od * n_c * tq, d)

    logits = scores_for(everything, cent_bf, squares)
    local_max, local_sum = row_summary(logits)

    src_vec = jnp.stack([a * n_d + (y - sy) % n_d for a, sy in shifts])
    hot_k = src_vec[None, :] == jnp.arange(n_od)[:, None]
    jj = jnp.arange(n_c)
    xor_map = q ^ jnp.asarray(xs, jnp.int32)
    hq = n_c // 2
    half_map = ((jj // hq) ^ h) * hq + jj % hq
    maps = []
    for a, sy in shifts:
        own_map = jj if sy == 0 else half_map
        maps.append(jnp.where(a == z, own_map, xor_map))
    c_map = jnp.stack(maps)
    hot_kc = c_map[:, None, :] == jj[None, :, None]

    def to_absolute(v):
        v = v.reshape(n_od, n_c, tq)
        v = jnp.sum(jnp.where(hot_kc[:, :, :, None], v[:, None, :, :], 0.0), axis=2)
        return jnp.sum(jnp.where(hot_k[:, :, None, None], v[None], 0.0), axis=1)

    def to_local(v):
        v = jnp.sum(jnp.where(hot_k[:, :, None, None], v[:, None], 0.0), axis=0)
        v = jnp.sum(jnp.where(hot_kc[:, :, :, None], v[:, :, None, :], 0.0), axis=1)
        return v.reshape(n_od * n_c * tq)

    both = jnp.stack([to_absolute(local_max), to_absolute(local_sum)])
    every = lax.all_gather(both, ("dp", "cent"), axis=0)
    maxes, sums = every[:, 0], every[:, 1]
    peak_abs = jnp.max(maxes, axis=0)
    mass_abs = jnp.sum(sums * jnp.exp(maxes - peak_abs[None]), axis=0)
    row_peak = to_local(peak_abs)
    row_mass = to_local(mass_abs)

    weights = (jnp.exp(logits - row_peak[:, None]) / row_mass[:, None]).astype(jnp.bfloat16)
    k = centroids.shape[0]
    pod = n_d * n_c * tq
    w_pods = weights.reshape(n_o, pod, k).astype(jnp.float32)
    weight_sum = jnp.sum(w_pods, axis=1)
    scaled = (w_pods / (weight_sum[:, None, :] + 1.0)).astype(jnp.bfloat16)
    pull = lax.dot_general(
        scaled.reshape(n_o * pod, k), everything, (((0,), (0,)), ((), ())),
        preferred_element_type=jnp.float32,
    )
    coef = None
    for a in range(n_o):
        term = weight_sum[a] / (weight_sum[a] + 1.0)
        coef = term if coef is None else coef + term
    return (pull - coef[:, None] * centroids) / n_o


def solution(mesh):
    n_o, n_d, n_c = mesh.shape["outer"], mesh.shape["dp"], mesh.shape["cent"]

    def shards(rows, centroids):
        t, d = rows.shape
        k = centroids.shape[0]
        n_all = t * n_o * n_d
        footprint = n_all * d * 2 + n_all * k * 4 * 2
        if footprint <= (24 << 20) and t % n_c == 0 and n_c >= 2 and (n_c & (n_c - 1)) == 0:
            return shards_all(rows, centroids)
        return shards_pod(rows, centroids)

    return jax.shard_map(
        shards,
        mesh=mesh,
        in_specs=(P(("outer", "dp"), None), P(("dp", "cent"), None)),
        out_specs=P(("dp", "cent"), None),
        check_vma=False,
    )
```

```python
import itertools

import jax
import jax.numpy as jnp
from jax import lax
from jax.sharding import PartitionSpec as P


def scores_for(piece, cent_bf, squares):
    product = lax.dot_general(
        piece, cent_bf, (((1,), (1,)), ((), ())), preferred_element_type=jnp.float32
    )
    return 0.5 * (2.0 * product - squares[None, :])


def row_summary(logits):
    local_max = jnp.max(logits, axis=1)
    local_sum = jnp.sum(jnp.exp(logits - local_max[:, None]), axis=1)
    return (local_max, local_sum)


def global_stats(local_max, local_sum):
    row_peak = lax.pmax(local_max, ("dp", "cent"))
    row_mass = lax.psum(local_sum * jnp.exp(local_max - row_peak), ("dp", "cent"))
    return (row_peak, row_mass)


def shards_pod(rows, centroids):
    rows_bf = rows.astype(jnp.bfloat16)
    cent_bf = centroids.astype(jnp.bfloat16)
    squares = jnp.sum(centroids * centroids, axis=1)
    gathered = lax.all_gather(rows_bf, "dp", axis=0, tiled=True)
    logits = scores_for(gathered, cent_bf, squares)
    local_max, local_sum = row_summary(logits)
    row_peak, row_mass = global_stats(local_max, local_sum)
    weights = (jnp.exp(logits - row_peak[:, None]) / row_mass[:, None]).astype(jnp.bfloat16)
    weight_sum = jnp.sum(weights.astype(jnp.float32), axis=0)
    pull = lax.dot_general(
        weights, gathered, (((0,), (0,)), ((), ())), preferred_element_type=jnp.float32
    )
    delta = (pull - weight_sum[:, None] * centroids) / (weight_sum[:, None] + 1.0)
    return lax.psum(delta, "outer") / lax.axis_size("outer")


def shards_all(rows, centroids):
    n_o = lax.axis_size("outer")
    n_d = lax.axis_size("dp")
    n_c = lax.axis_size("cent")
    z = lax.axis_index("outer")
    y = lax.axis_index("dp")
    q = lax.axis_index("cent")
    t, d = rows.shape
    tq = t // n_c
    n_od = n_o * n_d

    rows_bf = rows.astype(jnp.bfloat16)
    cent_bf = centroids.astype(jnp.bfloat16)
    squares = jnp.sum(centroids * centroids, axis=1)

    bits = []
    b = 1
    while b < n_c:
        bits.append(b)
        b *= 2
    xs = [0]
    for bit in reversed(bits):
        xs = xs + [x ^ bit for x in xs]

    mine = lax.dynamic_slice_in_dim(rows_bf, q * tq, tq, 0)
    shifts = list(itertools.product(range(n_o), range(n_d)))
    def pair_of(piece):
        across = [piece]
        for sy in range(1, n_d):
            across.append(lax.ppermute(piece, "dp", [(j, (j + sy) % n_d) for j in range(n_d)]))
        return jnp.stack(across)

    def spread(cur):
        for bit in reversed(bits):
            other = lax.ppermute(cur, "cent", [(i, i ^ bit) for i in range(n_c)])
            cur = jnp.concatenate([cur, other], axis=1)
        return cur

    landed = [mine]
    for sz in range(1, n_o):
        if n_o & (n_o - 1) == 0:
            pairs = [(i, i ^ sz) for i in range(n_o)]
        else:
            pairs = [(i, (i + sz) % n_o) for i in range(n_o)]
        landed.append(lax.ppermute(mine, "outer", pairs))
    def spread_x_first(piece):
        order = list(reversed(bits))
        other = lax.ppermute(piece, "cent", [(i, i ^ order[0]) for i in range(n_c)])
        cur = pair_of(jnp.concatenate([piece, other], axis=0))
        for bit in order[1:]:
            other = lax.ppermute(cur, "cent", [(i, i ^ bit) for i in range(n_c)])
            cur = jnp.concatenate([cur, other], axis=1)
        return cur

    parts = [None] + [
        spread_x_first(piece)
        for sz, piece in enumerate(landed[1:], start=1)
    ]

    h = q % 2
    half = t // 2
    my_half = lax.dynamic_slice_in_dim(rows_bf, h * half, half, 0)
    own_blocks = [rows_bf]
    for sy in range(1, n_d):
        got = lax.ppermute(my_half, "dp", [(j, (j + sy) % n_d) for j in range(n_d)])
        mate = lax.ppermute(got, "cent", [(i, i ^ 1) for i in range(n_c)])
        own_blocks.append(jnp.concatenate([got, mate], axis=0))
    parts[0] = jnp.stack(own_blocks)

    cur = jnp.zeros((n_o * n_d,) + parts[0].shape[1:], parts[0].dtype)
    for sz in range(n_o):
        pod_of = (z ^ sz) if n_o & (n_o - 1) == 0 else (z - sz) % n_o
        cur = lax.dynamic_update_slice_in_dim(cur, parts[sz], pod_of * n_d, axis=0)
    everything = cur.reshape(n_od * n_c * tq, d)

    logits = scores_for(everything, cent_bf, squares)
    local_max, local_sum = row_summary(logits)

    src_vec = jnp.stack([a * n_d + (y - sy) % n_d for a, sy in shifts])
    hot_k = src_vec[None, :] == jnp.arange(n_od)[:, None]
    jj = jnp.arange(n_c)
    xor_map = q ^ jnp.asarray(xs, jnp.int32)
    hq = n_c // 2
    half_map = ((jj // hq) ^ h) * hq + jj % hq
    maps = []
    for a, sy in shifts:
        own_map = jj if sy == 0 else half_map
        maps.append(jnp.where(a == z, own_map, xor_map))
    c_map = jnp.stack(maps)
    hot_kc = c_map[:, None, :] == jj[None, :, None]

    def to_absolute(v):
        v = v.reshape(n_od, n_c, tq)
        v = jnp.sum(jnp.where(hot_kc[:, :, :, None], v[:, None, :, :], 0.0), axis=2)
        return jnp.sum(jnp.where(hot_k[:, :, None, None], v[None], 0.0), axis=1)

    def to_local(v):
        v = jnp.sum(jnp.where(hot_k[:, :, None, None], v[:, None], 0.0), axis=0)
        v = jnp.sum(jnp.where(hot_kc[:, :, :, None], v[:, :, None, :], 0.0), axis=1)
        return v.reshape(n_od * n_c * tq)

    both = jnp.stack([to_absolute(local_max), to_absolute(local_sum)])
    every = lax.all_gather(both, ("dp", "cent"), axis=0)
    maxes, sums = every[:, 0], every[:, 1]
    peak_abs = jnp.max(maxes, axis=0)
    mass_abs = jnp.sum(sums * jnp.exp(maxes - peak_abs[None]), axis=0)
    row_peak = to_local(peak_abs)
    row_mass = to_local(mass_abs)

    weights = (jnp.exp(logits - row_peak[:, None]) / row_mass[:, None]).astype(jnp.bfloat16)
    k = centroids.shape[0]
    pod = n_d * n_c * tq
    w_pods = weights.reshape(n_o, pod, k).astype(jnp.float32)
    weight_sum = jnp.sum(w_pods, axis=1)
    scaled = (w_pods / (weight_sum[:, None, :] + 1.0)).astype(jnp.bfloat16)
    pull = lax.dot_general(
        scaled.reshape(n_o * pod, k), everything, (((0,), (0,)), ((), ())),
        preferred_element_type=jnp.float32,
    )
    coef = None
    for a in range(n_o):
        term = weight_sum[a] / (weight_sum[a] + 1.0)
        coef = term if coef is None else coef + term
    return (pull - coef[:, None] * centroids) / n_o


def solution(mesh):
    n_o, n_d, n_c = mesh.shape["outer"], mesh.shape["dp"], mesh.shape["cent"]

    def shards(rows, centroids):
        t, d = rows.shape
        k = centroids.shape[0]
        n_all = t * n_o * n_d
        footprint = n_all * d * 2 + n_all * k * 4 * 2
        if footprint <= (24 << 20) and t % n_c == 0 and n_c >= 2 and (n_c & (n_c - 1)) == 0:
            return shards_all(rows, centroids)
        return shards_pod(rows, centroids)

    return jax.shard_map(
        shards,
        mesh=mesh,
        in_specs=(P(("outer", "dp"), None), P(("dp", "cent"), None)),
        out_specs=P(("dp", "cent"), None),
        check_vma=False,
    )
```

```python
import itertools

import jax
import jax.numpy as jnp
from jax import lax
from jax.sharding import PartitionSpec as P


def scores_for(piece, cent_bf, squares):
    product = lax.dot_general(
        piece, cent_bf, (((1,), (1,)), ((), ())), preferred_element_type=jnp.float32
    )
    return 0.5 * (2.0 * product - squares[None, :])


def row_summary(logits):
    local_max = jnp.max(logits, axis=1)
    local_sum = jnp.sum(jnp.exp(logits - local_max[:, None]), axis=1)
    return (local_max, local_sum)


def global_stats(local_max, local_sum):
    row_peak = lax.pmax(local_max, ("dp", "cent"))
    row_mass = lax.psum(local_sum * jnp.exp(local_max - row_peak), ("dp", "cent"))
    return (row_peak, row_mass)


def shards_pod(rows, centroids):
    rows_bf = rows.astype(jnp.bfloat16)
    cent_bf = centroids.astype(jnp.bfloat16)
    squares = jnp.sum(centroids * centroids, axis=1)
    gathered = lax.all_gather(rows_bf, "dp", axis=0, tiled=True)
    logits = scores_for(gathered, cent_bf, squares)
    local_max, local_sum = row_summary(logits)
    row_peak, row_mass = global_stats(local_max, local_sum)
    weights = (jnp.exp(logits - row_peak[:, None]) / row_mass[:, None]).astype(jnp.bfloat16)
    weight_sum = jnp.sum(weights.astype(jnp.float32), axis=0)
    pull = lax.dot_general(
        weights, gathered, (((0,), (0,)), ((), ())), preferred_element_type=jnp.float32
    )
    delta = (pull - weight_sum[:, None] * centroids) / (weight_sum[:, None] + 1.0)
    return lax.psum(delta, "outer") / lax.axis_size("outer")


def shards_all(rows, centroids):
    n_o = lax.axis_size("outer")
    n_d = lax.axis_size("dp")
    n_c = lax.axis_size("cent")
    z = lax.axis_index("outer")
    y = lax.axis_index("dp")
    q = lax.axis_index("cent")
    t, d = rows.shape
    tq = t // n_c
    n_od = n_o * n_d

    rows_bf = rows.astype(jnp.bfloat16)
    cent_bf = centroids.astype(jnp.bfloat16)
    squares = jnp.sum(centroids * centroids, axis=1)

    bits = []
    b = 1
    while b < n_c:
        bits.append(b)
        b *= 2
    xs = [0]
    for bit in reversed(bits):
        xs = xs + [x ^ bit for x in xs]

    mine = lax.dynamic_slice_in_dim(rows, q * tq, tq, 0).astype(jnp.bfloat16)
    shifts = list(itertools.product(range(n_o), range(n_d)))
    def pair_of(piece):
        across = [piece]
        for sy in range(1, n_d):
            across.append(lax.ppermute(piece, "dp", [(j, (j + sy) % n_d) for j in range(n_d)]))
        return jnp.stack(across)

    def spread(cur):
        for bit in reversed(bits):
            other = lax.ppermute(cur, "cent", [(i, i ^ bit) for i in range(n_c)])
            cur = jnp.concatenate([cur, other], axis=1)
        return cur

    landed = [mine]
    for sz in range(1, n_o):
        if n_o & (n_o - 1) == 0:
            pairs = [(i, i ^ sz) for i in range(n_o)]
        else:
            pairs = [(i, (i + sz) % n_o) for i in range(n_o)]
        landed.append(lax.ppermute(mine, "outer", pairs))
    def spread_x_first(piece):
        order = list(reversed(bits))
        other = lax.ppermute(piece, "cent", [(i, i ^ order[0]) for i in range(n_c)])
        cur = pair_of(jnp.concatenate([piece, other], axis=0))
        for bit in order[1:]:
            other = lax.ppermute(cur, "cent", [(i, i ^ bit) for i in range(n_c)])
            cur = jnp.concatenate([cur, other], axis=1)
        return cur

    parts = [None] + [
        spread_x_first(piece) if sz in (1, 3) else spread(pair_of(piece))
        for sz, piece in enumerate(landed[1:], start=1)
    ]

    h = q % 2
    half = t // 2
    my_half = lax.dynamic_slice_in_dim(rows, h * half, half, 0).astype(jnp.bfloat16)
    own_blocks = [rows_bf]
    for sy in range(1, n_d):
        got = lax.ppermute(my_half, "dp", [(j, (j + sy) % n_d) for j in range(n_d)])
        mate = lax.ppermute(got, "cent", [(i, i ^ 1) for i in range(n_c)])
        own_blocks.append(jnp.concatenate([got, mate], axis=0))
    parts[0] = jnp.stack(own_blocks)

    cur = jnp.zeros((n_o * n_d,) + parts[0].shape[1:], parts[0].dtype)
    for sz in range(n_o):
        pod_of = (z ^ sz) if n_o & (n_o - 1) == 0 else (z - sz) % n_o
        cur = lax.dynamic_update_slice_in_dim(cur, parts[sz], pod_of * n_d, axis=0)
    everything = cur.reshape(n_od * n_c * tq, d)

    logits = scores_for(everything, cent_bf, squares)
    local_max, local_sum = row_summary(logits)

    src_vec = jnp.stack([a * n_d + (y - sy) % n_d for a, sy in shifts])
    hot_k = src_vec[None, :] == jnp.arange(n_od)[:, None]
    jj = jnp.arange(n_c)
    xor_map = q ^ jnp.asarray(xs, jnp.int32)
    hq = n_c // 2
    half_map = ((jj // hq) ^ h) * hq + jj % hq
    maps = []
    for a, sy in shifts:
        own_map = jj if sy == 0 else half_map
        maps.append(jnp.where(a == z, own_map, xor_map))
    c_map = jnp.stack(maps)
    hot_kc = c_map[:, None, :] == jj[None, :, None]

    def to_absolute(v):
        v = v.reshape(n_od, n_c, tq)
        v = jnp.sum(jnp.where(hot_kc[:, :, :, None], v[:, None, :, :], 0.0), axis=2)
        return jnp.sum(jnp.where(hot_k[:, :, None, None], v[None], 0.0), axis=1)

    def to_local(v):
        v = jnp.sum(jnp.where(hot_k[:, :, None, None], v[:, None], 0.0), axis=0)
        v = jnp.sum(jnp.where(hot_kc[:, :, :, None], v[:, :, None, :], 0.0), axis=1)
        return v.reshape(n_od * n_c * tq)

    both = jnp.stack([to_absolute(local_max), to_absolute(local_sum)])
    every = lax.all_gather(both, ("dp", "cent"), axis=0)
    maxes, sums = every[:, 0], every[:, 1]
    peak_abs = jnp.max(maxes, axis=0)
    mass_abs = jnp.sum(sums * jnp.exp(maxes - peak_abs[None]), axis=0)
    row_peak = to_local(peak_abs)
    row_mass = to_local(mass_abs)

    weights = (jnp.exp(logits - row_peak[:, None]) / row_mass[:, None]).astype(jnp.bfloat16)
    k = centroids.shape[0]
    pod = n_d * n_c * tq
    w_pods = weights.reshape(n_o, pod, k).astype(jnp.float32)
    weight_sum = jnp.sum(w_pods, axis=1)
    scaled = (w_pods / (weight_sum[:, None, :] + 1.0)).astype(jnp.bfloat16)
    pull = lax.dot_general(
        scaled.reshape(n_o * pod, k), everything, (((0,), (0,)), ((), ())),
        preferred_element_type=jnp.float32,
    )
    coef = None
    for a in range(n_o):
        term = weight_sum[a] / (weight_sum[a] + 1.0)
        coef = term if coef is None else coef + term
    return (pull - coef[:, None] * centroids) / n_o


def solution(mesh):
    n_o, n_d, n_c = mesh.shape["outer"], mesh.shape["dp"], mesh.shape["cent"]

    def shards(rows, centroids):
        t, d = rows.shape
        k = centroids.shape[0]
        n_all = t * n_o * n_d
        footprint = n_all * d * 2 + n_all * k * 4 * 2
        if footprint <= (24 << 20) and t % n_c == 0 and n_c >= 2 and (n_c & (n_c - 1)) == 0:
            return shards_all(rows, centroids)
        return shards_pod(rows, centroids)

    return jax.shard_map(
        shards,
        mesh=mesh,
        in_specs=(P(("outer", "dp"), None), P(("dp", "cent"), None)),
        out_specs=P(("dp", "cent"), None),
        check_vma=False,
    )
```

```python
import itertools

import jax
import jax.numpy as jnp
from jax import lax
from jax.sharding import PartitionSpec as P


def scores_for(piece, cent_bf, squares):
    product = lax.dot_general(
        piece, cent_bf, (((1,), (1,)), ((), ())), preferred_element_type=jnp.float32
    )
    return 0.5 * (2.0 * product - squares[None, :])


def row_summary(logits):
    local_max = jnp.max(logits, axis=1)
    local_sum = jnp.sum(jnp.exp(logits - local_max[:, None]), axis=1)
    return (local_max, local_sum)


def global_stats(local_max, local_sum):
    row_peak = lax.pmax(local_max, ("dp", "cent"))
    row_mass = lax.psum(local_sum * jnp.exp(local_max - row_peak), ("dp", "cent"))
    return (row_peak, row_mass)


def shards_pod(rows, centroids):
    rows_bf = rows.astype(jnp.bfloat16)
    cent_bf = centroids.astype(jnp.bfloat16)
    squares = jnp.sum(centroids * centroids, axis=1)
    gathered = lax.all_gather(rows_bf, "dp", axis=0, tiled=True)
    logits = scores_for(gathered, cent_bf, squares)
    local_max, local_sum = row_summary(logits)
    row_peak, row_mass = global_stats(local_max, local_sum)
    weights = (jnp.exp(logits - row_peak[:, None]) / row_mass[:, None]).astype(jnp.bfloat16)
    weight_sum = jnp.sum(weights.astype(jnp.float32), axis=0)
    pull = lax.dot_general(
        weights, gathered, (((0,), (0,)), ((), ())), preferred_element_type=jnp.float32
    )
    delta = (pull - weight_sum[:, None] * centroids) / (weight_sum[:, None] + 1.0)
    return lax.psum(delta, "outer") / lax.axis_size("outer")


def shards_all(rows, centroids):
    n_o = lax.axis_size("outer")
    n_d = lax.axis_size("dp")
    n_c = lax.axis_size("cent")
    z = lax.axis_index("outer")
    y = lax.axis_index("dp")
    q = lax.axis_index("cent")
    t, d = rows.shape
    tq = t // n_c
    n_od = n_o * n_d

    rows_bf = rows.astype(jnp.bfloat16)
    cent_bf = centroids.astype(jnp.bfloat16)
    squares = jnp.sum(centroids * centroids, axis=1)

    bits = []
    b = 1
    while b < n_c:
        bits.append(b)
        b *= 2
    xs = [0]
    for bit in reversed(bits):
        xs = xs + [x ^ bit for x in xs]

    mine = lax.dynamic_slice_in_dim(rows, q * tq, tq, 0).astype(jnp.bfloat16)
    shifts = list(itertools.product(range(n_o), range(n_d)))
    def pair_of(piece):
        across = [piece]
        for sy in range(1, n_d):
            across.append(lax.ppermute(piece, "dp", [(j, (j + sy) % n_d) for j in range(n_d)]))
        return jnp.stack(across)

    def spread(cur):
        for bit in reversed(bits):
            other = lax.ppermute(cur, "cent", [(i, i ^ bit) for i in range(n_c)])
            cur = jnp.concatenate([cur, other], axis=1)
        return cur

    landed = [mine]
    for sz in range(1, n_o):
        if n_o & (n_o - 1) == 0:
            pairs = [(i, i ^ sz) for i in range(n_o)]
        else:
            pairs = [(i, (i + sz) % n_o) for i in range(n_o)]
        landed.append(lax.ppermute(mine, "outer", pairs))
    def spread_x_first(piece):
        order = list(reversed(bits))
        other = lax.ppermute(piece, "cent", [(i, i ^ order[0]) for i in range(n_c)])
        cur = pair_of(jnp.concatenate([piece, other], axis=0))
        for bit in order[1:]:
            other = lax.ppermute(cur, "cent", [(i, i ^ bit) for i in range(n_c)])
            cur = jnp.concatenate([cur, other], axis=1)
        return cur

    parts = [None] + [
        spread_x_first(piece) if sz in (1, 3) else spread(pair_of(piece))
        for sz, piece in enumerate(landed[1:], start=1)
    ]

    parts[0] = spread(pair_of(mine))

    cur = jnp.zeros((n_o * n_d,) + parts[0].shape[1:], parts[0].dtype)
    for sz in range(n_o):
        pod_of = (z ^ sz) if n_o & (n_o - 1) == 0 else (z - sz) % n_o
        cur = lax.dynamic_update_slice_in_dim(cur, parts[sz], pod_of * n_d, axis=0)
    everything = cur.reshape(n_od * n_c * tq, d)

    logits = scores_for(everything, cent_bf, squares)
    local_max, local_sum = row_summary(logits)

    src_vec = jnp.stack([a * n_d + (y - sy) % n_d for a, sy in shifts])
    hot_k = src_vec[None, :] == jnp.arange(n_od)[:, None]
    jj = jnp.arange(n_c)
    xor_map = q ^ jnp.asarray(xs, jnp.int32)
    c_map = jnp.broadcast_to(xor_map[None, :], (n_od, n_c))
    hot_kc = c_map[:, None, :] == jj[None, :, None]

    def to_absolute(v):
        v = v.reshape(n_od, n_c, tq)
        v = jnp.sum(jnp.where(hot_kc[:, :, :, None], v[:, None, :, :], 0.0), axis=2)
        return jnp.sum(jnp.where(hot_k[:, :, None, None], v[None], 0.0), axis=1)

    def to_local(v):
        v = jnp.sum(jnp.where(hot_k[:, :, None, None], v[:, None], 0.0), axis=0)
        v = jnp.sum(jnp.where(hot_kc[:, :, :, None], v[:, :, None, :], 0.0), axis=1)
        return v.reshape(n_od * n_c * tq)

    both = jnp.stack([to_absolute(local_max), to_absolute(local_sum)])
    every = lax.all_gather(both, ("dp", "cent"), axis=0)
    maxes, sums = every[:, 0], every[:, 1]
    peak_abs = jnp.max(maxes, axis=0)
    mass_abs = jnp.sum(sums * jnp.exp(maxes - peak_abs[None]), axis=0)
    row_peak = to_local(peak_abs)
    row_mass = to_local(mass_abs)

    weights = (jnp.exp(logits - row_peak[:, None]) / row_mass[:, None]).astype(jnp.bfloat16)
    k = centroids.shape[0]
    pod = n_d * n_c * tq
    w_pods = weights.reshape(n_o, pod, k).astype(jnp.float32)
    weight_sum = jnp.sum(w_pods, axis=1)
    scaled = (w_pods / (weight_sum[:, None, :] + 1.0)).astype(jnp.bfloat16)
    pull = lax.dot_general(
        scaled.reshape(n_o * pod, k), everything, (((0,), (0,)), ((), ())),
        preferred_element_type=jnp.float32,
    )
    coef = None
    for a in range(n_o):
        term = weight_sum[a] / (weight_sum[a] + 1.0)
        coef = term if coef is None else coef + term
    return (pull - coef[:, None] * centroids) / n_o


def solution(mesh):
    n_o, n_d, n_c = mesh.shape["outer"], mesh.shape["dp"], mesh.shape["cent"]

    def shards(rows, centroids):
        t, d = rows.shape
        k = centroids.shape[0]
        n_all = t * n_o * n_d
        footprint = n_all * d * 2 + n_all * k * 4 * 2
        if footprint <= (24 << 20) and t % n_c == 0 and n_c >= 2 and (n_c & (n_c - 1)) == 0:
            return shards_all(rows, centroids)
        return shards_pod(rows, centroids)

    return jax.shard_map(
        shards,
        mesh=mesh,
        in_specs=(P(("outer", "dp"), None), P(("dp", "cent"), None)),
        out_specs=P(("dp", "cent"), None),
        check_vma=False,
    )
```

```python
import itertools

import jax
import jax.numpy as jnp
from jax import lax
from jax.sharding import PartitionSpec as P


def scores_for(piece, cent_bf, squares):
    product = lax.dot_general(
        piece, cent_bf, (((1,), (1,)), ((), ())), preferred_element_type=jnp.float32
    )
    return 0.5 * (2.0 * product - squares[None, :])


def row_summary(logits):
    local_max = jnp.max(logits, axis=1)
    local_sum = jnp.sum(jnp.exp(logits - local_max[:, None]), axis=1)
    return (local_max, local_sum)


def global_stats(local_max, local_sum):
    row_peak = lax.pmax(local_max, ("dp", "cent"))
    row_mass = lax.psum(local_sum * jnp.exp(local_max - row_peak), ("dp", "cent"))
    return (row_peak, row_mass)


def shards_pod(rows, centroids):
    rows_bf = rows.astype(jnp.bfloat16)
    cent_bf = centroids.astype(jnp.bfloat16)
    squares = jnp.sum(centroids * centroids, axis=1)
    gathered = lax.all_gather(rows_bf, "dp", axis=0, tiled=True)
    logits = scores_for(gathered, cent_bf, squares)
    local_max, local_sum = row_summary(logits)
    row_peak, row_mass = global_stats(local_max, local_sum)
    weights = (jnp.exp(logits - row_peak[:, None]) / row_mass[:, None]).astype(jnp.bfloat16)
    weight_sum = jnp.sum(weights.astype(jnp.float32), axis=0)
    pull = lax.dot_general(
        weights, gathered, (((0,), (0,)), ((), ())), preferred_element_type=jnp.float32
    )
    delta = (pull - weight_sum[:, None] * centroids) / (weight_sum[:, None] + 1.0)
    return lax.psum(delta, "outer") / lax.axis_size("outer")


def shards_all(rows, centroids):
    n_o = lax.axis_size("outer")
    n_d = lax.axis_size("dp")
    n_c = lax.axis_size("cent")
    z = lax.axis_index("outer")
    y = lax.axis_index("dp")
    q = lax.axis_index("cent")
    t, d = rows.shape
    tq = t // n_c
    n_od = n_o * n_d

    rows_bf = rows.astype(jnp.bfloat16)
    cent_bf = centroids.astype(jnp.bfloat16)
    squares = jnp.sum(centroids * centroids, axis=1)

    bits = []
    b = 1
    while b < n_c:
        bits.append(b)
        b *= 2
    xs = [0]
    for bit in reversed(bits):
        xs = xs + [x ^ bit for x in xs]

    mine = lax.dynamic_slice_in_dim(rows, q * tq, tq, 0).astype(jnp.bfloat16)
    shifts = list(itertools.product(range(n_o), range(n_d)))
    def pair_of(piece):
        across = [piece]
        for sy in range(1, n_d):
            across.append(lax.ppermute(piece, "dp", [(j, (j + sy) % n_d) for j in range(n_d)]))
        return jnp.stack(across)

    def spread(cur):
        for bit in reversed(bits):
            other = lax.ppermute(cur, "cent", [(i, i ^ bit) for i in range(n_c)])
            cur = jnp.concatenate([cur, other], axis=1)
        return cur

    landed = [mine]
    for sz in range(1, n_o):
        if n_o & (n_o - 1) == 0:
            pairs = [(i, i ^ sz) for i in range(n_o)]
        else:
            pairs = [(i, (i + sz) % n_o) for i in range(n_o)]
        landed.append(lax.ppermute(mine, "outer", pairs))
    def spread_x_first(piece):
        order = list(reversed(bits))
        other = lax.ppermute(piece, "cent", [(i, i ^ order[0]) for i in range(n_c)])
        cur = pair_of(jnp.concatenate([piece, other], axis=0))
        for bit in order[1:]:
            other = lax.ppermute(cur, "cent", [(i, i ^ bit) for i in range(n_c)])
            cur = jnp.concatenate([cur, other], axis=1)
        return cur

    parts = [None] + [
        spread_x_first(piece) if sz in (1, 3) else spread(pair_of(piece))
        for sz, piece in enumerate(landed[1:], start=1)
    ]

    parts[0] = spread(pair_of(mine))

    cur = jnp.zeros((n_o * n_d,) + parts[0].shape[1:], parts[0].dtype)
    for sz in range(n_o):
        pod_of = (z ^ sz) if n_o & (n_o - 1) == 0 else (z - sz) % n_o
        cur = lax.dynamic_update_slice_in_dim(cur, parts[sz], pod_of * n_d, axis=0)
    everything = cur.reshape(n_od * n_c * tq, d)

    logits = scores_for(everything, cent_bf, squares)
    local_max, local_sum = row_summary(logits)

    src_vec = jnp.stack([a * n_d + (y - sy) % n_d for a, sy in shifts])
    hot_k = src_vec[None, :] == jnp.arange(n_od)[:, None]
    jj = jnp.arange(n_c)
    xor_map = q ^ jnp.asarray(xs, jnp.int32)
    c_map = jnp.broadcast_to(xor_map[None, :], (n_od, n_c))
    hot_kc = c_map[:, None, :] == jj[None, :, None]

    def to_absolute(v):
        v = v.reshape(n_od, n_c, tq)
        v = jnp.sum(jnp.where(hot_kc[:, :, :, None], v[:, None, :, :], 0.0), axis=2)
        return jnp.sum(jnp.where(hot_k[:, :, None, None], v[None], 0.0), axis=1)

    def to_local(v):
        v = jnp.sum(jnp.where(hot_k[:, :, None, None], v[:, None], 0.0), axis=0)
        v = jnp.sum(jnp.where(hot_kc[:, :, :, None], v[:, :, None, :], 0.0), axis=1)
        return v.reshape(n_od * n_c * tq)

    peak_abs = to_absolute(local_max)
    mass_abs = to_absolute(local_sum)
    if n_d & (n_d - 1) == 0:
        rounds = [("cent", bit, n_c) for bit in bits]
        bd = 1
        while bd < n_d:
            rounds.append(("dp", bd, n_d))
            bd *= 2
        for axis, bit, n in rounds:
            other = lax.ppermute(jnp.stack([peak_abs, mass_abs]), axis, [(i, i ^ bit) for i in range(n)])
            top = jnp.maximum(peak_abs, other[0])
            mass_abs = mass_abs * jnp.exp(peak_abs - top) + other[1] * jnp.exp(other[0] - top)
            peak_abs = top
    else:
        both = jnp.stack([peak_abs, mass_abs])
        every = lax.all_gather(both, ("dp", "cent"), axis=0)
        maxes, sums = every[:, 0], every[:, 1]
        peak_abs = jnp.max(maxes, axis=0)
        mass_abs = jnp.sum(sums * jnp.exp(maxes - peak_abs[None]), axis=0)
    row_peak = to_local(peak_abs)
    row_mass = to_local(mass_abs)

    weights = (jnp.exp(logits - row_peak[:, None]) / row_mass[:, None]).astype(jnp.bfloat16)
    k = centroids.shape[0]
    pod = n_d * n_c * tq
    w_pods = weights.reshape(n_o, pod, k).astype(jnp.float32)
    weight_sum = jnp.sum(w_pods, axis=1)
    scaled = (w_pods / (weight_sum[:, None, :] + 1.0)).astype(jnp.bfloat16)
    pull = lax.dot_general(
        scaled.reshape(n_o * pod, k), everything, (((0,), (0,)), ((), ())),
        preferred_element_type=jnp.float32,
    )
    coef = None
    for a in range(n_o):
        term = weight_sum[a] / (weight_sum[a] + 1.0)
        coef = term if coef is None else coef + term
    return (pull - coef[:, None] * centroids) / n_o


def solution(mesh):
    n_o, n_d, n_c = mesh.shape["outer"], mesh.shape["dp"], mesh.shape["cent"]

    def shards(rows, centroids):
        t, d = rows.shape
        k = centroids.shape[0]
        n_all = t * n_o * n_d
        footprint = n_all * d * 2 + n_all * k * 4 * 2
        if footprint <= (24 << 20) and t % n_c == 0 and n_c >= 2 and (n_c & (n_c - 1)) == 0:
            return shards_all(rows, centroids)
        return shards_pod(rows, centroids)

    return jax.shard_map(
        shards,
        mesh=mesh,
        in_specs=(P(("outer", "dp"), None), P(("dp", "cent"), None)),
        out_specs=P(("dp", "cent"), None),
        check_vma=False,
    )
```

```python
import itertools

import jax
import jax.numpy as jnp
from jax import lax
from jax.sharding import PartitionSpec as P


def scores_for(piece, cent_bf, squares):
    product = lax.dot_general(
        piece, cent_bf, (((1,), (1,)), ((), ())), preferred_element_type=jnp.float32
    )
    return 0.5 * (2.0 * product - squares[None, :])


def row_summary(logits):
    local_max = jnp.max(logits, axis=1)
    local_sum = jnp.sum(jnp.exp(logits - local_max[:, None]), axis=1)
    return (local_max, local_sum)


def global_stats(local_max, local_sum):
    row_peak = lax.pmax(local_max, ("dp", "cent"))
    row_mass = lax.psum(local_sum * jnp.exp(local_max - row_peak), ("dp", "cent"))
    return (row_peak, row_mass)


def shards_pod(rows, centroids):
    rows_bf = rows.astype(jnp.bfloat16)
    cent_bf = centroids.astype(jnp.bfloat16)
    squares = jnp.sum(centroids * centroids, axis=1)
    gathered = lax.all_gather(rows_bf, "dp", axis=0, tiled=True)
    logits = scores_for(gathered, cent_bf, squares)
    local_max, local_sum = row_summary(logits)
    row_peak, row_mass = global_stats(local_max, local_sum)
    weights = (jnp.exp(logits - row_peak[:, None]) / row_mass[:, None]).astype(jnp.bfloat16)
    weight_sum = jnp.sum(weights.astype(jnp.float32), axis=0)
    pull = lax.dot_general(
        weights, gathered, (((0,), (0,)), ((), ())), preferred_element_type=jnp.float32
    )
    delta = (pull - weight_sum[:, None] * centroids) / (weight_sum[:, None] + 1.0)
    return lax.psum(delta, "outer") / lax.axis_size("outer")


def shards_all(rows, centroids):
    n_o = lax.axis_size("outer")
    n_d = lax.axis_size("dp")
    n_c = lax.axis_size("cent")
    z = lax.axis_index("outer")
    y = lax.axis_index("dp")
    q = lax.axis_index("cent")
    t, d = rows.shape
    tq = t // n_c
    n_od = n_o * n_d

    rows_bf = rows.astype(jnp.bfloat16)
    cent_bf = centroids.astype(jnp.bfloat16)
    squares = jnp.sum(centroids * centroids, axis=1)

    bits = []
    b = 1
    while b < n_c:
        bits.append(b)
        b *= 2
    xs = [0]
    for bit in reversed(bits):
        xs = xs + [x ^ bit for x in xs]

    mine = lax.dynamic_slice_in_dim(rows, q * tq, tq, 0).astype(jnp.bfloat16)
    shifts = list(itertools.product(range(n_o), range(n_d)))
    def pair_of(piece):
        across = [piece]
        for sy in range(1, n_d):
            across.append(lax.ppermute(piece, "dp", [(j, (j + sy) % n_d) for j in range(n_d)]))
        return jnp.stack(across)

    def spread(cur):
        for bit in reversed(bits):
            other = lax.ppermute(cur, "cent", [(i, i ^ bit) for i in range(n_c)])
            cur = jnp.concatenate([cur, other], axis=1)
        return cur

    landed = [mine]
    for sz in range(1, n_o):
        if n_o & (n_o - 1) == 0:
            pairs = [(i, i ^ sz) for i in range(n_o)]
        else:
            pairs = [(i, (i + sz) % n_o) for i in range(n_o)]
        landed.append(lax.ppermute(mine, "outer", pairs))
    def spread_x_first(piece):
        order = list(reversed(bits))
        other = lax.ppermute(piece, "cent", [(i, i ^ order[0]) for i in range(n_c)])
        cur = pair_of(jnp.concatenate([piece, other], axis=0))
        for bit in order[1:]:
            other = lax.ppermute(cur, "cent", [(i, i ^ bit) for i in range(n_c)])
            cur = jnp.concatenate([cur, other], axis=1)
        return cur

    parts = [None] + [
        spread_x_first(piece) if sz == 1 else spread(pair_of(piece))
        for sz, piece in enumerate(landed[1:], start=1)
    ]

    order = list(reversed(bits))
    own = lax.dynamic_slice_in_dim(rows, (q ^ order[0]) * tq, tq, 0).astype(jnp.bfloat16)
    own = pair_of(jnp.concatenate([mine, own], axis=0))
    for bit in order[1:]:
        other = lax.ppermute(own, "cent", [(i, i ^ bit) for i in range(n_c)])
        own = jnp.concatenate([own, other], axis=1)
    parts[0] = own

    cur = jnp.zeros((n_o * n_d,) + parts[0].shape[1:], parts[0].dtype)
    for sz in range(n_o):
        pod_of = (z ^ sz) if n_o & (n_o - 1) == 0 else (z - sz) % n_o
        cur = lax.dynamic_update_slice_in_dim(cur, parts[sz], pod_of * n_d, axis=0)
    everything = cur.reshape(n_od * n_c * tq, d)

    logits = scores_for(everything, cent_bf, squares)
    local_max, local_sum = row_summary(logits)

    src_vec = jnp.stack([a * n_d + (y - sy) % n_d for a, sy in shifts])
    hot_k = src_vec[None, :] == jnp.arange(n_od)[:, None]
    jj = jnp.arange(n_c)
    xor_map = q ^ jnp.asarray(xs, jnp.int32)
    c_map = jnp.broadcast_to(xor_map[None, :], (n_od, n_c))
    hot_kc = c_map[:, None, :] == jj[None, :, None]

    def to_absolute(v):
        v = v.reshape(n_od, n_c, tq)
        v = jnp.sum(jnp.where(hot_kc[:, :, :, None], v[:, None, :, :], 0.0), axis=2)
        return jnp.sum(jnp.where(hot_k[:, :, None, None], v[None], 0.0), axis=1)

    def to_local(v):
        v = jnp.sum(jnp.where(hot_k[:, :, None, None], v[:, None], 0.0), axis=0)
        v = jnp.sum(jnp.where(hot_kc[:, :, :, None], v[:, :, None, :], 0.0), axis=1)
        return v.reshape(n_od * n_c * tq)

    both = jnp.stack([to_absolute(local_max), to_absolute(local_sum)])
    every = lax.all_gather(both, ("dp", "cent"), axis=0)
    maxes, sums = every[:, 0], every[:, 1]
    peak_abs = jnp.max(maxes, axis=0)
    mass_abs = jnp.sum(sums * jnp.exp(maxes - peak_abs[None]), axis=0)
    row_peak = to_local(peak_abs)
    row_mass = to_local(mass_abs)

    weights = (jnp.exp(logits - row_peak[:, None]) / row_mass[:, None]).astype(jnp.bfloat16)
    k = centroids.shape[0]
    pod = n_d * n_c * tq
    w_pods = weights.reshape(n_o, pod, k).astype(jnp.float32)
    weight_sum = jnp.sum(w_pods, axis=1)
    scaled = (w_pods / (weight_sum[:, None, :] + 1.0)).astype(jnp.bfloat16)
    pull = lax.dot_general(
        scaled.reshape(n_o * pod, k), everything, (((0,), (0,)), ((), ())),
        preferred_element_type=jnp.float32,
    )
    coef = None
    for a in range(n_o):
        term = weight_sum[a] / (weight_sum[a] + 1.0)
        coef = term if coef is None else coef + term
    return (pull - coef[:, None] * centroids) / n_o


def solution(mesh):
    n_o, n_d, n_c = mesh.shape["outer"], mesh.shape["dp"], mesh.shape["cent"]

    def shards(rows, centroids):
        t, d = rows.shape
        k = centroids.shape[0]
        n_all = t * n_o * n_d
        footprint = n_all * d * 2 + n_all * k * 4 * 2
        if footprint <= (24 << 20) and t % n_c == 0 and n_c >= 2 and (n_c & (n_c - 1)) == 0:
            return shards_all(rows, centroids)
        return shards_pod(rows, centroids)

    return jax.shard_map(
        shards,
        mesh=mesh,
        in_specs=(P(("outer", "dp"), None), P(("dp", "cent"), None)),
        out_specs=P(("dp", "cent"), None),
        check_vma=False,
    )
```

```python
import itertools

import jax
import jax.numpy as jnp
from jax import lax
from jax.sharding import PartitionSpec as P


def scores_for(piece, cent_bf, squares):
    product = lax.dot_general(
        piece, cent_bf, (((1,), (1,)), ((), ())), preferred_element_type=jnp.float32
    )
    return 0.5 * (2.0 * product - squares[None, :])


def row_summary(logits):
    local_max = jnp.max(logits, axis=1)
    local_sum = jnp.sum(jnp.exp(logits - local_max[:, None]), axis=1)
    return (local_max, local_sum)


def global_stats(local_max, local_sum):
    row_peak = lax.pmax(local_max, ("dp", "cent"))
    row_mass = lax.psum(local_sum * jnp.exp(local_max - row_peak), ("dp", "cent"))
    return (row_peak, row_mass)


def shards_pod(rows, centroids):
    rows_bf = rows.astype(jnp.bfloat16)
    cent_bf = centroids.astype(jnp.bfloat16)
    squares = jnp.sum(centroids * centroids, axis=1)
    gathered = lax.all_gather(rows_bf, "dp", axis=0, tiled=True)
    logits = scores_for(gathered, cent_bf, squares)
    local_max, local_sum = row_summary(logits)
    row_peak, row_mass = global_stats(local_max, local_sum)
    weights = (jnp.exp(logits - row_peak[:, None]) / row_mass[:, None]).astype(jnp.bfloat16)
    weight_sum = jnp.sum(weights.astype(jnp.float32), axis=0)
    pull = lax.dot_general(
        weights, gathered, (((0,), (0,)), ((), ())), preferred_element_type=jnp.float32
    )
    delta = (pull - weight_sum[:, None] * centroids) / (weight_sum[:, None] + 1.0)
    return lax.psum(delta, "outer") / lax.axis_size("outer")


def shards_all(rows, centroids):
    n_o = lax.axis_size("outer")
    n_d = lax.axis_size("dp")
    n_c = lax.axis_size("cent")
    z = lax.axis_index("outer")
    y = lax.axis_index("dp")
    q = lax.axis_index("cent")
    t, d = rows.shape
    tq = t // n_c
    n_od = n_o * n_d

    rows_bf = rows.astype(jnp.bfloat16)
    cent_bf = centroids.astype(jnp.bfloat16)
    squares = jnp.sum(centroids * centroids, axis=1)

    bits = []
    b = 1
    while b < n_c:
        bits.append(b)
        b *= 2
    xs = [0]
    for bit in reversed(bits):
        xs = xs + [x ^ bit for x in xs]

    mine = lax.dynamic_slice_in_dim(rows, q * tq, tq, 0).astype(jnp.bfloat16)
    shifts = list(itertools.product(range(n_o), range(n_d)))
    def pair_of(piece):
        across = [piece]
        for sy in range(1, n_d):
            across.append(lax.ppermute(piece, "dp", [(j, (j + sy) % n_d) for j in range(n_d)]))
        return jnp.stack(across)

    def spread(cur):
        for bit in reversed(bits):
            other = lax.ppermute(cur, "cent", [(i, i ^ bit) for i in range(n_c)])
            cur = jnp.concatenate([cur, other], axis=1)
        return cur

    landed = [mine]
    for sz in range(1, n_o):
        if n_o & (n_o - 1) == 0:
            pairs = [(i, i ^ sz) for i in range(n_o)]
        else:
            pairs = [(i, (i + sz) % n_o) for i in range(n_o)]
        landed.append(lax.ppermute(mine, "outer", pairs))
    def spread_x_first(piece):
        order = list(reversed(bits))
        other = lax.ppermute(piece, "cent", [(i, i ^ order[0]) for i in range(n_c)])
        cur = pair_of(jnp.concatenate([piece, other], axis=0))
        for bit in order[1:]:
            other = lax.ppermute(cur, "cent", [(i, i ^ bit) for i in range(n_c)])
            cur = jnp.concatenate([cur, other], axis=1)
        return cur

    parts = [None] + [
        spread_x_first(piece) if sz in (1, 3) else spread(pair_of(piece))
        for sz, piece in enumerate(landed[1:], start=1)
    ]

    order = list(reversed(bits))
    own = lax.dynamic_slice_in_dim(rows, (q ^ order[0]) * tq, tq, 0).astype(jnp.bfloat16)
    own = pair_of(jnp.concatenate([mine, own], axis=0))
    for bit in order[1:]:
        other = lax.ppermute(own, "cent", [(i, i ^ bit) for i in range(n_c)])
        own = jnp.concatenate([own, other], axis=1)
    parts[0] = own

    cur = jnp.zeros((n_o * n_d,) + parts[0].shape[1:], parts[0].dtype)
    for sz in range(n_o):
        pod_of = (z ^ sz) if n_o & (n_o - 1) == 0 else (z - sz) % n_o
        cur = lax.dynamic_update_slice_in_dim(cur, parts[sz], pod_of * n_d, axis=0)
    everything = cur.reshape(n_od * n_c * tq, d)

    logits = scores_for(everything, cent_bf, squares)
    local_max, local_sum = row_summary(logits)

    src_vec = jnp.stack([a * n_d + (y - sy) % n_d for a, sy in shifts])
    hot_k = src_vec[None, :] == jnp.arange(n_od)[:, None]
    jj = jnp.arange(n_c)
    xor_map = q ^ jnp.asarray(xs, jnp.int32)
    c_map = jnp.broadcast_to(xor_map[None, :], (n_od, n_c))
    hot_kc = c_map[:, None, :] == jj[None, :, None]

    def to_absolute(v):
        v = v.reshape(n_od, n_c, tq)
        v = jnp.sum(jnp.where(hot_kc[:, :, :, None], v[:, None, :, :], 0.0), axis=2)
        return jnp.sum(jnp.where(hot_k[:, :, None, None], v[None], 0.0), axis=1)

    def to_local(v):
        v = jnp.sum(jnp.where(hot_k[:, :, None, None], v[:, None], 0.0), axis=0)
        v = jnp.sum(jnp.where(hot_kc[:, :, :, None], v[:, :, None, :], 0.0), axis=1)
        return v.reshape(n_od * n_c * tq)

    both = jnp.stack([to_absolute(local_max), to_absolute(local_sum)])
    every = lax.all_gather(both, ("dp", "cent"), axis=0)
    maxes, sums = every[:, 0], every[:, 1]
    peak_abs = jnp.max(maxes, axis=0)
    mass_abs = jnp.sum(sums * jnp.exp(maxes - peak_abs[None]), axis=0)
    row_peak = to_local(peak_abs)
    row_mass = to_local(mass_abs)

    weights = (jnp.exp(logits - row_peak[:, None]) / row_mass[:, None]).astype(jnp.bfloat16)
    k = centroids.shape[0]
    pod = n_d * n_c * tq
    w_pods = weights.reshape(n_o, pod, k).astype(jnp.float32)
    weight_sum = jnp.sum(w_pods, axis=1)
    scaled = (w_pods / (weight_sum[:, None, :] + 1.0)).astype(jnp.bfloat16)
    pull = lax.dot_general(
        scaled.reshape(n_o * pod, k), everything, (((0,), (0,)), ((), ())),
        preferred_element_type=jnp.float32,
    )
    coef = None
    for a in range(n_o):
        term = weight_sum[a] / (weight_sum[a] + 1.0)
        coef = term if coef is None else coef + term
    return (pull - coef[:, None] * centroids) / n_o


def solution(mesh):
    n_o, n_d, n_c = mesh.shape["outer"], mesh.shape["dp"], mesh.shape["cent"]

    def shards(rows, centroids):
        t, d = rows.shape
        k = centroids.shape[0]
        n_all = t * n_o * n_d
        footprint = n_all * d * 2 + n_all * k * 4 * 2
        if footprint <= (24 << 20) and t % n_c == 0 and n_c >= 2 and (n_c & (n_c - 1)) == 0:
            return shards_all(rows, centroids)
        return shards_pod(rows, centroids)

    return jax.shard_map(
        shards,
        mesh=mesh,
        in_specs=(P(("outer", "dp"), None), P(("dp", "cent"), None)),
        out_specs=P(("dp", "cent"), None),
        check_vma=False,
    )
```

```python
import itertools

import jax
import jax.numpy as jnp
from jax import lax
from jax.sharding import PartitionSpec as P


def scores_for(piece, cent_bf, squares):
    product = lax.dot_general(
        piece, cent_bf, (((1,), (1,)), ((), ())), preferred_element_type=jnp.float32
    )
    return 0.5 * (2.0 * product - squares[None, :])


def row_summary(logits):
    local_max = jnp.max(logits, axis=1)
    local_sum = jnp.sum(jnp.exp(logits - local_max[:, None]), axis=1)
    return (local_max, local_sum)


def global_stats(local_max, local_sum):
    row_peak = lax.pmax(local_max, ("dp", "cent"))
    row_mass = lax.psum(local_sum * jnp.exp(local_max - row_peak), ("dp", "cent"))
    return (row_peak, row_mass)


def shards_pod(rows, centroids):
    rows_bf = rows.astype(jnp.bfloat16)
    cent_bf = centroids.astype(jnp.bfloat16)
    squares = jnp.sum(centroids * centroids, axis=1)
    gathered = lax.all_gather(rows_bf, "dp", axis=0, tiled=True)
    logits = scores_for(gathered, cent_bf, squares)
    local_max, local_sum = row_summary(logits)
    row_peak, row_mass = global_stats(local_max, local_sum)
    weights = (jnp.exp(logits - row_peak[:, None]) / row_mass[:, None]).astype(jnp.bfloat16)
    weight_sum = jnp.sum(weights.astype(jnp.float32), axis=0)
    pull = lax.dot_general(
        weights, gathered, (((0,), (0,)), ((), ())), preferred_element_type=jnp.float32
    )
    delta = (pull - weight_sum[:, None] * centroids) / (weight_sum[:, None] + 1.0)
    return lax.psum(delta, "outer") / lax.axis_size("outer")


def shards_all(rows, centroids):
    n_o = lax.axis_size("outer")
    n_d = lax.axis_size("dp")
    n_c = lax.axis_size("cent")
    z = lax.axis_index("outer")
    y = lax.axis_index("dp")
    q = lax.axis_index("cent")
    t, d = rows.shape
    tq = t // n_c
    n_od = n_o * n_d

    rows_bf = rows.astype(jnp.bfloat16)
    cent_bf = centroids.astype(jnp.bfloat16)
    squares = jnp.sum(centroids * centroids, axis=1)

    bits = []
    b = 1
    while b < n_c:
        bits.append(b)
        b *= 2
    xs = [0]
    for bit in reversed(bits):
        xs = xs + [x ^ bit for x in xs]

    mine = lax.dynamic_slice_in_dim(rows, q * tq, tq, 0).astype(jnp.bfloat16)
    shifts = list(itertools.product(range(n_o), range(n_d)))
    def pair_of(piece):
        across = [piece]
        for sy in range(1, n_d):
            across.append(lax.ppermute(piece, "dp", [(j, (j + sy) % n_d) for j in range(n_d)]))
        return jnp.stack(across)

    def spread(cur):
        for bit in reversed(bits):
            other = lax.ppermute(cur, "cent", [(i, i ^ bit) for i in range(n_c)])
            cur = jnp.concatenate([cur, other], axis=1)
        return cur

    landed = [mine]
    for sz in range(1, n_o):
        if n_o & (n_o - 1) == 0:
            pairs = [(i, i ^ sz) for i in range(n_o)]
        else:
            pairs = [(i, (i + sz) % n_o) for i in range(n_o)]
        landed.append(lax.ppermute(mine, "outer", pairs))
    def spread_x_first(piece):
        order = list(reversed(bits))
        other = lax.ppermute(piece, "cent", [(i, i ^ order[0]) for i in range(n_c)])
        cur = pair_of(jnp.concatenate([piece, other], axis=0))
        for bit in order[1:]:
            other = lax.ppermute(cur, "cent", [(i, i ^ bit) for i in range(n_c)])
            cur = jnp.concatenate([cur, other], axis=1)
        return cur

    parts = [None] + [
        spread_x_first(piece) if sz in (2, 3) else spread(pair_of(piece))
        for sz, piece in enumerate(landed[1:], start=1)
    ]

    order = list(reversed(bits))
    own = lax.dynamic_slice_in_dim(rows, (q ^ order[0]) * tq, tq, 0).astype(jnp.bfloat16)
    own = pair_of(jnp.concatenate([mine, own], axis=0))
    for bit in order[1:]:
        other = lax.ppermute(own, "cent", [(i, i ^ bit) for i in range(n_c)])
        own = jnp.concatenate([own, other], axis=1)
    parts[0] = own

    cur = jnp.zeros((n_o * n_d,) + parts[0].shape[1:], parts[0].dtype)
    for sz in range(n_o):
        pod_of = (z ^ sz) if n_o & (n_o - 1) == 0 else (z - sz) % n_o
        cur = lax.dynamic_update_slice_in_dim(cur, parts[sz], pod_of * n_d, axis=0)
    everything = cur.reshape(n_od * n_c * tq, d)

    logits = scores_for(everything, cent_bf, squares)
    local_max, local_sum = row_summary(logits)

    src_vec = jnp.stack([a * n_d + (y - sy) % n_d for a, sy in shifts])
    hot_k = src_vec[None, :] == jnp.arange(n_od)[:, None]
    jj = jnp.arange(n_c)
    xor_map = q ^ jnp.asarray(xs, jnp.int32)
    c_map = jnp.broadcast_to(xor_map[None, :], (n_od, n_c))
    hot_kc = c_map[:, None, :] == jj[None, :, None]

    def to_absolute(v):
        v = v.reshape(n_od, n_c, tq)
        v = jnp.sum(jnp.where(hot_kc[:, :, :, None], v[:, None, :, :], 0.0), axis=2)
        return jnp.sum(jnp.where(hot_k[:, :, None, None], v[None], 0.0), axis=1)

    def to_local(v):
        v = jnp.sum(jnp.where(hot_k[:, :, None, None], v[:, None], 0.0), axis=0)
        v = jnp.sum(jnp.where(hot_kc[:, :, :, None], v[:, :, None, :], 0.0), axis=1)
        return v.reshape(n_od * n_c * tq)

    both = jnp.stack([to_absolute(local_max), to_absolute(local_sum)])
    every = lax.all_gather(both, ("dp", "cent"), axis=0)
    maxes, sums = every[:, 0], every[:, 1]
    peak_abs = jnp.max(maxes, axis=0)
    mass_abs = jnp.sum(sums * jnp.exp(maxes - peak_abs[None]), axis=0)
    row_peak = to_local(peak_abs)
    row_mass = to_local(mass_abs)

    weights = (jnp.exp(logits - row_peak[:, None]) / row_mass[:, None]).astype(jnp.bfloat16)
    k = centroids.shape[0]
    pod = n_d * n_c * tq
    w_pods = weights.reshape(n_o, pod, k).astype(jnp.float32)
    weight_sum = jnp.sum(w_pods, axis=1)
    scaled = (w_pods / (weight_sum[:, None, :] + 1.0)).astype(jnp.bfloat16)
    pull = lax.dot_general(
        scaled.reshape(n_o * pod, k), everything, (((0,), (0,)), ((), ())),
        preferred_element_type=jnp.float32,
    )
    coef = None
    for a in range(n_o):
        term = weight_sum[a] / (weight_sum[a] + 1.0)
        coef = term if coef is None else coef + term
    return (pull - coef[:, None] * centroids) / n_o


def solution(mesh):
    n_o, n_d, n_c = mesh.shape["outer"], mesh.shape["dp"], mesh.shape["cent"]

    def shards(rows, centroids):
        t, d = rows.shape
        k = centroids.shape[0]
        n_all = t * n_o * n_d
        footprint = n_all * d * 2 + n_all * k * 4 * 2
        if footprint <= (24 << 20) and t % n_c == 0 and n_c >= 2 and (n_c & (n_c - 1)) == 0:
            return shards_all(rows, centroids)
        return shards_pod(rows, centroids)

    return jax.shard_map(
        shards,
        mesh=mesh,
        in_specs=(P(("outer", "dp"), None), P(("dp", "cent"), None)),
        out_specs=P(("dp", "cent"), None),
        check_vma=False,
    )
```

```python
import itertools

import jax
import jax.numpy as jnp
from jax import lax
from jax.sharding import PartitionSpec as P


def scores_for(piece, cent_bf, squares):
    product = lax.dot_general(
        piece, cent_bf, (((1,), (1,)), ((), ())), preferred_element_type=jnp.float32
    )
    return 0.5 * (2.0 * product - squares[None, :])


def row_summary(logits):
    local_max = jnp.max(logits, axis=1)
    local_sum = jnp.sum(jnp.exp(logits - local_max[:, None]), axis=1)
    return (local_max, local_sum)


def global_stats(local_max, local_sum):
    row_peak = lax.pmax(local_max, ("dp", "cent"))
    row_mass = lax.psum(local_sum * jnp.exp(local_max - row_peak), ("dp", "cent"))
    return (row_peak, row_mass)


def shards_pod(rows, centroids):
    rows_bf = rows.astype(jnp.bfloat16)
    cent_bf = centroids.astype(jnp.bfloat16)
    squares = jnp.sum(centroids * centroids, axis=1)
    gathered = lax.all_gather(rows_bf, "dp", axis=0, tiled=True)
    logits = scores_for(gathered, cent_bf, squares)
    local_max, local_sum = row_summary(logits)
    row_peak, row_mass = global_stats(local_max, local_sum)
    weights = (jnp.exp(logits - row_peak[:, None]) / row_mass[:, None]).astype(jnp.bfloat16)
    weight_sum = jnp.sum(weights.astype(jnp.float32), axis=0)
    pull = lax.dot_general(
        weights, gathered, (((0,), (0,)), ((), ())), preferred_element_type=jnp.float32
    )
    delta = (pull - weight_sum[:, None] * centroids) / (weight_sum[:, None] + 1.0)
    return lax.psum(delta, "outer") / lax.axis_size("outer")


def shards_all(rows, centroids):
    n_o = lax.axis_size("outer")
    n_d = lax.axis_size("dp")
    n_c = lax.axis_size("cent")
    z = lax.axis_index("outer")
    y = lax.axis_index("dp")
    q = lax.axis_index("cent")
    t, d = rows.shape
    tq = t // n_c
    n_od = n_o * n_d

    rows_bf = rows.astype(jnp.bfloat16)
    cent_bf = centroids.astype(jnp.bfloat16)
    squares = jnp.sum(centroids * centroids, axis=1)

    bits = []
    b = 1
    while b < n_c:
        bits.append(b)
        b *= 2
    xs = [0]
    for bit in reversed(bits):
        xs = xs + [x ^ bit for x in xs]

    mine = lax.dynamic_slice_in_dim(rows, q * tq, tq, 0).astype(jnp.bfloat16)
    shifts = list(itertools.product(range(n_o), range(n_d)))
    def pair_of(piece):
        across = [piece]
        for sy in range(1, n_d):
            across.append(lax.ppermute(piece, "dp", [(j, (j + sy) % n_d) for j in range(n_d)]))
        return jnp.stack(across)

    def spread(cur):
        for bit in reversed(bits):
            other = lax.ppermute(cur, "cent", [(i, i ^ bit) for i in range(n_c)])
            cur = jnp.concatenate([cur, other], axis=1)
        return cur

    landed = [mine]
    for sz in range(1, n_o):
        if n_o & (n_o - 1) == 0:
            pairs = [(i, i ^ sz) for i in range(n_o)]
        else:
            pairs = [(i, (i + sz) % n_o) for i in range(n_o)]
        landed.append(lax.ppermute(mine, "outer", pairs))
    def spread_x_first(piece):
        order = list(reversed(bits))
        other = lax.ppermute(piece, "cent", [(i, i ^ order[0]) for i in range(n_c)])
        cur = pair_of(jnp.concatenate([piece, other], axis=0))
        for bit in order[1:]:
            other = lax.ppermute(cur, "cent", [(i, i ^ bit) for i in range(n_c)])
            cur = jnp.concatenate([cur, other], axis=1)
        return cur

    parts = [None] + [
        spread_x_first(piece) if sz in (1, 3) else spread(pair_of(piece))
        for sz, piece in enumerate(landed[1:], start=1)
    ]

    order = list(reversed(bits))
    own = lax.dynamic_slice_in_dim(rows, (q ^ order[0]) * tq, tq, 0).astype(jnp.bfloat16)
    own = pair_of(jnp.concatenate([mine, own], axis=0))
    for bit in order[1:]:
        other = lax.ppermute(own, "cent", [(i, i ^ bit) for i in range(n_c)])
        own = jnp.concatenate([own, other], axis=1)
    parts[0] = own

    cur = jnp.zeros((n_o * n_d,) + parts[0].shape[1:], parts[0].dtype)
    for sz in range(n_o):
        pod_of = (z ^ sz) if n_o & (n_o - 1) == 0 else (z - sz) % n_o
        cur = lax.dynamic_update_slice_in_dim(cur, parts[sz], pod_of * n_d, axis=0)
    everything = cur.reshape(n_od * n_c * tq, d)

    logits = scores_for(everything, cent_bf, squares)
    local_max, local_sum = row_summary(logits)

    src_vec = jnp.stack([a * n_d + (y - sy) % n_d for a, sy in shifts])
    hot_k = src_vec[None, :] == jnp.arange(n_od)[:, None]
    jj = jnp.arange(n_c)
    xor_map = q ^ jnp.asarray(xs, jnp.int32)
    c_map = jnp.broadcast_to(xor_map[None, :], (n_od, n_c))
    hot_kc = c_map[:, None, :] == jj[None, :, None]

    def to_absolute(v):
        v = v.reshape(n_od, n_c, tq)
        v = jnp.sum(jnp.where(hot_kc[:, :, :, None], v[:, None, :, :], 0.0), axis=2)
        return jnp.sum(jnp.where(hot_k[:, :, None, None], v[None], 0.0), axis=1)

    def to_local(v):
        v = jnp.sum(jnp.where(hot_k[:, :, None, None], v[:, None], 0.0), axis=0)
        v = jnp.sum(jnp.where(hot_kc[:, :, :, None], v[:, :, None, :], 0.0), axis=1)
        return v.reshape(n_od * n_c * tq)

    peak_abs = to_absolute(local_max)
    mass_abs = to_absolute(local_sum)
    if n_d & (n_d - 1) == 0:
        rounds = [("cent", bit, n_c) for bit in bits]
        bd = 1
        while bd < n_d:
            rounds.append(("dp", bd, n_d))
            bd *= 2
        for axis, bit, n in rounds:
            other = lax.ppermute(jnp.stack([peak_abs, mass_abs]), axis, [(i, i ^ bit) for i in range(n)])
            top = jnp.maximum(peak_abs, other[0])
            mass_abs = mass_abs * jnp.exp(peak_abs - top) + other[1] * jnp.exp(other[0] - top)
            peak_abs = top
    else:
        both = jnp.stack([peak_abs, mass_abs])
        every = lax.all_gather(both, ("dp", "cent"), axis=0)
        maxes, sums = every[:, 0], every[:, 1]
        peak_abs = jnp.max(maxes, axis=0)
        mass_abs = jnp.sum(sums * jnp.exp(maxes - peak_abs[None]), axis=0)
    row_peak = to_local(peak_abs)
    row_mass = to_local(mass_abs)

    weights = (jnp.exp(logits - row_peak[:, None]) / row_mass[:, None]).astype(jnp.bfloat16)
    k = centroids.shape[0]
    pod = n_d * n_c * tq
    w_pods = weights.reshape(n_o, pod, k).astype(jnp.float32)
    weight_sum = jnp.sum(w_pods, axis=1)
    scaled = (w_pods / (weight_sum[:, None, :] + 1.0)).astype(jnp.bfloat16)
    pull = lax.dot_general(
        scaled.reshape(n_o * pod, k), everything, (((0,), (0,)), ((), ())),
        preferred_element_type=jnp.float32,
    )
    coef = None
    for a in range(n_o):
        term = weight_sum[a] / (weight_sum[a] + 1.0)
        coef = term if coef is None else coef + term
    return (pull - coef[:, None] * centroids) / n_o


def solution(mesh):
    n_o, n_d, n_c = mesh.shape["outer"], mesh.shape["dp"], mesh.shape["cent"]

    def shards(rows, centroids):
        t, d = rows.shape
        k = centroids.shape[0]
        n_all = t * n_o * n_d
        footprint = n_all * d * 2 + n_all * k * 4 * 2
        if footprint <= (24 << 20) and t % n_c == 0 and n_c >= 2 and (n_c & (n_c - 1)) == 0:
            return shards_all(rows, centroids)
        return shards_pod(rows, centroids)

    return jax.shard_map(
        shards,
        mesh=mesh,
        in_specs=(P(("outer", "dp"), None), P(("dp", "cent"), None)),
        out_specs=P(("dp", "cent"), None),
        check_vma=False,
    )
```

```python
import itertools

import jax
import jax.numpy as jnp
from jax import lax
from jax.sharding import PartitionSpec as P


def scores_for(piece, cent_bf, squares):
    product = lax.dot_general(
        piece, cent_bf, (((1,), (1,)), ((), ())), preferred_element_type=jnp.float32
    )
    return 0.5 * (2.0 * product - squares[None, :])


def row_summary(logits):
    local_max = jnp.max(logits, axis=1)
    local_sum = jnp.sum(jnp.exp(logits - local_max[:, None]), axis=1)
    return (local_max, local_sum)


def global_stats(local_max, local_sum):
    row_peak = lax.pmax(local_max, ("dp", "cent"))
    row_mass = lax.psum(local_sum * jnp.exp(local_max - row_peak), ("dp", "cent"))
    return (row_peak, row_mass)


def shards_pod(rows, centroids):
    rows_bf = rows.astype(jnp.bfloat16)
    cent_bf = centroids.astype(jnp.bfloat16)
    squares = jnp.sum(centroids * centroids, axis=1)
    gathered = lax.all_gather(rows_bf, "dp", axis=0, tiled=True)
    logits = scores_for(gathered, cent_bf, squares)
    local_max, local_sum = row_summary(logits)
    row_peak, row_mass = global_stats(local_max, local_sum)
    weights = (jnp.exp(logits - row_peak[:, None]) / row_mass[:, None]).astype(jnp.bfloat16)
    weight_sum = jnp.sum(weights.astype(jnp.float32), axis=0)
    pull = lax.dot_general(
        weights, gathered, (((0,), (0,)), ((), ())), preferred_element_type=jnp.float32
    )
    delta = (pull - weight_sum[:, None] * centroids) / (weight_sum[:, None] + 1.0)
    return lax.psum(delta, "outer") / lax.axis_size("outer")


def shards_all(rows, centroids):
    n_o = lax.axis_size("outer")
    n_d = lax.axis_size("dp")
    n_c = lax.axis_size("cent")
    z = lax.axis_index("outer")
    y = lax.axis_index("dp")
    q = lax.axis_index("cent")
    t, d = rows.shape
    tq = t // n_c
    n_od = n_o * n_d

    rows_bf = rows.astype(jnp.bfloat16)
    cent_bf = centroids.astype(jnp.bfloat16)
    squares = jnp.sum(centroids * centroids, axis=1)

    bits = []
    b = 1
    while b < n_c:
        bits.append(b)
        b *= 2
    xs = [0]
    for bit in reversed(bits):
        xs = xs + [x ^ bit for x in xs]

    mine = lax.dynamic_slice_in_dim(rows, q * tq, tq, 0).astype(jnp.bfloat16)
    shifts = list(itertools.product(range(n_o), range(n_d)))
    def pair_of(piece):
        across = [piece]
        for sy in range(1, n_d):
            across.append(lax.ppermute(piece, "dp", [(j, (j + sy) % n_d) for j in range(n_d)]))
        return jnp.stack(across)

    def spread(cur):
        for bit in reversed(bits):
            other = lax.ppermute(cur, "cent", [(i, i ^ bit) for i in range(n_c)])
            cur = jnp.concatenate([cur, other], axis=1)
        return cur

    landed = [mine]
    for sz in range(1, n_o):
        if n_o & (n_o - 1) == 0:
            pairs = [(i, i ^ sz) for i in range(n_o)]
        else:
            pairs = [(i, (i + sz) % n_o) for i in range(n_o)]
        landed.append(lax.ppermute(mine, "outer", pairs))
    def spread_x_first(piece):
        order = list(reversed(bits))
        other = lax.ppermute(piece, "cent", [(i, i ^ order[0]) for i in range(n_c)])
        cur = pair_of(jnp.concatenate([piece, other], axis=0))
        for bit in order[1:]:
            other = lax.ppermute(cur, "cent", [(i, i ^ bit) for i in range(n_c)])
            cur = jnp.concatenate([cur, other], axis=1)
        return cur

    parts = [None] + [
        spread_x_first(piece) if sz == 3 else spread(pair_of(piece))
        for sz, piece in enumerate(landed[1:], start=1)
    ]

    order = list(reversed(bits))
    own = lax.dynamic_slice_in_dim(rows, (q ^ order[0]) * tq, tq, 0).astype(jnp.bfloat16)
    own = pair_of(jnp.concatenate([mine, own], axis=0))
    for bit in order[1:]:
        other = lax.ppermute(own, "cent", [(i, i ^ bit) for i in range(n_c)])
        own = jnp.concatenate([own, other], axis=1)
    parts[0] = own

    cur = jnp.zeros((n_o * n_d,) + parts[0].shape[1:], parts[0].dtype)
    for sz in range(n_o):
        pod_of = (z ^ sz) if n_o & (n_o - 1) == 0 else (z - sz) % n_o
        cur = lax.dynamic_update_slice_in_dim(cur, parts[sz], pod_of * n_d, axis=0)
    everything = cur.reshape(n_od * n_c * tq, d)

    logits = scores_for(everything, cent_bf, squares)
    local_max, local_sum = row_summary(logits)

    src_vec = jnp.stack([a * n_d + (y - sy) % n_d for a, sy in shifts])
    hot_k = src_vec[None, :] == jnp.arange(n_od)[:, None]
    jj = jnp.arange(n_c)
    xor_map = q ^ jnp.asarray(xs, jnp.int32)
    c_map = jnp.broadcast_to(xor_map[None, :], (n_od, n_c))
    hot_kc = c_map[:, None, :] == jj[None, :, None]

    def to_absolute(v):
        v = v.reshape(n_od, n_c, tq)
        v = jnp.sum(jnp.where(hot_kc[:, :, :, None], v[:, None, :, :], 0.0), axis=2)
        return jnp.sum(jnp.where(hot_k[:, :, None, None], v[None], 0.0), axis=1)

    def to_local(v):
        v = jnp.sum(jnp.where(hot_k[:, :, None, None], v[:, None], 0.0), axis=0)
        v = jnp.sum(jnp.where(hot_kc[:, :, :, None], v[:, :, None, :], 0.0), axis=1)
        return v.reshape(n_od * n_c * tq)

    peak_abs = to_absolute(local_max)
    mass_abs = to_absolute(local_sum)
    if n_d & (n_d - 1) == 0:
        rounds = [("cent", bit, n_c) for bit in bits]
        bd = 1
        while bd < n_d:
            rounds.append(("dp", bd, n_d))
            bd *= 2
        for axis, bit, n in rounds:
            other = lax.ppermute(jnp.stack([peak_abs, mass_abs]), axis, [(i, i ^ bit) for i in range(n)])
            top = jnp.maximum(peak_abs, other[0])
            mass_abs = mass_abs * jnp.exp(peak_abs - top) + other[1] * jnp.exp(other[0] - top)
            peak_abs = top
    else:
        both = jnp.stack([peak_abs, mass_abs])
        every = lax.all_gather(both, ("dp", "cent"), axis=0)
        maxes, sums = every[:, 0], every[:, 1]
        peak_abs = jnp.max(maxes, axis=0)
        mass_abs = jnp.sum(sums * jnp.exp(maxes - peak_abs[None]), axis=0)
    row_peak = to_local(peak_abs)
    row_mass = to_local(mass_abs)

    weights = (jnp.exp(logits - row_peak[:, None]) / row_mass[:, None]).astype(jnp.bfloat16)
    k = centroids.shape[0]
    pod = n_d * n_c * tq
    w_pods = weights.reshape(n_o, pod, k).astype(jnp.float32)
    weight_sum = jnp.sum(w_pods, axis=1)
    scaled = (w_pods / (weight_sum[:, None, :] + 1.0)).astype(jnp.bfloat16)
    pull = lax.dot_general(
        scaled.reshape(n_o * pod, k), everything, (((0,), (0,)), ((), ())),
        preferred_element_type=jnp.float32,
    )
    coef = None
    for a in range(n_o):
        term = weight_sum[a] / (weight_sum[a] + 1.0)
        coef = term if coef is None else coef + term
    return (pull - coef[:, None] * centroids) / n_o


def solution(mesh):
    n_o, n_d, n_c = mesh.shape["outer"], mesh.shape["dp"], mesh.shape["cent"]

    def shards(rows, centroids):
        t, d = rows.shape
        k = centroids.shape[0]
        n_all = t * n_o * n_d
        footprint = n_all * d * 2 + n_all * k * 4 * 2
        if footprint <= (24 << 20) and t % n_c == 0 and n_c >= 2 and (n_c & (n_c - 1)) == 0:
            return shards_all(rows, centroids)
        return shards_pod(rows, centroids)

    return jax.shard_map(
        shards,
        mesh=mesh,
        in_specs=(P(("outer", "dp"), None), P(("dp", "cent"), None)),
        out_specs=P(("dp", "cent"), None),
        check_vma=False,
    )
```

```python
import itertools

import jax
import jax.numpy as jnp
from jax import lax
from jax.sharding import PartitionSpec as P


def scores_for(piece, cent_bf, squares):
    product = lax.dot_general(
        piece, cent_bf, (((1,), (1,)), ((), ())), preferred_element_type=jnp.float32
    )
    return 0.5 * (2.0 * product - squares[None, :])


def row_summary(logits):
    local_max = jnp.max(logits, axis=1)
    local_sum = jnp.sum(jnp.exp(logits - local_max[:, None]), axis=1)
    return (local_max, local_sum)


def global_stats(local_max, local_sum):
    row_peak = lax.pmax(local_max, ("dp", "cent"))
    row_mass = lax.psum(local_sum * jnp.exp(local_max - row_peak), ("dp", "cent"))
    return (row_peak, row_mass)


def shards_pod(rows, centroids):
    rows_bf = rows.astype(jnp.bfloat16)
    cent_bf = centroids.astype(jnp.bfloat16)
    squares = jnp.sum(centroids * centroids, axis=1)
    gathered = lax.all_gather(rows_bf, "dp", axis=0, tiled=True)
    logits = scores_for(gathered, cent_bf, squares)
    local_max, local_sum = row_summary(logits)
    row_peak, row_mass = global_stats(local_max, local_sum)
    weights = (jnp.exp(logits - row_peak[:, None]) / row_mass[:, None]).astype(jnp.bfloat16)
    weight_sum = jnp.sum(weights.astype(jnp.float32), axis=0)
    pull = lax.dot_general(
        weights, gathered, (((0,), (0,)), ((), ())), preferred_element_type=jnp.float32
    )
    delta = (pull - weight_sum[:, None] * centroids) / (weight_sum[:, None] + 1.0)
    return lax.psum(delta, "outer") / lax.axis_size("outer")


def shards_all(rows, centroids):
    n_o = lax.axis_size("outer")
    n_d = lax.axis_size("dp")
    n_c = lax.axis_size("cent")
    z = lax.axis_index("outer")
    y = lax.axis_index("dp")
    q = lax.axis_index("cent")
    t, d = rows.shape
    tq = t // n_c
    n_od = n_o * n_d

    rows_bf = rows.astype(jnp.bfloat16)
    cent_bf = centroids.astype(jnp.bfloat16)
    squares = jnp.sum(centroids * centroids, axis=1)

    bits = []
    b = 1
    while b < n_c:
        bits.append(b)
        b *= 2
    xs = [0]
    for bit in reversed(bits):
        xs = xs + [x ^ bit for x in xs]

    mine = lax.dynamic_slice_in_dim(rows, q * tq, tq, 0).astype(jnp.bfloat16)
    shifts = list(itertools.product(range(n_o), range(n_d)))
    def pair_of(piece):
        across = [piece]
        for sy in range(1, n_d):
            across.append(lax.ppermute(piece, "dp", [(j, (j + sy) % n_d) for j in range(n_d)]))
        return jnp.stack(across)

    def spread(cur):
        for bit in reversed(bits):
            other = lax.ppermute(cur, "cent", [(i, i ^ bit) for i in range(n_c)])
            cur = jnp.concatenate([cur, other], axis=1)
        return cur

    landed = [mine]
    for sz in range(1, n_o):
        if n_o & (n_o - 1) == 0:
            pairs = [(i, i ^ sz) for i in range(n_o)]
        else:
            pairs = [(i, (i + sz) % n_o) for i in range(n_o)]
        landed.append(lax.ppermute(mine, "outer", pairs))
    def spread_x_first(piece):
        order = list(reversed(bits))
        other = lax.ppermute(piece, "cent", [(i, i ^ order[0]) for i in range(n_c)])
        cur = pair_of(jnp.concatenate([piece, other], axis=0))
        for bit in order[1:]:
            other = lax.ppermute(cur, "cent", [(i, i ^ bit) for i in range(n_c)])
            cur = jnp.concatenate([cur, other], axis=1)
        return cur

    parts = [None] + [
        spread_x_first(piece) if sz in (1, 3) else spread(pair_of(piece))
        for sz, piece in enumerate(landed[1:], start=1)
    ]

    order = list(reversed(bits))
    own = lax.dynamic_slice_in_dim(rows, (q ^ order[0]) * tq, tq, 0).astype(jnp.bfloat16)
    own = pair_of(jnp.concatenate([mine, own], axis=0))
    for bit in order[1:]:
        other = lax.ppermute(own, "cent", [(i, i ^ bit) for i in range(n_c)])
        own = jnp.concatenate([own, other], axis=1)
    parts[0] = own

    cur = jnp.zeros((n_o * n_d,) + parts[0].shape[1:], parts[0].dtype)
    for sz in range(n_o):
        pod_of = (z ^ sz) if n_o & (n_o - 1) == 0 else (z - sz) % n_o
        cur = lax.dynamic_update_slice_in_dim(cur, parts[sz], pod_of * n_d, axis=0)
    everything = cur.reshape(n_od * n_c * tq, d)

    logits = scores_for(everything, cent_bf, squares)
    local_max, local_sum = row_summary(logits)

    src_vec = jnp.stack([a * n_d + (y - sy) % n_d for a, sy in shifts])
    hot_k = src_vec[None, :] == jnp.arange(n_od)[:, None]
    jj = jnp.arange(n_c)
    xor_map = q ^ jnp.asarray(xs, jnp.int32)
    c_map = jnp.broadcast_to(xor_map[None, :], (n_od, n_c))
    hot_kc = c_map[:, None, :] == jj[None, :, None]

    def to_absolute(v):
        v = v.reshape(n_od, n_c, tq)
        v = jnp.sum(jnp.where(hot_kc[:, :, :, None], v[:, None, :, :], 0.0), axis=2)
        return jnp.sum(jnp.where(hot_k[:, :, None, None], v[None], 0.0), axis=1)

    def to_local(v):
        v = jnp.sum(jnp.where(hot_k[:, :, None, None], v[:, None], 0.0), axis=0)
        v = jnp.sum(jnp.where(hot_kc[:, :, :, None], v[:, :, None, :], 0.0), axis=1)
        return v.reshape(n_od * n_c * tq)

    peak_abs = to_absolute(local_max)
    mass_abs = to_absolute(local_sum)
    if n_d & (n_d - 1) == 0:
        rounds = []
        bd = 1
        while bd < n_d:
            rounds.append(("dp", bd, n_d))
            bd *= 2
        rounds += [("cent", bit, n_c) for bit in reversed(bits)]
        for axis, bit, n in rounds:
            other = lax.ppermute(jnp.stack([peak_abs, mass_abs]), axis, [(i, i ^ bit) for i in range(n)])
            top = jnp.maximum(peak_abs, other[0])
            mass_abs = mass_abs * jnp.exp(peak_abs - top) + other[1] * jnp.exp(other[0] - top)
            peak_abs = top
    else:
        both = jnp.stack([peak_abs, mass_abs])
        every = lax.all_gather(both, ("dp", "cent"), axis=0)
        maxes, sums = every[:, 0], every[:, 1]
        peak_abs = jnp.max(maxes, axis=0)
        mass_abs = jnp.sum(sums * jnp.exp(maxes - peak_abs[None]), axis=0)
    row_peak = to_local(peak_abs)
    row_mass = to_local(mass_abs)

    weights = (jnp.exp(logits - row_peak[:, None]) / row_mass[:, None]).astype(jnp.bfloat16)
    k = centroids.shape[0]
    pod = n_d * n_c * tq
    w_pods = weights.reshape(n_o, pod, k).astype(jnp.float32)
    weight_sum = jnp.sum(w_pods, axis=1)
    scaled = (w_pods / (weight_sum[:, None, :] + 1.0)).astype(jnp.bfloat16)
    pull = lax.dot_general(
        scaled.reshape(n_o * pod, k), everything, (((0,), (0,)), ((), ())),
        preferred_element_type=jnp.float32,
    )
    coef = None
    for a in range(n_o):
        term = weight_sum[a] / (weight_sum[a] + 1.0)
        coef = term if coef is None else coef + term
    return (pull - coef[:, None] * centroids) / n_o


def solution(mesh):
    n_o, n_d, n_c = mesh.shape["outer"], mesh.shape["dp"], mesh.shape["cent"]

    def shards(rows, centroids):
        t, d = rows.shape
        k = centroids.shape[0]
        n_all = t * n_o * n_d
        footprint = n_all * d * 2 + n_all * k * 4 * 2
        if footprint <= (24 << 20) and t % n_c == 0 and n_c >= 2 and (n_c & (n_c - 1)) == 0:
            return shards_all(rows, centroids)
        return shards_pod(rows, centroids)

    return jax.shard_map(
        shards,
        mesh=mesh,
        in_specs=(P(("outer", "dp"), None), P(("dp", "cent"), None)),
        out_specs=P(("dp", "cent"), None),
        check_vma=False,
    )
```
